32 devices in a mesh: req: 8 (over z, y), ep: 4 (over x, core).
Axes of the slice: x: 2, y: 2, z: 4, core: 2. Of those that a mesh axis runs over, the one named last changes fastest.
Arguments:
- tokens: bfloat16 [4096, 1536], P(('req', 'ep')), may hold values from -6 to 6
- seg_ids: int32 [4096], P(('req', 'ep')), may hold values from 0 to 3, never falling along the last dimension, each value on 1 to 2048 neighbouring positions
- routes: int32 [4096, 8], P(('req', 'ep')), may hold values from 0 to 39, all different within a row; in each aligned block of 128 rows (0 to 127, 128 to 255, ...) at most 48 rows name the same one
- route_weights: float32 [4096, 8], P(('req', 'ep')), may hold values from 0.05 to 0.3
- norm1_gain: float32 [1536], replicated, may hold values from 0.5 to 1.5
- norm2_gain: float32 [1536], replicated, may hold values from 0.5 to 1.5
- w_query: bfloat16 [1536, 1536], P(None, 'ep')
- key_weight: bfloat16 [1536, 512], P(None, 'ep')
- value_weight: bfloat16 [1536, 512], P(None, 'ep'), may hold values from -0.15625 to 0.15625
- w_out_attn: bfloat16 [1536, 1536], P('ep'), may hold values from -0.15625 to 0.15625
- w_in: bfloat16 [40, 1536, 1024], P('ep'), may hold values from -0.15625 to 0.15625
- w_out: bfloat16 [40, 512, 1536], P('ep'), may hold values from -0.25 to 0.25
- paged_key_value_cache: bfloat16 [96, 8, 2, 64, 64], P('req', 'ep'), may hold values from -6 to 6
- page_table: int32 [64], replicated, may hold values from 0 to 95, as said below
Outputs:
- attn_out: bfloat16 [4096, 1536], P(('req', 'ep'))
- moe_out: bfloat16 [4096, 1536], P(('req', 'ep'))
- new_cache: bfloat16 [96, 8, 2, 64, 64], P('req', 'ep')
The draws below stay inside these ranges and needn't reach their ends.
Inputs may be any that keep to these rules, and one draw needn't show every extreme that they name: `seg_ids`: segment ids never fall along the stream; the longest prompt holds exactly half of the 4096 tokens. `routes`: each token names 8 different experts; within the rows of one device no expert is named more than 48 times, a bound that some block reaches. `page_table`: entries are distinct.
All inputs are finite; a program needn't handle non-finite values.
Results may differ from the reference program's by a relative error of at most 0.017.
Values may be sent and summed in bfloat16 or wider, within the bound.
No kernel may reach another device: no remote copies, remote signals or barrier semaphores. Data moves between devices by JAX's collectives and lax.ppermute only.
A program may use at most 192 MiB of HBM per device.

```python
import math
import jax
import jax.numpy as jnp
import numpy as np
from jax import lax

MODEL_WIDTH = 1536
QUERY_HEADS = 24
KEY_VALUE_HEADS = 8
HEAD_SIZE = 64
E = 40
FFE = 512
TOPK = 8
TOK_DEV = 128
PAGE_TOKENS = 64
REQUEST_TOKENS = 512
STREAM_TOKENS = 4096
CAP = 48
SEGS = 4
TARGET_PAGES = 64
TOTAL_PAGES = 96
N_REQ = 8
N_EP = 4


def key_offset(key):
    return jax.random.normal(jax.random.fold_in(key, 11), (MODEL_WIDTH, KEY_VALUE_HEADS * HEAD_SIZE), jnp.float32) * MODEL_WIDTH ** (-0.5)


def draw_key_weight(key, part):
    return key_offset(key).astype(jnp.bfloat16)


def draw_w_query(key, part):
    loose = jax.random.normal(jax.random.fold_in(key, 12), (MODEL_WIDTH, QUERY_HEADS * HEAD_SIZE), jnp.float32) * (20.0 * MODEL_WIDTH ** (-0.5))
    return loose.astype(jnp.bfloat16)


def draw_page_table(key, part):
    order = jax.random.permutation(jax.random.fold_in(key, 21), TOTAL_PAGES).astype(jnp.int32)
    chosen = order[:TARGET_PAGES]
    chosen = chosen.at[0].set(jnp.where(jnp.any(chosen == TOTAL_PAGES - 1), chosen[0], TOTAL_PAGES - 1))
    second = jnp.where(chosen[1] == TOTAL_PAGES - 1, 2, 1)
    chosen = chosen.at[second].set(jnp.where(jnp.any(chosen == 0), chosen[second], 0))
    return chosen.astype(jnp.int32)


def block_levels(rng, shape, cuts, smallest, top_value):
    level = 1.0
    for dim, shards_of in cuts:
        heights = jax.random.uniform(jax.random.fold_in(jax.random.fold_in(rng, 6), dim), (shards_of,), jnp.float32, smallest / len(cuts), top_value / len(cuts))
        level = level * jnp.repeat(jnp.exp(heights), shape[dim] // shards_of).reshape((-1,) + (1,) * (len(shape) - 1 - dim))
    return level


def length_profile(count, total, reach, skew):
    weights = [(1 << 20) // math.isqrt(grade ** skew) + 1 for grade in range(2, count + 1)]
    rest, counts = total - reach - (count - 1), [1] * (count - 1)
    while rest > 0:
        movable = [i for i in range(count - 1) if counts[i] < reach]
        whole, budget = sum([weights[i] for i in movable]), rest
        for i in movable:
            addition = min(reach - counts[i], max(1, budget * weights[i] // whole), rest)
            counts[i] = counts[i] + addition
            rest = rest - addition
    return np.array([reach] + counts)


def uneven_parts(rng, amount, total, bound, skew):
    if amount == 2:
        one = jax.random.randint(rng, (), max(1, total - bound), min(bound, total - 1) + 1)
        return jnp.stack([one, total - one])
    tallies = jnp.asarray(length_profile(amount, total, bound, skew), jnp.int32)
    couples = (amount - 1) // 2
    donor, receiver = tallies[1:1 + 2 * couples:2], tallies[2:2 + 2 * couples:2]
    slack = jnp.minimum(donor - 1, bound - receiver)
    shifted = jax.random.randint(jax.random.fold_in(rng, 1), (couples,), 0, 1 << 20) % (slack + 1)
    tallies = tallies.at[1:1 + 2 * couples:2].set(donor - shifted).at[2:2 + 2 * couples:2].set(receiver + shifted)
    return tallies[jax.random.permutation(jax.random.fold_in(rng, 2), amount)]


def routed_block(own_key, own, number, rows, number_of, top, bound, slope):
    ranking = jax.random.permutation(own_key, number_of)
    packed, ordinary = shares(number_of, rows * top, bound, slope, True), shares(number_of, rows * top, bound, slope, False)
    places = jnp.arange(number_of)

    def named(tallies, offset_by):
        used = int((tallies > 0).sum())
        fixed = max(1, used // 4)
        passed = fixed + (places - fixed + offset_by * (used - fixed)) % max(1, number_of - fixed)
        return jnp.zeros((number_of,), jnp.int32).at[ranking[jnp.where(places < fixed, places, passed)]].set(jnp.asarray(tallies, jnp.int32))

    tallies = jnp.where(number % 4 == 0, named(packed, number // 4), named(ordinary, number - number // 4 - 1))
    mixed = jax.random.permutation(jax.random.fold_in(own, 3), number_of)
    giver, sink = mixed[0:number_of // 2 * 2:2], mixed[1:number_of // 2 * 2:2]
    slack = jnp.minimum(tallies[giver] - 1, bound - tallies[sink]) // 2
    slack = jnp.where((giver == ranking[0]) | (sink == ranking[0]) | (tallies[sink] == 0), 0, jnp.maximum(slack, 0))
    passed = jax.random.randint(jax.random.fold_in(own, 4), (number_of // 2,), 0, 1 << 20) % (slack + 1)
    tallies = tallies.at[giver].add(-passed).at[sink].add(passed)
    members = jnp.searchsorted(jnp.cumsum(tallies), jnp.arange(rows * top), side="right").astype(jnp.int32)
    listing = members.reshape(top, rows).T
    listing = listing[jax.random.permutation(jax.random.fold_in(own, 1), rows)]
    offset_by = jax.random.randint(jax.random.fold_in(own, 2), (rows, 1), 0, top)
    return jnp.take_along_axis(listing, (jnp.arange(top)[None, :] + offset_by) % top, axis=1)


def shares(number_of, total, most, slope, full):
    weights = [(1 << 20) // math.isqrt(grade ** slope) + 1 for grade in range(1, number_of + 1)]
    largest = most if full else min(most, max(-(-total // number_of), total * weights[0] // sum(weights)))
    least = 1 if total - largest >= number_of - 1 else 0
    given, spare = [largest] + [least] * (number_of - 1), total - largest - least * (number_of - 1)
    while spare > 0:
        free = [i for i in range(1, number_of) if given[i] < largest] or [i for i in range(1, number_of) if given[i] < most]
        whole, budget = sum([weights[i] for i in free]), spare
        for i in free:
            more = min(most - given[i], max(1, budget * weights[i] // whole), spare)
            given[i] = given[i] + more
            spare = spare - more
    return np.array(given)


def scatter_about(own_key, dims, scale, limit, split=(), kind=jnp.bfloat16):
    values = jax.random.normal(own_key, dims, jnp.float32) * scale
    if len(split) > 0:
        values = block_levels(own_key, dims, split, -0.22, 0.18) * values
    return jnp.clip(values, min=-limit, max=limit).astype(kind)


def setup_inputs(seed: int = 0) -> dict:
    key_list = jax.random.split(jax.random.key(seed), 15)
    tokens = scatter_about(key_list[0], (STREAM_TOKENS, MODEL_WIDTH), 1.0, 6.0, ((0, 32),))
    seg_ids = jnp.searchsorted(jnp.cumsum(uneven_parts(key_list[1], SEGS, STREAM_TOKENS, STREAM_TOKENS // 2, 1)), jnp.arange(STREAM_TOKENS), side="right").astype(jnp.int32)
    routes_keys = jax.random.split(jax.random.fold_in(key_list[2], 1), STREAM_TOKENS // TOK_DEV)
    routes_turns = jax.random.permutation(jax.random.fold_in(key_list[2], 3), STREAM_TOKENS // TOK_DEV)
    routes = jax.vmap(lambda own, number: routed_block(jax.random.fold_in(key_list[2], 2), own, number, TOK_DEV, E, TOPK, CAP, 2))(routes_keys, routes_turns).reshape((STREAM_TOKENS, TOPK))
    route_weights = jnp.clip(0.05 + 0.25 * jax.random.uniform(key_list[3], (STREAM_TOKENS, TOPK), jnp.float32) ** block_levels(key_list[3], (STREAM_TOKENS, TOPK), ((0, 32),), -0.2, 0.2), 0.05, 0.3)
    norm1_gain = jnp.clip(1.0 + 0.1 * jax.random.normal(key_list[4], (MODEL_WIDTH,), jnp.float32), 0.5, 1.5)
    norm2_gain = jnp.clip(1.0 + 0.1 * jax.random.normal(key_list[5], (MODEL_WIDTH,), jnp.float32), 0.5, 1.5)
    w_query = draw_w_query(jax.random.fold_in(key_list[14], 71), 0)
    key_weight = draw_key_weight(jax.random.fold_in(key_list[14], 71), 0)
    value_weight = scatter_about(key_list[8], (MODEL_WIDTH, KEY_VALUE_HEADS * HEAD_SIZE), MODEL_WIDTH ** -0.5, 0.15625, ((1, 4),))
    w_out_attn = scatter_about(key_list[9], (QUERY_HEADS * HEAD_SIZE, MODEL_WIDTH), (QUERY_HEADS * HEAD_SIZE) ** -0.5, 0.15625, ((0, 4),))
    w_in = scatter_about(key_list[10], (E, MODEL_WIDTH, 2 * FFE), MODEL_WIDTH ** -0.5, 0.15625, ((0, 4),))
    w_out = scatter_about(key_list[11], (E, FFE, MODEL_WIDTH), FFE ** -0.5, 0.25, ((0, 4),))
    paged_key_value_cache = scatter_about(key_list[12], (TOTAL_PAGES, KEY_VALUE_HEADS, 2, PAGE_TOKENS, HEAD_SIZE), 1.0, 6.0, ((0, 8), (1, 4)))
    page_table = draw_page_table(jax.random.fold_in(key_list[14], 71), 0)
    return {"tokens": tokens, "seg_ids": seg_ids, "routes": routes, "route_weights": route_weights, "norm1_gain": norm1_gain, "norm2_gain": norm2_gain, "w_query": w_query, "key_weight": key_weight, "value_weight": value_weight, "w_out_attn": w_out_attn, "w_in": w_in, "w_out": w_out, "paged_key_value_cache": paged_key_value_cache, "page_table": page_table}


norm_eps = 1e-06
score_scale = 0.015625
residual_scale = 0.22
rope_base = 10000.0

def rms_scale(rows, gain):
    mean_sq = lax.optimization_barrier(jnp.mean(rows * rows, axis=-1, keepdims=True))
    return rows * lax.rsqrt(mean_sq + norm_eps) * gain

def positions_of(segments):
    tok_index = jnp.arange(segments.shape[0], dtype=jnp.int32)
    previous = jnp.concatenate([jnp.full((1,), -1, jnp.int32), segments[:-1]])
    starts = jnp.where(segments != previous, tok_index, 0).astype(jnp.int32)
    return (tok_index - lax.cummax(starts, axis=0)).astype(jnp.int32)

def rotary_apply(heads_in, token_positions):
    half_dim = heads_in.shape[-1] // 2
    inverse_freq = rope_base ** (-jnp.arange(half_dim, dtype=jnp.float32) * 2.0 / heads_in.shape[-1])
    angles = token_positions.astype(jnp.float32)[:, None] * inverse_freq[None, :]
    cos_part = jnp.cos(angles)[:, None, :]
    sine_part = jnp.sin(angles)[:, None, :]
    first_half = heads_in[..., :half_dim]
    second_half = heads_in[..., half_dim:]
    return jnp.concatenate([first_half * cos_part - second_half * sine_part, second_half * cos_part + first_half * sine_part], axis=-1)

def reference(tokens, seg_ids, routes, route_weights, norm1_gain, norm2_gain, w_query, key_weight, value_weight, w_out_attn, w_in, w_out, paged_key_value_cache, page_table):
    heads_ratio = QUERY_HEADS // KEY_VALUE_HEADS
    token_positions = positions_of(seg_ids)
    attention_input = rms_scale(tokens.astype(jnp.float32), norm1_gain).astype(jnp.bfloat16)
    query_rows = rotary_apply(jnp.dot(attention_input, w_query, preferred_element_type=jnp.float32).reshape(STREAM_TOKENS, QUERY_HEADS, HEAD_SIZE), token_positions).astype(jnp.bfloat16)
    key_matrix = rotary_apply(jnp.dot(attention_input, key_weight, preferred_element_type=jnp.float32).reshape(STREAM_TOKENS, KEY_VALUE_HEADS, HEAD_SIZE), token_positions).astype(jnp.bfloat16)
    value_rows = jnp.dot(attention_input, value_weight, preferred_element_type=jnp.float32).astype(jnp.bfloat16).reshape(STREAM_TOKENS, KEY_VALUE_HEADS, HEAD_SIZE)
    query_grouped = query_rows.reshape(STREAM_TOKENS, KEY_VALUE_HEADS, heads_ratio, HEAD_SIZE)
    window = min(STREAM_TOKENS, STREAM_TOKENS // 2 + REQUEST_TOKENS)

    def single_entry(item_no):
        kv_head = item_no // N_REQ
        q_block = item_no % N_REQ
        q_start = (q_block * REQUEST_TOKENS).astype(jnp.int32)
        k_start = jnp.clip(q_start + REQUEST_TOKENS - window, 0, STREAM_TOKENS - window).astype(jnp.int32)
        zero = jnp.zeros((), jnp.int32)
        q_rows = lax.dynamic_slice(query_grouped, (q_start, kv_head.astype(jnp.int32), zero, zero), (REQUEST_TOKENS, 1, heads_ratio, HEAD_SIZE))[:, 0]
        key_head = lax.dynamic_slice(key_matrix, (k_start, kv_head.astype(jnp.int32), zero), (window, 1, HEAD_SIZE))[:, 0]
        value_head = lax.dynamic_slice(value_rows, (k_start, kv_head.astype(jnp.int32), zero), (window, 1, HEAD_SIZE))[:, 0]
        scores = jnp.einsum('qrd,kd->rqk', q_rows.astype(jnp.float32), key_head.astype(jnp.float32)) * score_scale
        q_index = q_start + jnp.arange(REQUEST_TOKENS, dtype=jnp.int32)
        k_index = k_start + jnp.arange(window, dtype=jnp.int32)
        seg_q = lax.dynamic_slice(seg_ids, (q_start,), (REQUEST_TOKENS,))
        seg_k = lax.dynamic_slice(seg_ids, (k_start,), (window,))
        allowed = (seg_q[:, None] == seg_k[None, :]) & (k_index[None, :] <= q_index[:, None])
        masked = jnp.where(allowed[None], scores, -jnp.inf)
        row_max = lax.optimization_barrier(jnp.max(masked, axis=-1, keepdims=True))
        exponent = jnp.where(allowed[None], jnp.exp(masked - row_max), 0.0)
        row_sum = lax.optimization_barrier(jnp.sum(exponent, axis=-1))
        probabilities = exponent.astype(jnp.bfloat16)
        mixed = jnp.einsum('rqk,kd->rqd', probabilities.astype(jnp.float32), value_head.astype(jnp.float32))
        return (mixed / row_sum[..., None]).astype(jnp.bfloat16)
    attention_result = lax.map(single_entry, jnp.arange(KEY_VALUE_HEADS * N_REQ, dtype=jnp.int32))
    attention_result = attention_result.reshape(KEY_VALUE_HEADS, N_REQ, heads_ratio, REQUEST_TOKENS, HEAD_SIZE).transpose(1, 3, 0, 2, 4).reshape(STREAM_TOKENS, QUERY_HEADS * HEAD_SIZE)
    attention = jnp.dot(attention_result, w_out_attn, preferred_element_type=jnp.float32)
    attn_out = attention.astype(jnp.bfloat16)
    moe_in = rms_scale(tokens.astype(jnp.float32) + residual_scale * attention, norm2_gain).astype(jnp.bfloat16)
    blocks = N_REQ * N_EP
    flat_routes = routes.reshape(blocks, TOK_DEV * TOPK)
    onehot = (flat_routes[:, :, None] == jnp.arange(E, dtype=jnp.int32)[None, None, :]).astype(jnp.int32)
    slot_of = lax.optimization_barrier(jnp.sum((jnp.cumsum(onehot, axis=1) - 1) * onehot, axis=-1))
    place_of = (jnp.arange(blocks, dtype=jnp.int32)[:, None] * CAP + slot_of).reshape(-1).astype(jnp.int32)
    owner_of = (jnp.arange(STREAM_TOKENS * TOPK, dtype=jnp.int32) // TOPK).astype(jnp.int32)
    slot_table = jnp.full((E, blocks * CAP), STREAM_TOKENS, jnp.int32).at[flat_routes.reshape(-1), place_of].set(owner_of)
    padded = jnp.concatenate([moe_in, jnp.zeros((1, MODEL_WIDTH), jnp.bfloat16)], axis=0)

    def per_expert(running, expert):
        gathered = padded[slot_table[expert]]
        gate_up = jnp.dot(gathered, w_in[expert], preferred_element_type=jnp.float32)
        activated = (jax.nn.silu(gate_up[:, :FFE]) * gate_up[:, FFE:]).astype(jnp.bfloat16)
        result = jnp.dot(activated, w_out[expert], preferred_element_type=jnp.float32).astype(jnp.bfloat16)
        spread = jnp.zeros((STREAM_TOKENS + 1, MODEL_WIDTH), jnp.bfloat16).at[slot_table[expert]].set(result)[:STREAM_TOKENS]
        share = lax.optimization_barrier(jnp.sum(jnp.where(routes == expert, route_weights, 0.0), axis=1))
        return (running + share[:, None] * spread.astype(jnp.float32), None)
    moe_sum, unused = lax.scan(per_expert, jnp.zeros((STREAM_TOKENS, MODEL_WIDTH), jnp.float32), jnp.arange(E, dtype=jnp.int32))
    moe_out = moe_sum.astype(jnp.bfloat16)
    paged_keys = key_matrix.reshape(TARGET_PAGES, PAGE_TOKENS, KEY_VALUE_HEADS, HEAD_SIZE).transpose(0, 2, 1, 3)
    paged_values = value_rows.reshape(TARGET_PAGES, PAGE_TOKENS, KEY_VALUE_HEADS, HEAD_SIZE).transpose(0, 2, 1, 3)
    fresh = jnp.stack([paged_keys, paged_values], axis=2)
    new_cache = paged_key_value_cache.at[page_table].set(fresh)
    return (attn_out, moe_out, new_cache)
```

```python
import jax
import jax.numpy as jnp
from jax import lax
from jax.sharding import PartitionSpec as P
from jax.experimental import pallas as pl
from jax.experimental.pallas import tpu as pltpu

HEAD_SIZE = 64
E = 40
PAGE_TOKENS = 64
CAP = 48


norm_eps = 1e-06
score_scale = 0.015625
residual_scale = 0.22
rope_base = 10000.0
neg_fill = -1e30


def rms_scale(rows, gain):
    mean_sq = jnp.mean(rows * rows, axis=-1, keepdims=True)
    return rows * lax.rsqrt(mean_sq + norm_eps) * gain


def positions_of(segments):
    tok_index = jnp.arange(segments.shape[0], dtype=jnp.int32)
    previous = jnp.concatenate([jnp.full((1,), -1, jnp.int32), segments[:-1]])
    starts = jnp.where(segments != previous, tok_index, 0)
    return tok_index - lax.cummax(starts, axis=0)


def rotary_apply(heads_in, token_positions):
    half_dim = heads_in.shape[-1] // 2
    inverse_freq = rope_base ** (
        -jnp.arange(half_dim, dtype=jnp.float32) * 2.0 / heads_in.shape[-1]
    )
    angles = token_positions.astype(jnp.float32)[:, None] * inverse_freq[None, :]
    cos_part = jnp.cos(angles)[:, None, :]
    sine_part = jnp.sin(angles)[:, None, :]
    first_half = heads_in[..., :half_dim]
    second_half = heads_in[..., half_dim:]
    return jnp.concatenate(
        [
            first_half * cos_part - second_half * sine_part,
            second_half * cos_part + first_half * sine_part,
        ],
        axis=-1,
    )


Q_TILE = 128
K_TILE = 256


def flash_body(lo_ref, hi_ref, q_ref, k_ref, v_ref, tok_ref, begin_ref, o_ref):
    qb = pl.program_id(1)
    ratio = q_ref.shape[1]
    q_tile = q_ref.shape[2]
    head_dim = q_ref.shape[3]
    q = q_ref[0].reshape(ratio * q_tile, head_dim)
    tok = tok_ref[...]
    begin = begin_ref[...]

    def step(kb, carry):
        m_old, l_old, acc_old = carry
        k0 = pl.multiple_of(kb * K_TILE, K_TILE)
        k_blk = k_ref[0, pl.ds(k0, K_TILE), :]
        v_blk = v_ref[0, pl.ds(k0, K_TILE), :]
        s = lax.dot_general(
            q, k_blk, (((1,), (1,)), ((), ())), preferred_element_type=jnp.float32
        )
        s = (s * score_scale).reshape(ratio, q_tile, K_TILE)
        key_at = k0 + lax.broadcasted_iota(jnp.int32, (q_tile, K_TILE), 1)
        allowed = (key_at >= begin) & (key_at <= tok)
        s = jnp.where(allowed[None], s, -jnp.inf)
        m_new = jnp.maximum(m_old, jnp.max(s, axis=-1, keepdims=True))
        alpha = jnp.exp(m_old - m_new)
        p = jnp.exp(s - m_new)
        l_new = alpha * l_old + jnp.sum(p, axis=-1, keepdims=True)
        pv = lax.dot_general(
            p.reshape(ratio * q_tile, K_TILE).astype(jnp.bfloat16),
            v_blk,
            (((1,), (0,)), ((), ())),
            preferred_element_type=jnp.float32,
        )
        acc_new = alpha * acc_old + pv.reshape(ratio, q_tile, head_dim)
        return m_new, l_new, acc_new

    init = (
        jnp.full((ratio, q_tile, 1), neg_fill, jnp.float32),
        jnp.zeros((ratio, q_tile, 1), jnp.float32),
        jnp.zeros((ratio, q_tile, head_dim), jnp.float32),
    )
    m_fin, l_fin, acc_fin = lax.fori_loop(lo_ref[qb], hi_ref[qb] + 1, step, init)
    o_ref[0] = (acc_fin / l_fin).astype(o_ref.dtype)


def flash_attention(query_grouped, kv_all, q_index, q_begin):
    kv_heads, ratio, group_len, head_dim = query_grouped.shape
    n_rows = kv_all.shape[1]
    n_q = group_len // Q_TILE
    lo = jnp.min(q_begin.reshape(n_q, Q_TILE), axis=1) // K_TILE
    hi = jnp.max(q_index.reshape(n_q, Q_TILE), axis=1) // K_TILE
    grid_spec = pltpu.PrefetchScalarGridSpec(
        num_scalar_prefetch=2,
        grid=(kv_heads, n_q),
        in_specs=[
            pl.BlockSpec((1, ratio, Q_TILE, head_dim), lambda g, qb, lo, hi: (g, 0, qb, 0)),
            pl.BlockSpec((1, n_rows, head_dim), lambda g, qb, lo, hi: (g, 0, 0)),
            pl.BlockSpec((1, n_rows, head_dim), lambda g, qb, lo, hi: (kv_heads + g, 0, 0)),
            pl.BlockSpec((Q_TILE, 1), lambda g, qb, lo, hi: (qb, 0)),
            pl.BlockSpec((Q_TILE, 1), lambda g, qb, lo, hi: (qb, 0)),
        ],
        out_specs=pl.BlockSpec((1, ratio, Q_TILE, head_dim), lambda g, qb, lo, hi: (g, 0, qb, 0)),
    )
    out = pl.pallas_call(
        flash_body,
        grid_spec=grid_spec,
        out_shape=jax.ShapeDtypeStruct(query_grouped.shape, jnp.bfloat16),
    )(lo, hi, query_grouped, kv_all, kv_all, q_index[:, None], q_begin[:, None])
    return out


def body(
    tokens,
    seg_ids,
    routes,
    route_weights,
    norm1_gain,
    norm2_gain,
    w_query,
    key_weight,
    value_weight,
    w_out_attn,
    w_in,
    w_out,
    paged_key_value_cache,
    page_table,
):
    tok_dev = tokens.shape[0]
    ep_count = lax.axis_size("ep")
    group_len = tok_dev * ep_count
    req_pos = lax.axis_index("req")
    all_segs = lax.all_gather(seg_ids, ("req", "ep"), axis=0, tiled=True)
    all_pos = positions_of(all_segs)
    group_start = req_pos * group_len
    group_pos = lax.dynamic_slice_in_dim(all_pos, group_start, group_len)
    group_seg = lax.dynamic_slice_in_dim(all_segs, group_start, group_len)
    normed = rms_scale(tokens.astype(jnp.float32), norm1_gain).astype(jnp.bfloat16)
    joined = jnp.concatenate([w_query, key_weight, value_weight], axis=1)
    projected = jnp.dot(
        lax.all_gather(normed, "ep", axis=0, tiled=True), joined, preferred_element_type=jnp.float32
    )
    query_width = w_query.shape[1]
    kv_width = key_weight.shape[1]
    q_heads = query_width // HEAD_SIZE
    kv_heads = kv_width // HEAD_SIZE
    heads_ratio = q_heads // kv_heads
    query_rows = rotary_apply(
        projected[:, :query_width].reshape(group_len, q_heads, HEAD_SIZE), group_pos
    ).astype(jnp.bfloat16)
    key_rows = rotary_apply(
        projected[:, query_width : query_width + kv_width].reshape(
            group_len, kv_heads, HEAD_SIZE
        ),
        group_pos,
    ).astype(jnp.bfloat16)
    value_rows = (
        projected[:, query_width + kv_width :]
        .astype(jnp.bfloat16)
        .reshape(group_len, kv_heads, HEAD_SIZE)
    )
    query_grouped = query_rows.reshape(group_len, kv_heads, heads_ratio, HEAD_SIZE).transpose(
        1, 2, 0, 3
    )
    kv_local = jnp.concatenate(
        [key_rows.transpose(1, 0, 2), value_rows.transpose(1, 0, 2)], axis=0
    )
    kv_all = lax.all_gather(kv_local, "req", axis=1, tiled=True)
    n_rows = kv_all.shape[1]
    q_index = group_start + jnp.arange(group_len, dtype=jnp.int32)
    q_begin = q_index - group_pos
    head_out = flash_attention(query_grouped, kv_all, q_index, q_begin)
    pages_here = paged_key_value_cache.shape[0]
    page_first = req_pos * pages_here
    piece_pages = n_rows // PAGE_TOKENS
    local_pages = page_first + jnp.arange(pages_here, dtype=jnp.int32)
    match = local_pages[:, None] == page_table[None, :]
    hit = jnp.any(match, axis=1)
    block_of = jnp.argmax(match, axis=1).astype(jnp.int32)
    kv_paged = kv_all.reshape(2, kv_heads, piece_pages, PAGE_TOKENS, HEAD_SIZE)
    picked = jnp.take(kv_paged, block_of, axis=2, mode="clip").transpose(2, 1, 0, 3, 4)
    new_cache = jnp.where(hit[:, None, None, None, None], picked, paged_key_value_cache)
    head_out = head_out.transpose(2, 0, 1, 3).reshape(group_len, query_width)
    attention = lax.psum_scatter(
        jnp.dot(head_out, w_out_attn, preferred_element_type=jnp.float32).astype(jnp.bfloat16),
        "ep",
        scatter_dimension=0,
        tiled=True,
    ).astype(jnp.float32)
    attn_out = attention.astype(jnp.bfloat16)
    moe_in = rms_scale(tokens.astype(jnp.float32) + residual_scale * attention, norm2_gain).astype(
        jnp.bfloat16
    )
    ffe_width = w_out.shape[1]
    exp_here = w_in.shape[0]
    expert_ids = jnp.arange(E, dtype=jnp.int32)
    shares = jnp.sum(
        jnp.where(routes[:, :, None] == expert_ids[None, None, :], route_weights[:, :, None], 0.0),
        axis=1,
    )
    rows_all = lax.all_gather(moe_in, "ep", axis=0, tiled=True)
    shares_all = lax.all_gather(shares, "ep", axis=0, tiled=True)
    first_expert = lax.axis_index("ep") * exp_here
    shares_here = lax.dynamic_slice_in_dim(shares_all, first_expert, exp_here, 1)
    total_rows = rows_all.shape[0]
    chosen = (shares_here > 0.0).astype(jnp.int32).reshape(ep_count, tok_dev, exp_here)
    slot_in = jnp.cumsum(chosen, axis=1) - 1
    source_ids = jnp.arange(ep_count, dtype=jnp.int32)[:, None, None]
    local_slot = (source_ids * CAP + slot_in).reshape(total_rows, exp_here)
    live = (chosen > 0).reshape(total_rows, exp_here)
    slot_ids = jnp.arange(ep_count * CAP, dtype=jnp.int32)
    dispatch = (local_slot.T[:, None, :] == slot_ids[None, :, None]) & live.T[:, None, :]
    arrived = jnp.einsum(
        "esr,rd->esd", dispatch.astype(jnp.bfloat16), rows_all, preferred_element_type=jnp.float32
    ).astype(jnp.bfloat16)
    gate_up = jnp.einsum("esd,edf->esf", arrived, w_in, preferred_element_type=jnp.float32)
    activated = (jax.nn.silu(gate_up[..., :ffe_width]) * gate_up[..., ffe_width:]).astype(
        jnp.bfloat16
    )
    result = jnp.einsum(
        "esf,efd->esd", activated, w_out, preferred_element_type=jnp.float32
    ).astype(jnp.bfloat16)
    slot_weight = jnp.sum(jnp.where(dispatch, shares_here.T[:, None, :], 0.0), axis=2)
    weighted = result.astype(jnp.float32) * slot_weight[..., None]
    partial_rows = jnp.einsum(
        "esr,esd->rd",
        dispatch.astype(jnp.float32),
        weighted,
        precision=lax.Precision.HIGHEST,
        preferred_element_type=jnp.float32,
    )
    moe_out = lax.psum_scatter(
        partial_rows.astype(jnp.bfloat16), "ep", scatter_dimension=0, tiled=True
    )
    return (attn_out, moe_out, new_cache)


def solution(mesh):
    in_specs = (
        P(("req", "ep"), None),
        P(("req", "ep")),
        P(("req", "ep"), None),
        P(("req", "ep"), None),
        P(),
        P(),
        P(None, "ep"),
        P(None, "ep"),
        P(None, "ep"),
        P("ep", None),
        P("ep", None, None),
        P("ep", None, None),
        P("req", "ep", None, None, None),
        P(),
    )
    out_specs = (P(("req", "ep"), None), P(("req", "ep"), None), P("req", "ep", None, None, None))
    return jax.shard_map(body, mesh=mesh, in_specs=in_specs, out_specs=out_specs, check_vma=False)
```

```python
import jax
import jax.numpy as jnp
from jax import lax
from jax.sharding import PartitionSpec as P
from jax.experimental import pallas as pl
from jax.experimental.pallas import tpu as pltpu

HEAD_SIZE = 64
E = 40
PAGE_TOKENS = 64
CAP = 48


norm_eps = 1e-06
score_scale = 0.015625
residual_scale = 0.22
rope_base = 10000.0
neg_fill = -1e30


def rms_scale(rows, gain):
    mean_sq = jnp.mean(rows * rows, axis=-1, keepdims=True)
    return rows * lax.rsqrt(mean_sq + norm_eps) * gain


def positions_of(segments):
    tok_index = jnp.arange(segments.shape[0], dtype=jnp.int32)
    previous = jnp.concatenate([jnp.full((1,), -1, jnp.int32), segments[:-1]])
    starts = jnp.where(segments != previous, tok_index, 0)
    return tok_index - lax.cummax(starts, axis=0)


def rotary_apply(heads_in, token_positions):
    half_dim = heads_in.shape[-1] // 2
    inverse_freq = rope_base ** (
        -jnp.arange(half_dim, dtype=jnp.float32) * 2.0 / heads_in.shape[-1]
    )
    angles = token_positions.astype(jnp.float32)[:, None] * inverse_freq[None, :]
    cos_part = jnp.cos(angles)[:, None, :]
    sine_part = jnp.sin(angles)[:, None, :]
    first_half = heads_in[..., :half_dim]
    second_half = heads_in[..., half_dim:]
    return jnp.concatenate(
        [
            first_half * cos_part - second_half * sine_part,
            second_half * cos_part + first_half * sine_part,
        ],
        axis=-1,
    )


def gather_rows(x, axis_name, axis=0):
    count = lax.axis_size(axis_name)
    spread = jnp.broadcast_to(x[None], (count,) + x.shape)
    got = lax.all_to_all(spread, axis_name, 0, 0, tiled=True)
    got = jnp.moveaxis(got, 0, axis)
    shape = list(x.shape)
    shape[axis] = shape[axis] * count
    return got.reshape(shape)


def scatter_sum_rows(x, axis_name):
    count = lax.axis_size(axis_name)
    parts = x.reshape((count, x.shape[0] // count) + x.shape[1:])
    got = lax.all_to_all(parts, axis_name, 0, 0, tiled=True)
    return jnp.sum(got.astype(jnp.float32), axis=0)


Q_TILE = 128
K_TILE = 256


def flash_body(lo_ref, hi_ref, q_ref, k_ref, v_ref, tok_ref, begin_ref, o_ref):
    qb = pl.program_id(1)
    ratio = q_ref.shape[1]
    q_tile = q_ref.shape[2]
    head_dim = q_ref.shape[3]
    q = q_ref[0].reshape(ratio * q_tile, head_dim)
    tok = tok_ref[...]
    begin = begin_ref[...]

    def step(kb, carry):
        m_old, l_old, acc_old = carry
        k0 = pl.multiple_of(kb * K_TILE, K_TILE)
        k_blk = k_ref[0, pl.ds(k0, K_TILE), :]
        v_blk = v_ref[0, pl.ds(k0, K_TILE), :]
        s = lax.dot_general(
            q, k_blk, (((1,), (1,)), ((), ())), preferred_element_type=jnp.float32
        )
        s = (s * score_scale).reshape(ratio, q_tile, K_TILE)
        key_at = k0 + lax.broadcasted_iota(jnp.int32, (q_tile, K_TILE), 1)
        allowed = (key_at >= begin) & (key_at <= tok)
        s = jnp.where(allowed[None], s, -jnp.inf)
        m_new = jnp.maximum(m_old, jnp.max(s, axis=-1, keepdims=True))
        alpha = jnp.exp(m_old - m_new)
        p = jnp.exp(s - m_new)
        l_new = alpha * l_old + jnp.sum(p, axis=-1, keepdims=True)
        pv = lax.dot_general(
            p.reshape(ratio * q_tile, K_TILE).astype(jnp.bfloat16),
            v_blk,
            (((1,), (0,)), ((), ())),
            preferred_element_type=jnp.float32,
        )
        acc_new = alpha * acc_old + pv.reshape(ratio, q_tile, head_dim)
        return m_new, l_new, acc_new

    init = (
        jnp.full((ratio, q_tile, 1), neg_fill, jnp.float32),
        jnp.zeros((ratio, q_tile, 1), jnp.float32),
        jnp.zeros((ratio, q_tile, head_dim), jnp.float32),
    )
    m_fin, l_fin, acc_fin = lax.fori_loop(lo_ref[qb], hi_ref[qb] + 1, step, init)
    o_ref[0] = (acc_fin / l_fin).astype(o_ref.dtype)


def flash_attention(query_grouped, kv_all, q_index, q_begin):
    kv_heads, ratio, group_len, head_dim = query_grouped.shape
    n_rows = kv_all.shape[1]
    n_q = group_len // Q_TILE
    lo = jnp.min(q_begin.reshape(n_q, Q_TILE), axis=1) // K_TILE
    hi = jnp.max(q_index.reshape(n_q, Q_TILE), axis=1) // K_TILE
    grid_spec = pltpu.PrefetchScalarGridSpec(
        num_scalar_prefetch=2,
        grid=(kv_heads, n_q),
        in_specs=[
            pl.BlockSpec((1, ratio, Q_TILE, head_dim), lambda g, qb, lo, hi: (g, 0, qb, 0)),
            pl.BlockSpec((1, n_rows, head_dim), lambda g, qb, lo, hi: (g, 0, 0)),
            pl.BlockSpec((1, n_rows, head_dim), lambda g, qb, lo, hi: (kv_heads + g, 0, 0)),
            pl.BlockSpec((Q_TILE, 1), lambda g, qb, lo, hi: (qb, 0)),
            pl.BlockSpec((Q_TILE, 1), lambda g, qb, lo, hi: (qb, 0)),
        ],
        out_specs=pl.BlockSpec((1, ratio, Q_TILE, head_dim), lambda g, qb, lo, hi: (g, 0, qb, 0)),
    )
    out = pl.pallas_call(
        flash_body,
        grid_spec=grid_spec,
        out_shape=jax.ShapeDtypeStruct(query_grouped.shape, jnp.bfloat16),
    )(lo, hi, query_grouped, kv_all, kv_all, q_index[:, None], q_begin[:, None])
    return out


def body(
    tokens,
    seg_ids,
    routes,
    route_weights,
    norm1_gain,
    norm2_gain,
    w_query,
    key_weight,
    value_weight,
    w_out_attn,
    w_in,
    w_out,
    paged_key_value_cache,
    page_table,
):
    tok_dev = tokens.shape[0]
    ep_count = lax.axis_size("ep")
    group_len = tok_dev * ep_count
    req_pos = lax.axis_index("req")
    all_segs = gather_rows(seg_ids, ("req", "ep"))
    all_pos = positions_of(all_segs)
    group_start = req_pos * group_len
    group_pos = lax.dynamic_slice_in_dim(all_pos, group_start, group_len)
    group_seg = lax.dynamic_slice_in_dim(all_segs, group_start, group_len)
    normed = rms_scale(tokens.astype(jnp.float32), norm1_gain).astype(jnp.bfloat16)
    joined = jnp.concatenate([w_query, key_weight, value_weight], axis=1)
    projected = jnp.dot(
        gather_rows(normed, "ep"), joined, preferred_element_type=jnp.float32
    )
    query_width = w_query.shape[1]
    kv_width = key_weight.shape[1]
    q_heads = query_width // HEAD_SIZE
    kv_heads = kv_width // HEAD_SIZE
    heads_ratio = q_heads // kv_heads
    query_rows = rotary_apply(
        projected[:, :query_width].reshape(group_len, q_heads, HEAD_SIZE), group_pos
    ).astype(jnp.bfloat16)
    key_rows = rotary_apply(
        projected[:, query_width : query_width + kv_width].reshape(
            group_len, kv_heads, HEAD_SIZE
        ),
        group_pos,
    ).astype(jnp.bfloat16)
    value_rows = (
        projected[:, query_width + kv_width :]
        .astype(jnp.bfloat16)
        .reshape(group_len, kv_heads, HEAD_SIZE)
    )
    query_grouped = query_rows.reshape(group_len, kv_heads, heads_ratio, HEAD_SIZE).transpose(
        1, 2, 0, 3
    )
    kv_local = jnp.concatenate(
        [key_rows.transpose(1, 0, 2), value_rows.transpose(1, 0, 2)], axis=0
    )
    kv_all = gather_rows(kv_local, "req", axis=1)
    n_rows = kv_all.shape[1]
    q_index = group_start + jnp.arange(group_len, dtype=jnp.int32)
    q_begin = q_index - group_pos
    head_out = flash_attention(query_grouped, kv_all, q_index, q_begin)
    pages_here = paged_key_value_cache.shape[0]
    page_first = req_pos * pages_here
    piece_pages = n_rows // PAGE_TOKENS
    local_pages = page_first + jnp.arange(pages_here, dtype=jnp.int32)
    match = local_pages[:, None] == page_table[None, :]
    hit = jnp.any(match, axis=1)
    block_of = jnp.argmax(match, axis=1).astype(jnp.int32)
    kv_paged = kv_all.reshape(2, kv_heads, piece_pages, PAGE_TOKENS, HEAD_SIZE)
    picked = jnp.take(kv_paged, block_of, axis=2, mode="clip").transpose(2, 1, 0, 3, 4)
    new_cache = jnp.where(hit[:, None, None, None, None], picked, paged_key_value_cache)
    head_out = head_out.transpose(2, 0, 1, 3).reshape(group_len, query_width)
    attention = scatter_sum_rows(
        jnp.dot(head_out, w_out_attn, preferred_element_type=jnp.float32).astype(jnp.bfloat16),
        "ep",
    )
    attn_out = attention.astype(jnp.bfloat16)
    moe_in = rms_scale(tokens.astype(jnp.float32) + residual_scale * attention, norm2_gain).astype(
        jnp.bfloat16
    )
    ffe_width = w_out.shape[1]
    exp_here = w_in.shape[0]
    expert_ids = jnp.arange(E, dtype=jnp.int32)
    shares = jnp.sum(
        jnp.where(routes[:, :, None] == expert_ids[None, None, :], route_weights[:, :, None], 0.0),
        axis=1,
    )
    rows_all = gather_rows(moe_in, "ep")
    shares_all = gather_rows(shares, "ep")
    first_expert = lax.axis_index("ep") * exp_here
    shares_here = lax.dynamic_slice_in_dim(shares_all, first_expert, exp_here, 1)
    total_rows = rows_all.shape[0]
    chosen = (shares_here > 0.0).astype(jnp.int32).reshape(ep_count, tok_dev, exp_here)
    slot_in = jnp.cumsum(chosen, axis=1) - 1
    source_ids = jnp.arange(ep_count, dtype=jnp.int32)[:, None, None]
    local_slot = (source_ids * CAP + slot_in).reshape(total_rows, exp_here)
    live = (chosen > 0).reshape(total_rows, exp_here)
    slot_ids = jnp.arange(ep_count * CAP, dtype=jnp.int32)
    dispatch = (local_slot.T[:, None, :] == slot_ids[None, :, None]) & live.T[:, None, :]
    arrived = jnp.einsum(
        "esr,rd->esd", dispatch.astype(jnp.bfloat16), rows_all, preferred_element_type=jnp.float32
    ).astype(jnp.bfloat16)
    gate_up = jnp.einsum("esd,edf->esf", arrived, w_in, preferred_element_type=jnp.float32)
    activated = (jax.nn.silu(gate_up[..., :ffe_width]) * gate_up[..., ffe_width:]).astype(
        jnp.bfloat16
    )
    result = jnp.einsum(
        "esf,efd->esd", activated, w_out, preferred_element_type=jnp.float32
    ).astype(jnp.bfloat16)
    slot_weight = jnp.sum(jnp.where(dispatch, shares_here.T[:, None, :], 0.0), axis=2)
    weighted = result.astype(jnp.float32) * slot_weight[..., None]
    partial_rows = jnp.einsum(
        "esr,esd->rd",
        dispatch.astype(jnp.float32),
        weighted,
        precision=lax.Precision.HIGHEST,
        preferred_element_type=jnp.float32,
    )
    moe_out = scatter_sum_rows(partial_rows.astype(jnp.bfloat16), "ep").astype(jnp.bfloat16)
    return (attn_out, moe_out, new_cache)


def solution(mesh):
    in_specs = (
        P(("req", "ep"), None),
        P(("req", "ep")),
        P(("req", "ep"), None),
        P(("req", "ep"), None),
        P(),
        P(),
        P(None, "ep"),
        P(None, "ep"),
        P(None, "ep"),
        P("ep", None),
        P("ep", None, None),
        P("ep", None, None),
        P("req", "ep", None, None, None),
        P(),
    )
    out_specs = (P(("req", "ep"), None), P(("req", "ep"), None), P("req", "ep", None, None, None))
    return jax.shard_map(body, mesh=mesh, in_specs=in_specs, out_specs=out_specs, check_vma=False)
```

```python
import jax
import jax.numpy as jnp
from jax import lax
from jax.sharding import PartitionSpec as P
from jax.experimental import pallas as pl
from jax.experimental.pallas import tpu as pltpu

HEAD_SIZE = 64
E = 40
PAGE_TOKENS = 64
CAP = 48


norm_eps = 1e-06
score_scale = 0.015625
residual_scale = 0.22
rope_base = 10000.0
neg_fill = -1e30


def rms_scale(rows, gain):
    mean_sq = jnp.mean(rows * rows, axis=-1, keepdims=True)
    return rows * lax.rsqrt(mean_sq + norm_eps) * gain


def positions_of(segments):
    tok_index = jnp.arange(segments.shape[0], dtype=jnp.int32)
    previous = jnp.concatenate([jnp.full((1,), -1, jnp.int32), segments[:-1]])
    starts = jnp.where(segments != previous, tok_index, 0)
    return tok_index - lax.cummax(starts, axis=0)


def rotary_apply(heads_in, token_positions):
    half_dim = heads_in.shape[-1] // 2
    inverse_freq = rope_base ** (
        -jnp.arange(half_dim, dtype=jnp.float32) * 2.0 / heads_in.shape[-1]
    )
    angles = token_positions.astype(jnp.float32)[:, None] * inverse_freq[None, :]
    cos_part = jnp.cos(angles)[:, None, :]
    sine_part = jnp.sin(angles)[:, None, :]
    first_half = heads_in[..., :half_dim]
    second_half = heads_in[..., half_dim:]
    return jnp.concatenate(
        [
            first_half * cos_part - second_half * sine_part,
            second_half * cos_part + first_half * sine_part,
        ],
        axis=-1,
    )


def gather_rows(x, axis_name, axis=0):
    count = lax.axis_size(axis_name)
    spread = jnp.broadcast_to(x[None], (count,) + x.shape)
    got = lax.all_to_all(spread, axis_name, 0, 0, tiled=True)
    got = jnp.moveaxis(got, 0, axis)
    shape = list(x.shape)
    shape[axis] = shape[axis] * count
    return got.reshape(shape)


def scatter_sum_rows(x, axis_name):
    count = lax.axis_size(axis_name)
    parts = x.reshape((count, x.shape[0] // count) + x.shape[1:])
    got = lax.all_to_all(parts, axis_name, 0, 0, tiled=True)
    return jnp.sum(got.astype(jnp.float32), axis=0)


Q_TILE = 128
K_TILE = 256


def flash_body(lo_ref, hi_ref, q_ref, k_ref, v_ref, tok_ref, begin_ref, o_ref):
    qb = pl.program_id(1)
    ratio = q_ref.shape[1]
    q_tile = q_ref.shape[2]
    head_dim = q_ref.shape[3]
    q = q_ref[0].reshape(ratio * q_tile, head_dim)
    tok = tok_ref[...]
    begin = begin_ref[...]

    def step(kb, carry):
        m_old, l_old, acc_old = carry
        k0 = pl.multiple_of(kb * K_TILE, K_TILE)
        k_blk = k_ref[0, pl.ds(k0, K_TILE), :]
        v_blk = v_ref[0, pl.ds(k0, K_TILE), :]
        s = lax.dot_general(
            q, k_blk, (((1,), (1,)), ((), ())), preferred_element_type=jnp.float32
        )
        s = (s * score_scale).reshape(ratio, q_tile, K_TILE)
        key_at = k0 + lax.broadcasted_iota(jnp.int32, (q_tile, K_TILE), 1)
        allowed = (key_at >= begin) & (key_at <= tok)
        s = jnp.where(allowed[None], s, -jnp.inf)
        m_new = jnp.maximum(m_old, jnp.max(s, axis=-1, keepdims=True))
        alpha = jnp.exp(m_old - m_new)
        p = jnp.exp(s - m_new)
        l_new = alpha * l_old + jnp.sum(p, axis=-1, keepdims=True)
        pv = lax.dot_general(
            p.reshape(ratio * q_tile, K_TILE).astype(jnp.bfloat16),
            v_blk,
            (((1,), (0,)), ((), ())),
            preferred_element_type=jnp.float32,
        )
        acc_new = alpha * acc_old + pv.reshape(ratio, q_tile, head_dim)
        return m_new, l_new, acc_new

    init = (
        jnp.full((ratio, q_tile, 1), neg_fill, jnp.float32),
        jnp.zeros((ratio, q_tile, 1), jnp.float32),
        jnp.zeros((ratio, q_tile, head_dim), jnp.float32),
    )
    m_fin, l_fin, acc_fin = lax.fori_loop(lo_ref[qb], hi_ref[qb] + 1, step, init)
    o_ref[0] = (acc_fin / l_fin).astype(o_ref.dtype)


def flash_attention(query_grouped, kv_all, q_index, q_begin):
    kv_heads, ratio, group_len, head_dim = query_grouped.shape
    n_rows = kv_all.shape[1]
    n_q = group_len // Q_TILE
    lo = jnp.min(q_begin.reshape(n_q, Q_TILE), axis=1) // K_TILE
    hi = jnp.max(q_index.reshape(n_q, Q_TILE), axis=1) // K_TILE
    grid_spec = pltpu.PrefetchScalarGridSpec(
        num_scalar_prefetch=2,
        grid=(kv_heads, n_q),
        in_specs=[
            pl.BlockSpec((1, ratio, Q_TILE, head_dim), lambda g, qb, lo, hi: (g, 0, qb, 0)),
            pl.BlockSpec((1, n_rows, head_dim), lambda g, qb, lo, hi: (g, 0, 0)),
            pl.BlockSpec((1, n_rows, head_dim), lambda g, qb, lo, hi: (kv_heads + g, 0, 0)),
            pl.BlockSpec((Q_TILE, 1), lambda g, qb, lo, hi: (qb, 0)),
            pl.BlockSpec((Q_TILE, 1), lambda g, qb, lo, hi: (qb, 0)),
        ],
        out_specs=pl.BlockSpec((1, ratio, Q_TILE, head_dim), lambda g, qb, lo, hi: (g, 0, qb, 0)),
    )
    out = pl.pallas_call(
        flash_body,
        grid_spec=grid_spec,
        out_shape=jax.ShapeDtypeStruct(query_grouped.shape, jnp.bfloat16),
    )(lo, hi, query_grouped, kv_all, kv_all, q_index[:, None], q_begin[:, None])
    return out


def body(
    tokens,
    seg_ids,
    routes,
    route_weights,
    norm1_gain,
    norm2_gain,
    w_query,
    key_weight,
    value_weight,
    w_out_attn,
    w_in,
    w_out,
    paged_key_value_cache,
    page_table,
):
    tok_dev = tokens.shape[0]
    ep_count = lax.axis_size("ep")
    group_len = tok_dev * ep_count
    req_pos = lax.axis_index("req")
    all_segs = gather_rows(seg_ids, ("req", "ep"))
    all_pos = positions_of(all_segs)
    group_start = req_pos * group_len
    group_pos = lax.dynamic_slice_in_dim(all_pos, group_start, group_len)
    group_seg = lax.dynamic_slice_in_dim(all_segs, group_start, group_len)
    normed = rms_scale(tokens.astype(jnp.float32), norm1_gain).astype(jnp.bfloat16)
    joined = jnp.concatenate([w_query, key_weight, value_weight], axis=1)
    projected = jnp.dot(
        gather_rows(normed, "ep"), joined, preferred_element_type=jnp.float32
    )
    query_width = w_query.shape[1]
    kv_width = key_weight.shape[1]
    q_heads = query_width // HEAD_SIZE
    kv_heads = kv_width // HEAD_SIZE
    heads_ratio = q_heads // kv_heads
    query_rows = rotary_apply(
        projected[:, :query_width].reshape(group_len, q_heads, HEAD_SIZE), group_pos
    ).astype(jnp.bfloat16)
    key_rows = rotary_apply(
        projected[:, query_width : query_width + kv_width].reshape(
            group_len, kv_heads, HEAD_SIZE
        ),
        group_pos,
    ).astype(jnp.bfloat16)
    value_rows = (
        projected[:, query_width + kv_width :]
        .astype(jnp.bfloat16)
        .reshape(group_len, kv_heads, HEAD_SIZE)
    )
    query_grouped = query_rows.reshape(group_len, kv_heads, heads_ratio, HEAD_SIZE).transpose(
        1, 2, 0, 3
    )
    kv_local = jnp.concatenate(
        [key_rows.transpose(1, 0, 2), value_rows.transpose(1, 0, 2)], axis=0
    )
    kv_all = gather_rows(kv_local, "req", axis=1)
    n_rows = kv_all.shape[1]
    q_index = group_start + jnp.arange(group_len, dtype=jnp.int32)
    q_begin = q_index - group_pos
    head_out = flash_attention(query_grouped, kv_all, q_index, q_begin)
    pages_here = paged_key_value_cache.shape[0]
    page_first = req_pos * pages_here
    piece_pages = n_rows // PAGE_TOKENS
    local_pages = page_first + jnp.arange(pages_here, dtype=jnp.int32)
    match = local_pages[:, None] == page_table[None, :]
    hit = jnp.any(match, axis=1)
    block_of = jnp.argmax(match, axis=1).astype(jnp.int32)
    kv_paged = kv_all.reshape(2, kv_heads, piece_pages, PAGE_TOKENS, HEAD_SIZE)
    picked = jnp.take(kv_paged, block_of, axis=2, mode="clip").transpose(2, 1, 0, 3, 4)
    new_cache = jnp.where(hit[:, None, None, None, None], picked, paged_key_value_cache)
    head_out = head_out.transpose(2, 0, 1, 3).reshape(group_len, query_width)
    attention = scatter_sum_rows(
        jnp.dot(head_out, w_out_attn, preferred_element_type=jnp.float32).astype(jnp.bfloat16),
        "ep",
    )
    attn_out = attention.astype(jnp.bfloat16)
    moe_in = rms_scale(tokens.astype(jnp.float32) + residual_scale * attention, norm2_gain).astype(
        jnp.bfloat16
    )
    ffe_width = w_out.shape[1]
    exp_here = w_in.shape[0]
    expert_ids = jnp.arange(E, dtype=jnp.int32)
    shares = jnp.sum(
        jnp.where(routes[:, :, None] == expert_ids[None, None, :], route_weights[:, :, None], 0.0),
        axis=1,
    )
    rows_all = gather_rows(moe_in, "ep")
    shares_all = gather_rows(shares, "ep")
    first_expert = lax.axis_index("ep") * exp_here
    shares_here = lax.dynamic_slice_in_dim(shares_all, first_expert, exp_here, 1)
    total_rows = rows_all.shape[0]
    chosen = (shares_here > 0.0).astype(jnp.int32).reshape(ep_count, tok_dev, exp_here)
    slot_in = jnp.cumsum(chosen, axis=1) - 1
    source_ids = jnp.arange(ep_count, dtype=jnp.int32)[:, None, None]
    local_slot = (source_ids * CAP + slot_in).reshape(total_rows, exp_here)
    live = (chosen > 0).reshape(total_rows, exp_here)
    slot_ids = jnp.arange(ep_count * CAP, dtype=jnp.int32)
    dispatch = (local_slot.T[:, None, :] == slot_ids[None, :, None]) & live.T[:, None, :]
    arrived = jnp.einsum(
        "esr,rd->esd", dispatch.astype(jnp.bfloat16), rows_all, preferred_element_type=jnp.float32
    ).astype(jnp.bfloat16)
    gate_up = jnp.einsum("esd,edf->esf", arrived, w_in, preferred_element_type=jnp.float32)
    activated = (jax.nn.silu(gate_up[..., :ffe_width]) * gate_up[..., ffe_width:]).astype(
        jnp.bfloat16
    )
    result = jnp.einsum(
        "esf,efd->esd", activated, w_out, preferred_element_type=jnp.float32
    ).astype(jnp.bfloat16)
    combine = jnp.where(dispatch, shares_here.T[:, None, :], 0.0)
    combine_hi = combine.astype(jnp.bfloat16)
    combine_lo = (combine - combine_hi.astype(jnp.float32)).astype(jnp.bfloat16)
    partial_rows = jnp.einsum(
        "esr,esd->rd", combine_hi, result, preferred_element_type=jnp.float32
    ) + jnp.einsum("esr,esd->rd", combine_lo, result, preferred_element_type=jnp.float32)
    moe_out = scatter_sum_rows(partial_rows.astype(jnp.bfloat16), "ep").astype(jnp.bfloat16)
    return (attn_out, moe_out, new_cache)


def solution(mesh):
    in_specs = (
        P(("req", "ep"), None),
        P(("req", "ep")),
        P(("req", "ep"), None),
        P(("req", "ep"), None),
        P(),
        P(),
        P(None, "ep"),
        P(None, "ep"),
        P(None, "ep"),
        P("ep", None),
        P("ep", None, None),
        P("ep", None, None),
        P("req", "ep", None, None, None),
        P(),
    )
    out_specs = (P(("req", "ep"), None), P(("req", "ep"), None), P("req", "ep", None, None, None))
    return jax.shard_map(body, mesh=mesh, in_specs=in_specs, out_specs=out_specs, check_vma=False)
```

```python
import jax
import jax.numpy as jnp
from jax import lax
from jax.sharding import PartitionSpec as P
from jax.experimental import pallas as pl
from jax.experimental.pallas import tpu as pltpu

HEAD_SIZE = 64
E = 40
PAGE_TOKENS = 64
CAP = 48


norm_eps = 1e-06
score_scale = 0.015625
residual_scale = 0.22
rope_base = 10000.0
neg_fill = -1e30


def rms_scale(rows, gain):
    mean_sq = jnp.mean(rows * rows, axis=-1, keepdims=True)
    return rows * lax.rsqrt(mean_sq + norm_eps) * gain


def positions_of(segments):
    tok_index = jnp.arange(segments.shape[0], dtype=jnp.int32)
    previous = jnp.concatenate([jnp.full((1,), -1, jnp.int32), segments[:-1]])
    starts = jnp.where(segments != previous, tok_index, 0)
    return tok_index - lax.cummax(starts, axis=0)


def rotary_apply(heads_in, token_positions):
    half_dim = heads_in.shape[-1] // 2
    inverse_freq = rope_base ** (
        -jnp.arange(half_dim, dtype=jnp.float32) * 2.0 / heads_in.shape[-1]
    )
    angles = token_positions.astype(jnp.float32)[:, None] * inverse_freq[None, :]
    cos_part = jnp.cos(angles)[:, None, :]
    sine_part = jnp.sin(angles)[:, None, :]
    first_half = heads_in[..., :half_dim]
    second_half = heads_in[..., half_dim:]
    return jnp.concatenate(
        [
            first_half * cos_part - second_half * sine_part,
            second_half * cos_part + first_half * sine_part,
        ],
        axis=-1,
    )


def gather_rows(x, axis_name, axis=0):
    count = lax.axis_size(axis_name)
    spread = jnp.broadcast_to(x[None], (count,) + x.shape)
    got = lax.all_to_all(spread, axis_name, 0, 0, tiled=True)
    got = jnp.moveaxis(got, 0, axis)
    shape = list(x.shape)
    shape[axis] = shape[axis] * count
    return got.reshape(shape)


def scatter_sum_rows(x, axis_name):
    count = lax.axis_size(axis_name)
    parts = x.reshape((count, x.shape[0] // count) + x.shape[1:])
    got = lax.all_to_all(parts, axis_name, 0, 0, tiled=True)
    return jnp.sum(got.astype(jnp.float32), axis=0)


Q_TILE = 128
K_TILE = 256


def flash_body(lo_ref, hi_ref, q_ref, k_ref, v_ref, tok_ref, begin_ref, o_ref):
    qb = pl.program_id(1)
    ratio = q_ref.shape[1]
    q_tile = q_ref.shape[2]
    head_dim = q_ref.shape[3]
    q = q_ref[0].reshape(ratio * q_tile, head_dim)
    tok = tok_ref[...]
    begin = begin_ref[...]

    def step(kb, carry):
        m_old, l_old, acc_old = carry
        k0 = pl.multiple_of(kb * K_TILE, K_TILE)
        k_blk = k_ref[0, pl.ds(k0, K_TILE), :]
        v_blk = v_ref[0, pl.ds(k0, K_TILE), :]
        s = lax.dot_general(
            q, k_blk, (((1,), (1,)), ((), ())), preferred_element_type=jnp.float32
        )
        s = (s * score_scale).reshape(ratio, q_tile, K_TILE)
        key_at = k0 + lax.broadcasted_iota(jnp.int32, (q_tile, K_TILE), 1)
        allowed = (key_at >= begin) & (key_at <= tok)
        s = jnp.where(allowed[None], s, -jnp.inf)
        m_new = jnp.maximum(m_old, jnp.max(s, axis=-1, keepdims=True))
        alpha = jnp.exp(m_old - m_new)
        p = jnp.exp(s - m_new)
        l_new = alpha * l_old + jnp.sum(p, axis=-1, keepdims=True)
        pv = lax.dot_general(
            p.reshape(ratio * q_tile, K_TILE).astype(jnp.bfloat16),
            v_blk,
            (((1,), (0,)), ((), ())),
            preferred_element_type=jnp.float32,
        )
        acc_new = alpha * acc_old + pv.reshape(ratio, q_tile, head_dim)
        return m_new, l_new, acc_new

    init = (
        jnp.full((ratio, q_tile, 1), neg_fill, jnp.float32),
        jnp.zeros((ratio, q_tile, 1), jnp.float32),
        jnp.zeros((ratio, q_tile, head_dim), jnp.float32),
    )
    m_fin, l_fin, acc_fin = lax.fori_loop(lo_ref[qb], hi_ref[qb] + 1, step, init)
    o_ref[0] = (acc_fin / l_fin).astype(o_ref.dtype)


def flash_attention(query_grouped, kv_all, q_index, q_begin):
    kv_heads, ratio, group_len, head_dim = query_grouped.shape
    n_rows = kv_all.shape[1]
    n_q = group_len // Q_TILE
    lo = jnp.min(q_begin.reshape(n_q, Q_TILE), axis=1) // K_TILE
    hi = jnp.max(q_index.reshape(n_q, Q_TILE), axis=1) // K_TILE
    grid_spec = pltpu.PrefetchScalarGridSpec(
        num_scalar_prefetch=2,
        grid=(kv_heads, n_q),
        in_specs=[
            pl.BlockSpec((1, ratio, Q_TILE, head_dim), lambda g, qb, lo, hi: (g, 0, qb, 0)),
            pl.BlockSpec((1, n_rows, head_dim), lambda g, qb, lo, hi: (g, 0, 0)),
            pl.BlockSpec((1, n_rows, head_dim), lambda g, qb, lo, hi: (kv_heads + g, 0, 0)),
            pl.BlockSpec((Q_TILE, 1), lambda g, qb, lo, hi: (qb, 0)),
            pl.BlockSpec((Q_TILE, 1), lambda g, qb, lo, hi: (qb, 0)),
        ],
        out_specs=pl.BlockSpec((1, ratio, Q_TILE, head_dim), lambda g, qb, lo, hi: (g, 0, qb, 0)),
    )
    out = pl.pallas_call(
        flash_body,
        grid_spec=grid_spec,
        out_shape=jax.ShapeDtypeStruct(query_grouped.shape, jnp.bfloat16),
    )(lo, hi, query_grouped, kv_all, kv_all, q_index[:, None], q_begin[:, None])
    return out


def body(
    tokens,
    seg_ids,
    routes,
    route_weights,
    norm1_gain,
    norm2_gain,
    w_query,
    key_weight,
    value_weight,
    w_out_attn,
    w_in,
    w_out,
    paged_key_value_cache,
    page_table,
):
    tok_dev = tokens.shape[0]
    ep_count = lax.axis_size("ep")
    group_len = tok_dev * ep_count
    req_pos = lax.axis_index("req")
    all_segs = gather_rows(seg_ids, ("req", "ep"))
    all_pos = positions_of(all_segs)
    group_start = req_pos * group_len
    group_pos = lax.dynamic_slice_in_dim(all_pos, group_start, group_len)
    group_seg = lax.dynamic_slice_in_dim(all_segs, group_start, group_len)
    normed = rms_scale(tokens.astype(jnp.float32), norm1_gain).astype(jnp.bfloat16)
    joined = jnp.concatenate([w_query, key_weight, value_weight], axis=1)
    projected = jnp.dot(
        gather_rows(normed, "ep"), joined, preferred_element_type=jnp.float32
    )
    query_width = w_query.shape[1]
    kv_width = key_weight.shape[1]
    q_heads = query_width // HEAD_SIZE
    kv_heads = kv_width // HEAD_SIZE
    heads_ratio = q_heads // kv_heads
    query_rows = rotary_apply(
        projected[:, :query_width].reshape(group_len, q_heads, HEAD_SIZE), group_pos
    ).astype(jnp.bfloat16)
    key_rows = rotary_apply(
        projected[:, query_width : query_width + kv_width].reshape(
            group_len, kv_heads, HEAD_SIZE
        ),
        group_pos,
    ).astype(jnp.bfloat16)
    value_rows = (
        projected[:, query_width + kv_width :]
        .astype(jnp.bfloat16)
        .reshape(group_len, kv_heads, HEAD_SIZE)
    )
    query_grouped = query_rows.reshape(group_len, kv_heads, heads_ratio, HEAD_SIZE).transpose(
        1, 2, 0, 3
    )
    kv_local = jnp.concatenate(
        [key_rows.transpose(1, 0, 2), value_rows.transpose(1, 0, 2)], axis=0
    )
    req_count = lax.axis_size("req")
    stream_len = group_len * req_count
    reach = min(req_count - 1, -(-(stream_len // 2 - 1) // group_len))
    pieces = [kv_local]
    for shift in range(1, reach + 1):
        pairs = [(src_at, src_at + shift) for src_at in range(req_count - shift)]
        pieces.insert(0, lax.ppermute(kv_local, "req", pairs))
    kv_window = jnp.concatenate(pieces, axis=1)
    window_base = (req_pos - reach) * group_len
    q_index = group_start + jnp.arange(group_len, dtype=jnp.int32)
    q_begin = q_index - group_pos
    head_out = flash_attention(
        query_grouped, kv_window, q_index - window_base, q_begin - window_base
    )
    kv_all = lax.all_gather(kv_local, "req", axis=1, tiled=True)
    n_rows = kv_all.shape[1]
    pages_here = paged_key_value_cache.shape[0]
    page_first = req_pos * pages_here
    piece_pages = n_rows // PAGE_TOKENS
    local_pages = page_first + jnp.arange(pages_here, dtype=jnp.int32)
    match = local_pages[:, None] == page_table[None, :]
    hit = jnp.any(match, axis=1)
    block_of = jnp.argmax(match, axis=1).astype(jnp.int32)
    kv_paged = kv_all.reshape(2, kv_heads, piece_pages, PAGE_TOKENS, HEAD_SIZE)
    picked = jnp.take(kv_paged, block_of, axis=2, mode="clip").transpose(2, 1, 0, 3, 4)
    new_cache = jnp.where(hit[:, None, None, None, None], picked, paged_key_value_cache)
    head_out = head_out.transpose(2, 0, 1, 3).reshape(group_len, query_width)
    attention = scatter_sum_rows(
        jnp.dot(head_out, w_out_attn, preferred_element_type=jnp.float32).astype(jnp.bfloat16),
        "ep",
    )
    attn_out = attention.astype(jnp.bfloat16)
    moe_in = rms_scale(tokens.astype(jnp.float32) + residual_scale * attention, norm2_gain).astype(
        jnp.bfloat16
    )
    ffe_width = w_out.shape[1]
    exp_here = w_in.shape[0]
    expert_ids = jnp.arange(E, dtype=jnp.int32)
    shares = jnp.sum(
        jnp.where(routes[:, :, None] == expert_ids[None, None, :], route_weights[:, :, None], 0.0),
        axis=1,
    )
    rows_all = gather_rows(moe_in, "ep")
    shares_all = gather_rows(shares, "ep")
    first_expert = lax.axis_index("ep") * exp_here
    shares_here = lax.dynamic_slice_in_dim(shares_all, first_expert, exp_here, 1)
    total_rows = rows_all.shape[0]
    chosen = (shares_here > 0.0).astype(jnp.int32).reshape(ep_count, tok_dev, exp_here)
    slot_in = jnp.cumsum(chosen, axis=1) - 1
    source_ids = jnp.arange(ep_count, dtype=jnp.int32)[:, None, None]
    local_slot = (source_ids * CAP + slot_in).reshape(total_rows, exp_here)
    live = (chosen > 0).reshape(total_rows, exp_here)
    slot_ids = jnp.arange(ep_count * CAP, dtype=jnp.int32)
    dispatch = (local_slot.T[:, None, :] == slot_ids[None, :, None]) & live.T[:, None, :]
    arrived = jnp.einsum(
        "esr,rd->esd", dispatch.astype(jnp.bfloat16), rows_all, preferred_element_type=jnp.float32
    ).astype(jnp.bfloat16)
    gate_up = jnp.einsum("esd,edf->esf", arrived, w_in, preferred_element_type=jnp.float32)
    activated = (jax.nn.silu(gate_up[..., :ffe_width]) * gate_up[..., ffe_width:]).astype(
        jnp.bfloat16
    )
    result = jnp.einsum(
        "esf,efd->esd", activated, w_out, preferred_element_type=jnp.float32
    ).astype(jnp.bfloat16)
    combine = jnp.where(dispatch, shares_here.T[:, None, :], 0.0)
    combine_hi = combine.astype(jnp.bfloat16)
    combine_lo = (combine - combine_hi.astype(jnp.float32)).astype(jnp.bfloat16)
    partial_rows = jnp.einsum(
        "esr,esd->rd", combine_hi, result, preferred_element_type=jnp.float32
    ) + jnp.einsum("esr,esd->rd", combine_lo, result, preferred_element_type=jnp.float32)
    moe_out = scatter_sum_rows(partial_rows.astype(jnp.bfloat16), "ep").astype(jnp.bfloat16)
    return (attn_out, moe_out, new_cache)


def solution(mesh):
    in_specs = (
        P(("req", "ep"), None),
        P(("req", "ep")),
        P(("req", "ep"), None),
        P(("req", "ep"), None),
        P(),
        P(),
        P(None, "ep"),
        P(None, "ep"),
        P(None, "ep"),
        P("ep", None),
        P("ep", None, None),
        P("ep", None, None),
        P("req", "ep", None, None, None),
        P(),
    )
    out_specs = (P(("req", "ep"), None), P(("req", "ep"), None), P("req", "ep", None, None, None))
    return jax.shard_map(body, mesh=mesh, in_specs=in_specs, out_specs=out_specs, check_vma=False)
```

```python
import jax
import jax.numpy as jnp
from jax import lax
from jax.sharding import PartitionSpec as P
from jax.experimental import pallas as pl
from jax.experimental.pallas import tpu as pltpu

HEAD_SIZE = 64
E = 40
PAGE_TOKENS = 64
CAP = 48


norm_eps = 1e-06
score_scale = 0.015625
residual_scale = 0.22
rope_base = 10000.0
neg_fill = -1e30


def rms_scale(rows, gain):
    mean_sq = jnp.mean(rows * rows, axis=-1, keepdims=True)
    return rows * lax.rsqrt(mean_sq + norm_eps) * gain


def positions_of(segments):
    tok_index = jnp.arange(segments.shape[0], dtype=jnp.int32)
    previous = jnp.concatenate([jnp.full((1,), -1, jnp.int32), segments[:-1]])
    starts = jnp.where(segments != previous, tok_index, 0)
    return tok_index - lax.cummax(starts, axis=0)


def rotary_apply(heads_in, token_positions):
    half_dim = heads_in.shape[-1] // 2
    inverse_freq = rope_base ** (
        -jnp.arange(half_dim, dtype=jnp.float32) * 2.0 / heads_in.shape[-1]
    )
    angles = token_positions.astype(jnp.float32)[:, None] * inverse_freq[None, :]
    cos_part = jnp.cos(angles)[:, None, :]
    sine_part = jnp.sin(angles)[:, None, :]
    first_half = heads_in[..., :half_dim]
    second_half = heads_in[..., half_dim:]
    return jnp.concatenate(
        [
            first_half * cos_part - second_half * sine_part,
            second_half * cos_part + first_half * sine_part,
        ],
        axis=-1,
    )


def gather_rows(x, axis_name, axis=0):
    count = lax.axis_size(axis_name)
    spread = jnp.broadcast_to(x[None], (count,) + x.shape)
    got = lax.all_to_all(spread, axis_name, 0, 0, tiled=True)
    got = jnp.moveaxis(got, 0, axis)
    shape = list(x.shape)
    shape[axis] = shape[axis] * count
    return got.reshape(shape)


def scatter_sum_rows(x, axis_name):
    count = lax.axis_size(axis_name)
    parts = x.reshape((count, x.shape[0] // count) + x.shape[1:])
    got = lax.all_to_all(parts, axis_name, 0, 0, tiled=True)
    return jnp.sum(got.astype(jnp.float32), axis=0)


def chip_pairs(count, shift):
    chips = count // 2
    return [(d, ((d // 2 + shift) % chips) * 2 + d % 2) for d in range(count)]


def gather_ep(x):
    count = lax.axis_size("ep")
    if count % 2:
        return gather_rows(x, "ep")
    chips = count // 2
    me = lax.axis_index("ep")
    chip = me // 2
    core = me % 2
    side = [x]
    for shift in range(1, chips):
        side.append(lax.ppermute(x, "ep", chip_pairs(count, shift)))
    side = jnp.stack(side)
    other = lax.ppermute(side, "ep", [(d, d ^ 1) for d in range(count)])
    both = jnp.where(core == 0, jnp.stack([side, other], 1), jnp.stack([other, side], 1))
    order = (chip - jnp.arange(chips, dtype=jnp.int32)) % chips
    full = jnp.take(both, order, axis=0, mode="clip")
    return full.reshape((count * x.shape[0],) + x.shape[1:])


def scatter_sum_ep(p):
    count = lax.axis_size("ep")
    if count % 2:
        return scatter_sum_rows(p, "ep")
    chips = count // 2
    me = lax.axis_index("ep")
    chip = me // 2
    core = me % 2
    rows = p.shape[0] // count
    parts = p.reshape((chips, 2, rows) + p.shape[1:])
    mine = jnp.where(core == 0, parts[:, 0], parts[:, 1])
    theirs = jnp.where(core == 0, parts[:, 1], parts[:, 0])
    got = lax.ppermute(theirs, "ep", [(d, d ^ 1) for d in range(count)])
    sums = mine.astype(jnp.float32) + got.astype(jnp.float32)
    total = lax.dynamic_index_in_dim(sums, chip, 0, keepdims=False)
    for shift in range(1, chips):
        piece = lax.dynamic_index_in_dim(sums, (chip + shift) % chips, 0, keepdims=False)
        total = total + lax.ppermute(
            piece.astype(jnp.bfloat16), "ep", chip_pairs(count, shift)
        ).astype(jnp.float32)
    return total


Q_TILE = 128
K_TILE = 256


def flash_body(lo_ref, hi_ref, q_ref, k_ref, v_ref, tok_ref, begin_ref, o_ref):
    qb = pl.program_id(1)
    ratio = q_ref.shape[1]
    q_tile = q_ref.shape[2]
    head_dim = q_ref.shape[3]
    q = q_ref[0].reshape(ratio * q_tile, head_dim)
    tok = tok_ref[...]
    begin = begin_ref[...]

    def step(kb, carry):
        m_old, l_old, acc_old = carry
        k0 = pl.multiple_of(kb * K_TILE, K_TILE)
        k_blk = k_ref[0, pl.ds(k0, K_TILE), :]
        v_blk = v_ref[0, pl.ds(k0, K_TILE), :]
        s = lax.dot_general(
            q, k_blk, (((1,), (1,)), ((), ())), preferred_element_type=jnp.float32
        )
        s = (s * score_scale).reshape(ratio, q_tile, K_TILE)
        key_at = k0 + lax.broadcasted_iota(jnp.int32, (q_tile, K_TILE), 1)
        allowed = (key_at >= begin) & (key_at <= tok)
        s = jnp.where(allowed[None], s, -jnp.inf)
        m_new = jnp.maximum(m_old, jnp.max(s, axis=-1, keepdims=True))
        alpha = jnp.exp(m_old - m_new)
        p = jnp.exp(s - m_new)
        l_new = alpha * l_old + jnp.sum(p, axis=-1, keepdims=True)
        pv = lax.dot_general(
            p.reshape(ratio * q_tile, K_TILE).astype(jnp.bfloat16),
            v_blk,
            (((1,), (0,)), ((), ())),
            preferred_element_type=jnp.float32,
        )
        acc_new = alpha * acc_old + pv.reshape(ratio, q_tile, head_dim)
        return m_new, l_new, acc_new

    init = (
        jnp.full((ratio, q_tile, 1), neg_fill, jnp.float32),
        jnp.zeros((ratio, q_tile, 1), jnp.float32),
        jnp.zeros((ratio, q_tile, head_dim), jnp.float32),
    )
    m_fin, l_fin, acc_fin = lax.fori_loop(lo_ref[qb], hi_ref[qb] + 1, step, init)
    o_ref[0] = (acc_fin / l_fin).astype(o_ref.dtype)


def flash_attention(query_grouped, kv_all, q_index, q_begin):
    kv_heads, ratio, group_len, head_dim = query_grouped.shape
    n_rows = kv_all.shape[1]
    n_q = group_len // Q_TILE
    lo = jnp.min(q_begin.reshape(n_q, Q_TILE), axis=1) // K_TILE
    hi = jnp.max(q_index.reshape(n_q, Q_TILE), axis=1) // K_TILE
    grid_spec = pltpu.PrefetchScalarGridSpec(
        num_scalar_prefetch=2,
        grid=(kv_heads, n_q),
        in_specs=[
            pl.BlockSpec((1, ratio, Q_TILE, head_dim), lambda g, qb, lo, hi: (g, 0, qb, 0)),
            pl.BlockSpec((1, n_rows, head_dim), lambda g, qb, lo, hi: (g, 0, 0)),
            pl.BlockSpec((1, n_rows, head_dim), lambda g, qb, lo, hi: (kv_heads + g, 0, 0)),
            pl.BlockSpec((Q_TILE, 1), lambda g, qb, lo, hi: (qb, 0)),
            pl.BlockSpec((Q_TILE, 1), lambda g, qb, lo, hi: (qb, 0)),
        ],
        out_specs=pl.BlockSpec((1, ratio, Q_TILE, head_dim), lambda g, qb, lo, hi: (g, 0, qb, 0)),
    )
    out = pl.pallas_call(
        flash_body,
        grid_spec=grid_spec,
        out_shape=jax.ShapeDtypeStruct(query_grouped.shape, jnp.bfloat16),
    )(lo, hi, query_grouped, kv_all, kv_all, q_index[:, None], q_begin[:, None])
    return out


def body(
    tokens,
    seg_ids,
    routes,
    route_weights,
    norm1_gain,
    norm2_gain,
    w_query,
    key_weight,
    value_weight,
    w_out_attn,
    w_in,
    w_out,
    paged_key_value_cache,
    page_table,
):
    tok_dev = tokens.shape[0]
    ep_count = lax.axis_size("ep")
    group_len = tok_dev * ep_count
    req_pos = lax.axis_index("req")
    all_segs = gather_rows(seg_ids, ("req", "ep"))
    all_pos = positions_of(all_segs)
    group_start = req_pos * group_len
    group_pos = lax.dynamic_slice_in_dim(all_pos, group_start, group_len)
    group_seg = lax.dynamic_slice_in_dim(all_segs, group_start, group_len)
    normed = rms_scale(tokens.astype(jnp.float32), norm1_gain).astype(jnp.bfloat16)
    joined = jnp.concatenate([w_query, key_weight, value_weight], axis=1)
    projected = jnp.dot(
        gather_ep(normed), joined, preferred_element_type=jnp.float32
    )
    query_width = w_query.shape[1]
    kv_width = key_weight.shape[1]
    q_heads = query_width // HEAD_SIZE
    kv_heads = kv_width // HEAD_SIZE
    heads_ratio = q_heads // kv_heads
    query_rows = rotary_apply(
        projected[:, :query_width].reshape(group_len, q_heads, HEAD_SIZE), group_pos
    ).astype(jnp.bfloat16)
    key_rows = rotary_apply(
        projected[:, query_width : query_width + kv_width].reshape(
            group_len, kv_heads, HEAD_SIZE
        ),
        group_pos,
    ).astype(jnp.bfloat16)
    value_rows = (
        projected[:, query_width + kv_width :]
        .astype(jnp.bfloat16)
        .reshape(group_len, kv_heads, HEAD_SIZE)
    )
    query_grouped = query_rows.reshape(group_len, kv_heads, heads_ratio, HEAD_SIZE).transpose(
        1, 2, 0, 3
    )
    kv_local = jnp.concatenate(
        [key_rows.transpose(1, 0, 2), value_rows.transpose(1, 0, 2)], axis=0
    )
    kv_all = gather_rows(kv_local, "req", axis=1)
    n_rows = kv_all.shape[1]
    q_index = group_start + jnp.arange(group_len, dtype=jnp.int32)
    q_begin = q_index - group_pos
    head_out = flash_attention(query_grouped, kv_all, q_index, q_begin)
    pages_here = paged_key_value_cache.shape[0]
    page_first = req_pos * pages_here
    piece_pages = n_rows // PAGE_TOKENS
    local_pages = page_first + jnp.arange(pages_here, dtype=jnp.int32)
    match = local_pages[:, None] == page_table[None, :]
    hit = jnp.any(match, axis=1)
    block_of = jnp.argmax(match, axis=1).astype(jnp.int32)
    kv_paged = kv_all.reshape(2, kv_heads, piece_pages, PAGE_TOKENS, HEAD_SIZE)
    picked = jnp.take(kv_paged, block_of, axis=2, mode="clip").transpose(2, 1, 0, 3, 4)
    new_cache = jnp.where(hit[:, None, None, None, None], picked, paged_key_value_cache)
    head_out = head_out.transpose(2, 0, 1, 3).reshape(group_len, query_width)
    attention = scatter_sum_ep(
        jnp.dot(head_out, w_out_attn, preferred_element_type=jnp.float32).astype(jnp.bfloat16)
    )
    attn_out = attention.astype(jnp.bfloat16)
    moe_in = rms_scale(tokens.astype(jnp.float32) + residual_scale * attention, norm2_gain).astype(
        jnp.bfloat16
    )
    ffe_width = w_out.shape[1]
    exp_here = w_in.shape[0]
    expert_ids = jnp.arange(E, dtype=jnp.int32)
    shares = jnp.sum(
        jnp.where(routes[:, :, None] == expert_ids[None, None, :], route_weights[:, :, None], 0.0),
        axis=1,
    )
    rows_all = gather_ep(moe_in)
    shares_all = gather_rows(shares, "ep")
    first_expert = lax.axis_index("ep") * exp_here
    shares_here = lax.dynamic_slice_in_dim(shares_all, first_expert, exp_here, 1)
    total_rows = rows_all.shape[0]
    chosen = (shares_here > 0.0).astype(jnp.int32).reshape(ep_count, tok_dev, exp_here)
    slot_in = jnp.cumsum(chosen, axis=1) - 1
    source_ids = jnp.arange(ep_count, dtype=jnp.int32)[:, None, None]
    local_slot = (source_ids * CAP + slot_in).reshape(total_rows, exp_here)
    live = (chosen > 0).reshape(total_rows, exp_here)
    slot_ids = jnp.arange(ep_count * CAP, dtype=jnp.int32)
    dispatch = (local_slot.T[:, None, :] == slot_ids[None, :, None]) & live.T[:, None, :]
    arrived = jnp.einsum(
        "esr,rd->esd", dispatch.astype(jnp.bfloat16), rows_all, preferred_element_type=jnp.float32
    ).astype(jnp.bfloat16)
    gate_up = jnp.einsum("esd,edf->esf", arrived, w_in, preferred_element_type=jnp.float32)
    activated = (jax.nn.silu(gate_up[..., :ffe_width]) * gate_up[..., ffe_width:]).astype(
        jnp.bfloat16
    )
    result = jnp.einsum(
        "esf,efd->esd", activated, w_out, preferred_element_type=jnp.float32
    ).astype(jnp.bfloat16)
    combine = jnp.where(dispatch, shares_here.T[:, None, :], 0.0)
    combine_hi = combine.astype(jnp.bfloat16)
    combine_lo = (combine - combine_hi.astype(jnp.float32)).astype(jnp.bfloat16)
    partial_rows = jnp.einsum(
        "esr,esd->rd", combine_hi, result, preferred_element_type=jnp.float32
    ) + jnp.einsum("esr,esd->rd", combine_lo, result, preferred_element_type=jnp.float32)
    moe_out = scatter_sum_ep(partial_rows.astype(jnp.bfloat16)).astype(jnp.bfloat16)
    return (attn_out, moe_out, new_cache)


def solution(mesh):
    in_specs = (
        P(("req", "ep"), None),
        P(("req", "ep")),
        P(("req", "ep"), None),
        P(("req", "ep"), None),
        P(),
        P(),
        P(None, "ep"),
        P(None, "ep"),
        P(None, "ep"),
        P("ep", None),
        P("ep", None, None),
        P("ep", None, None),
        P("req", "ep", None, None, None),
        P(),
    )
    out_specs = (P(("req", "ep"), None), P(("req", "ep"), None), P("req", "ep", None, None, None))
    return jax.shard_map(body, mesh=mesh, in_specs=in_specs, out_specs=out_specs, check_vma=False)
```

```python
import jax
import jax.numpy as jnp
from jax import lax
from jax.sharding import PartitionSpec as P
from jax.experimental import pallas as pl
from jax.experimental.pallas import tpu as pltpu

HEAD_SIZE = 64
E = 40
PAGE_TOKENS = 64
CAP = 48


norm_eps = 1e-06
score_scale = 0.015625
residual_scale = 0.22
rope_base = 10000.0
neg_fill = -1e30


def rms_scale(rows, gain):
    mean_sq = jnp.mean(rows * rows, axis=-1, keepdims=True)
    return rows * lax.rsqrt(mean_sq + norm_eps) * gain


def positions_of(segments):
    tok_index = jnp.arange(segments.shape[0], dtype=jnp.int32)
    previous = jnp.concatenate([jnp.full((1,), -1, jnp.int32), segments[:-1]])
    starts = jnp.where(segments != previous, tok_index, 0)
    return tok_index - lax.cummax(starts, axis=0)


def rotary_apply(heads_in, token_positions):
    half_dim = heads_in.shape[-1] // 2
    inverse_freq = rope_base ** (
        -jnp.arange(half_dim, dtype=jnp.float32) * 2.0 / heads_in.shape[-1]
    )
    angles = token_positions.astype(jnp.float32)[:, None] * inverse_freq[None, :]
    cos_part = jnp.cos(angles)[:, None, :]
    sine_part = jnp.sin(angles)[:, None, :]
    first_half = heads_in[..., :half_dim]
    second_half = heads_in[..., half_dim:]
    return jnp.concatenate(
        [
            first_half * cos_part - second_half * sine_part,
            second_half * cos_part + first_half * sine_part,
        ],
        axis=-1,
    )


def gather_rows(x, axis_name, axis=0):
    count = lax.axis_size(axis_name)
    spread = jnp.broadcast_to(x[None], (count,) + x.shape)
    got = lax.all_to_all(spread, axis_name, 0, 0, tiled=True)
    got = jnp.moveaxis(got, 0, axis)
    shape = list(x.shape)
    shape[axis] = shape[axis] * count
    return got.reshape(shape)


def scatter_sum_rows(x, axis_name):
    count = lax.axis_size(axis_name)
    parts = x.reshape((count, x.shape[0] // count) + x.shape[1:])
    got = lax.all_to_all(parts, axis_name, 0, 0, tiled=True)
    return jnp.sum(got.astype(jnp.float32), axis=0)


def chip_pairs(count, shift):
    chips = count // 2
    return [(d, ((d // 2 + shift) % chips) * 2 + d % 2) for d in range(count)]


def gather_ep(x):
    count = lax.axis_size("ep")
    if count % 2:
        return gather_rows(x, "ep")
    chips = count // 2
    me = lax.axis_index("ep")
    chip = me // 2
    core = me % 2
    side = [x]
    for shift in range(1, chips):
        side.append(lax.ppermute(x, "ep", chip_pairs(count, shift)))
    side = jnp.stack(side)
    other = lax.ppermute(side, "ep", [(d, d ^ 1) for d in range(count)])
    both = jnp.where(core == 0, jnp.stack([side, other], 1), jnp.stack([other, side], 1))
    order = (chip - jnp.arange(chips, dtype=jnp.int32)) % chips
    full = jnp.take(both, order, axis=0, mode="clip")
    return full.reshape((count * x.shape[0],) + x.shape[1:])


def scatter_sum_ep(p):
    count = lax.axis_size("ep")
    if count % 2:
        return scatter_sum_rows(p, "ep")
    chips = count // 2
    me = lax.axis_index("ep")
    chip = me // 2
    core = me % 2
    rows = p.shape[0] // count
    parts = p.reshape((chips, 2, rows) + p.shape[1:])
    mine = jnp.where(core == 0, parts[:, 0], parts[:, 1])
    theirs = jnp.where(core == 0, parts[:, 1], parts[:, 0])
    got = lax.ppermute(theirs, "ep", [(d, d ^ 1) for d in range(count)])
    sums = mine.astype(jnp.float32) + got.astype(jnp.float32)
    total = lax.dynamic_index_in_dim(sums, chip, 0, keepdims=False)
    for shift in range(1, chips):
        piece = lax.dynamic_index_in_dim(sums, (chip + shift) % chips, 0, keepdims=False)
        total = total + lax.ppermute(
            piece.astype(jnp.bfloat16), "ep", chip_pairs(count, shift)
        ).astype(jnp.float32)
    return total


Q_TILE = 128
K_TILE = 256


def flash_body(lo_ref, hi_ref, q_ref, k_ref, v_ref, tok_ref, begin_ref, o_ref):
    qb = pl.program_id(1)
    ratio = q_ref.shape[1]
    q_tile = q_ref.shape[2]
    head_dim = q_ref.shape[3]
    q = q_ref[0].reshape(ratio * q_tile, head_dim)
    tok = tok_ref[...]
    begin = begin_ref[...]

    def step(kb, carry):
        m_old, l_old, acc_old = carry
        k0 = pl.multiple_of(kb * K_TILE, K_TILE)
        k_blk = k_ref[0, pl.ds(k0, K_TILE), :]
        v_blk = v_ref[0, pl.ds(k0, K_TILE), :]
        s = lax.dot_general(
            q, k_blk, (((1,), (1,)), ((), ())), preferred_element_type=jnp.float32
        )
        s = (s * score_scale).reshape(ratio, q_tile, K_TILE)
        key_at = k0 + lax.broadcasted_iota(jnp.int32, (q_tile, K_TILE), 1)
        allowed = (key_at >= begin) & (key_at <= tok)
        s = jnp.where(allowed[None], s, -jnp.inf)
        m_new = jnp.maximum(m_old, jnp.max(s, axis=-1, keepdims=True))
        alpha = jnp.exp(m_old - m_new)
        p = jnp.exp(s - m_new)
        l_new = alpha * l_old + jnp.sum(p, axis=-1, keepdims=True)
        pv = lax.dot_general(
            p.reshape(ratio * q_tile, K_TILE).astype(jnp.bfloat16),
            v_blk,
            (((1,), (0,)), ((), ())),
            preferred_element_type=jnp.float32,
        )
        acc_new = alpha * acc_old + pv.reshape(ratio, q_tile, head_dim)
        return m_new, l_new, acc_new

    init = (
        jnp.full((ratio, q_tile, 1), neg_fill, jnp.float32),
        jnp.zeros((ratio, q_tile, 1), jnp.float32),
        jnp.zeros((ratio, q_tile, head_dim), jnp.float32),
    )
    m_fin, l_fin, acc_fin = lax.fori_loop(lo_ref[qb], hi_ref[qb] + 1, step, init)
    o_ref[0] = (acc_fin / l_fin).astype(o_ref.dtype)


def flash_attention(query_grouped, kv_all, q_index, q_begin):
    kv_heads, ratio, group_len, head_dim = query_grouped.shape
    n_rows = kv_all.shape[1]
    n_q = group_len // Q_TILE
    lo = jnp.min(q_begin.reshape(n_q, Q_TILE), axis=1) // K_TILE
    hi = jnp.max(q_index.reshape(n_q, Q_TILE), axis=1) // K_TILE
    grid_spec = pltpu.PrefetchScalarGridSpec(
        num_scalar_prefetch=2,
        grid=(kv_heads, n_q),
        in_specs=[
            pl.BlockSpec((1, ratio, Q_TILE, head_dim), lambda g, qb, lo, hi: (g, 0, qb, 0)),
            pl.BlockSpec((1, n_rows, head_dim), lambda g, qb, lo, hi: (g, 0, 0)),
            pl.BlockSpec((1, n_rows, head_dim), lambda g, qb, lo, hi: (kv_heads + g, 0, 0)),
            pl.BlockSpec((Q_TILE, 1), lambda g, qb, lo, hi: (qb, 0)),
            pl.BlockSpec((Q_TILE, 1), lambda g, qb, lo, hi: (qb, 0)),
        ],
        out_specs=pl.BlockSpec((1, ratio, Q_TILE, head_dim), lambda g, qb, lo, hi: (g, 0, qb, 0)),
    )
    out = pl.pallas_call(
        flash_body,
        grid_spec=grid_spec,
        out_shape=jax.ShapeDtypeStruct(query_grouped.shape, jnp.bfloat16),
    )(lo, hi, query_grouped, kv_all, kv_all, q_index[:, None], q_begin[:, None])
    return out


def body(
    tokens,
    seg_ids,
    routes,
    route_weights,
    norm1_gain,
    norm2_gain,
    w_query,
    key_weight,
    value_weight,
    w_out_attn,
    w_in,
    w_out,
    paged_key_value_cache,
    page_table,
):
    tok_dev = tokens.shape[0]
    ep_count = lax.axis_size("ep")
    group_len = tok_dev * ep_count
    req_pos = lax.axis_index("req")
    all_segs = gather_rows(seg_ids, ("req", "ep"))
    all_pos = positions_of(all_segs)
    group_start = req_pos * group_len
    group_pos = lax.dynamic_slice_in_dim(all_pos, group_start, group_len)
    group_seg = lax.dynamic_slice_in_dim(all_segs, group_start, group_len)
    normed = rms_scale(tokens.astype(jnp.float32), norm1_gain).astype(jnp.bfloat16)
    joined = jnp.concatenate([w_query, key_weight, value_weight], axis=1)
    projected = jnp.dot(
        gather_ep(normed), joined, preferred_element_type=jnp.float32
    )
    query_width = w_query.shape[1]
    kv_width = key_weight.shape[1]
    q_heads = query_width // HEAD_SIZE
    kv_heads = kv_width // HEAD_SIZE
    heads_ratio = q_heads // kv_heads
    query_rows = rotary_apply(
        projected[:, :query_width].reshape(group_len, q_heads, HEAD_SIZE), group_pos
    ).astype(jnp.bfloat16)
    key_rows = rotary_apply(
        projected[:, query_width : query_width + kv_width].reshape(
            group_len, kv_heads, HEAD_SIZE
        ),
        group_pos,
    ).astype(jnp.bfloat16)
    value_rows = (
        projected[:, query_width + kv_width :]
        .astype(jnp.bfloat16)
        .reshape(group_len, kv_heads, HEAD_SIZE)
    )
    query_grouped = query_rows.reshape(group_len, kv_heads, heads_ratio, HEAD_SIZE).transpose(
        1, 2, 0, 3
    )
    kv_local = jnp.concatenate(
        [key_rows.transpose(1, 0, 2), value_rows.transpose(1, 0, 2)], axis=0
    )
    req_count = lax.axis_size("req")
    stream_len = group_len * req_count
    reach = min(req_count - 1, -(-(stream_len // 2 - 1) // group_len))
    pieces = [kv_local]
    for shift in range(1, reach + 1):
        pairs = [(src_at, src_at + shift) for src_at in range(req_count - shift)]
        pieces.insert(0, lax.ppermute(kv_local, "req", pairs))
    kv_window = jnp.concatenate(pieces, axis=1)
    window_base = (req_pos - reach) * group_len
    q_index = group_start + jnp.arange(group_len, dtype=jnp.int32)
    q_begin = q_index - group_pos
    head_out = flash_attention(
        query_grouped, kv_window, q_index - window_base, q_begin - window_base
    )
    kv_all = gather_rows(kv_local, "req", axis=1)
    n_rows = kv_all.shape[1]
    pages_here = paged_key_value_cache.shape[0]
    page_first = req_pos * pages_here
    piece_pages = n_rows // PAGE_TOKENS
    local_pages = page_first + jnp.arange(pages_here, dtype=jnp.int32)
    match = local_pages[:, None] == page_table[None, :]
    hit = jnp.any(match, axis=1)
    block_of = jnp.argmax(match, axis=1).astype(jnp.int32)
    kv_paged = kv_all.reshape(2, kv_heads, piece_pages, PAGE_TOKENS, HEAD_SIZE)
    picked = jnp.take(kv_paged, block_of, axis=2, mode="clip").transpose(2, 1, 0, 3, 4)
    new_cache = jnp.where(hit[:, None, None, None, None], picked, paged_key_value_cache)
    head_out = head_out.transpose(2, 0, 1, 3).reshape(group_len, query_width)
    attention = scatter_sum_ep(
        jnp.dot(head_out, w_out_attn, preferred_element_type=jnp.float32).astype(jnp.bfloat16)
    )
    attn_out = attention.astype(jnp.bfloat16)
    moe_in = rms_scale(tokens.astype(jnp.float32) + residual_scale * attention, norm2_gain).astype(
        jnp.bfloat16
    )
    ffe_width = w_out.shape[1]
    exp_here = w_in.shape[0]
    expert_ids = jnp.arange(E, dtype=jnp.int32)
    shares = jnp.sum(
        jnp.where(routes[:, :, None] == expert_ids[None, None, :], route_weights[:, :, None], 0.0),
        axis=1,
    )
    rows_all = gather_ep(moe_in)
    shares_all = gather_rows(shares, "ep")
    first_expert = lax.axis_index("ep") * exp_here
    shares_here = lax.dynamic_slice_in_dim(shares_all, first_expert, exp_here, 1)
    total_rows = rows_all.shape[0]
    chosen = (shares_here > 0.0).astype(jnp.int32).reshape(ep_count, tok_dev, exp_here)
    slot_in = jnp.cumsum(chosen, axis=1) - 1
    source_ids = jnp.arange(ep_count, dtype=jnp.int32)[:, None, None]
    local_slot = (source_ids * CAP + slot_in).reshape(total_rows, exp_here)
    live = (chosen > 0).reshape(total_rows, exp_here)
    slot_ids = jnp.arange(ep_count * CAP, dtype=jnp.int32)
    dispatch = (local_slot.T[:, None, :] == slot_ids[None, :, None]) & live.T[:, None, :]
    arrived = jnp.einsum(
        "esr,rd->esd", dispatch.astype(jnp.bfloat16), rows_all, preferred_element_type=jnp.float32
    ).astype(jnp.bfloat16)
    gate_up = jnp.einsum("esd,edf->esf", arrived, w_in, preferred_element_type=jnp.float32)
    activated = (jax.nn.silu(gate_up[..., :ffe_width]) * gate_up[..., ffe_width:]).astype(
        jnp.bfloat16
    )
    result = jnp.einsum(
        "esf,efd->esd", activated, w_out, preferred_element_type=jnp.float32
    ).astype(jnp.bfloat16)
    combine = jnp.where(dispatch, shares_here.T[:, None, :], 0.0)
    combine_hi = combine.astype(jnp.bfloat16)
    combine_lo = (combine - combine_hi.astype(jnp.float32)).astype(jnp.bfloat16)
    partial_rows = jnp.einsum(
        "esr,esd->rd", combine_hi, result, preferred_element_type=jnp.float32
    ) + jnp.einsum("esr,esd->rd", combine_lo, result, preferred_element_type=jnp.float32)
    moe_out = scatter_sum_ep(partial_rows.astype(jnp.bfloat16)).astype(jnp.bfloat16)
    return (attn_out, moe_out, new_cache)


def solution(mesh):
    in_specs = (
        P(("req", "ep"), None),
        P(("req", "ep")),
        P(("req", "ep"), None),
        P(("req", "ep"), None),
        P(),
        P(),
        P(None, "ep"),
        P(None, "ep"),
        P(None, "ep"),
        P("ep", None),
        P("ep", None, None),
        P("ep", None, None),
        P("req", "ep", None, None, None),
        P(),
    )
    out_specs = (P(("req", "ep"), None), P(("req", "ep"), None), P("req", "ep", None, None, None))
    return jax.shard_map(body, mesh=mesh, in_specs=in_specs, out_specs=out_specs, check_vma=False)
```

```python
import jax
import jax.numpy as jnp
from jax import lax
from jax.sharding import PartitionSpec as P
from jax.experimental import pallas as pl
from jax.experimental.pallas import tpu as pltpu

HEAD_SIZE = 64
E = 40
PAGE_TOKENS = 64
CAP = 48


norm_eps = 1e-06
score_scale = 0.015625
residual_scale = 0.22
rope_base = 10000.0
neg_fill = -1e30


def rms_scale(rows, gain):
    mean_sq = jnp.mean(rows * rows, axis=-1, keepdims=True)
    return rows * lax.rsqrt(mean_sq + norm_eps) * gain


def positions_of(segments):
    tok_index = jnp.arange(segments.shape[0], dtype=jnp.int32)
    previous = jnp.concatenate([jnp.full((1,), -1, jnp.int32), segments[:-1]])
    starts = jnp.where(segments != previous, tok_index, 0)
    return tok_index - lax.cummax(starts, axis=0)


def rotary_apply(heads_in, token_positions):
    half_dim = heads_in.shape[-1] // 2
    inverse_freq = rope_base ** (
        -jnp.arange(half_dim, dtype=jnp.float32) * 2.0 / heads_in.shape[-1]
    )
    angles = token_positions.astype(jnp.float32)[:, None] * inverse_freq[None, :]
    cos_part = jnp.cos(angles)[:, None, :]
    sine_part = jnp.sin(angles)[:, None, :]
    first_half = heads_in[..., :half_dim]
    second_half = heads_in[..., half_dim:]
    return jnp.concatenate(
        [
            first_half * cos_part - second_half * sine_part,
            second_half * cos_part + first_half * sine_part,
        ],
        axis=-1,
    )


def gather_rows(x, axis_name, axis=0):
    count = lax.axis_size(axis_name)
    spread = jnp.broadcast_to(x[None], (count,) + x.shape)
    got = lax.all_to_all(spread, axis_name, 0, 0, tiled=True)
    got = jnp.moveaxis(got, 0, axis)
    shape = list(x.shape)
    shape[axis] = shape[axis] * count
    return got.reshape(shape)


def scatter_sum_rows(x, axis_name):
    count = lax.axis_size(axis_name)
    parts = x.reshape((count, x.shape[0] // count) + x.shape[1:])
    got = lax.all_to_all(parts, axis_name, 0, 0, tiled=True)
    return jnp.sum(got.astype(jnp.float32), axis=0)


def chip_pairs(count, shift):
    chips = count // 2
    return [(d, ((d // 2 + shift) % chips) * 2 + d % 2) for d in range(count)]


def gather_ep(x):
    count = lax.axis_size("ep")
    if count % 2:
        return gather_rows(x, "ep")
    chips = count // 2
    me = lax.axis_index("ep")
    chip = me // 2
    core = me % 2
    side = [x]
    for shift in range(1, chips):
        side.append(lax.ppermute(x, "ep", chip_pairs(count, shift)))
    side = jnp.stack(side)
    other = lax.ppermute(side, "ep", [(d, d ^ 1) for d in range(count)])
    both = jnp.where(core == 0, jnp.stack([side, other], 1), jnp.stack([other, side], 1))
    order = (chip - jnp.arange(chips, dtype=jnp.int32)) % chips
    full = jnp.take(both, order, axis=0, mode="clip")
    return full.reshape((count * x.shape[0],) + x.shape[1:])


def scatter_sum_ep(p):
    count = lax.axis_size("ep")
    if count % 2:
        return scatter_sum_rows(p, "ep")
    chips = count // 2
    me = lax.axis_index("ep")
    chip = me // 2
    core = me % 2
    rows = p.shape[0] // count
    parts = p.reshape((chips, 2, rows) + p.shape[1:])
    mine = jnp.where(core == 0, parts[:, 0], parts[:, 1])
    theirs = jnp.where(core == 0, parts[:, 1], parts[:, 0])
    got = lax.ppermute(theirs, "ep", [(d, d ^ 1) for d in range(count)])
    sums = mine.astype(jnp.float32) + got.astype(jnp.float32)
    total = lax.dynamic_index_in_dim(sums, chip, 0, keepdims=False)
    for shift in range(1, chips):
        piece = lax.dynamic_index_in_dim(sums, (chip + shift) % chips, 0, keepdims=False)
        total = total + lax.ppermute(
            piece.astype(jnp.bfloat16), "ep", chip_pairs(count, shift)
        ).astype(jnp.float32)
    return total


Q_TILE = 128
K_TILE = 256


def flash_body(lo_ref, hi_ref, q_ref, k_ref, v_ref, tok_ref, begin_ref, o_ref):
    qb = pl.program_id(1)
    ratio = q_ref.shape[1]
    q_tile = q_ref.shape[2]
    head_dim = q_ref.shape[3]
    q = q_ref[0].reshape(ratio * q_tile, head_dim)
    tok = tok_ref[...]
    begin = begin_ref[...]

    def step(kb, carry):
        m_old, l_old, acc_old = carry
        k0 = pl.multiple_of(kb * K_TILE, K_TILE)
        k_blk = k_ref[0, pl.ds(k0, K_TILE), :]
        v_blk = v_ref[0, pl.ds(k0, K_TILE), :]
        s = lax.dot_general(
            q, k_blk, (((1,), (1,)), ((), ())), preferred_element_type=jnp.float32
        )
        s = (s * score_scale).reshape(ratio, q_tile, K_TILE)
        key_at = k0 + lax.broadcasted_iota(jnp.int32, (q_tile, K_TILE), 1)
        allowed = (key_at >= begin) & (key_at <= tok)
        s = jnp.where(allowed[None], s, -jnp.inf)
        m_new = jnp.maximum(m_old, jnp.max(s, axis=-1, keepdims=True))
        alpha = jnp.exp(m_old - m_new)
        p = jnp.exp(s - m_new)
        l_new = alpha * l_old + jnp.sum(p, axis=-1, keepdims=True)
        pv = lax.dot_general(
            p.reshape(ratio * q_tile, K_TILE).astype(jnp.bfloat16),
            v_blk,
            (((1,), (0,)), ((), ())),
            preferred_element_type=jnp.float32,
        )
        acc_new = alpha * acc_old + pv.reshape(ratio, q_tile, head_dim)
        return m_new, l_new, acc_new

    init = (
        jnp.full((ratio, q_tile, 1), neg_fill, jnp.float32),
        jnp.zeros((ratio, q_tile, 1), jnp.float32),
        jnp.zeros((ratio, q_tile, head_dim), jnp.float32),
    )
    m_fin, l_fin, acc_fin = lax.fori_loop(lo_ref[qb], hi_ref[qb] + 1, step, init)
    o_ref[0] = (acc_fin / l_fin).astype(o_ref.dtype)


def flash_attention(query_grouped, kv_all, q_index, q_begin):
    kv_heads, ratio, group_len, head_dim = query_grouped.shape
    n_rows = kv_all.shape[1]
    n_q = group_len // Q_TILE
    lo = jnp.min(q_begin.reshape(n_q, Q_TILE), axis=1) // K_TILE
    hi = jnp.max(q_index.reshape(n_q, Q_TILE), axis=1) // K_TILE
    grid_spec = pltpu.PrefetchScalarGridSpec(
        num_scalar_prefetch=2,
        grid=(kv_heads, n_q),
        in_specs=[
            pl.BlockSpec((1, ratio, Q_TILE, head_dim), lambda g, qb, lo, hi: (g, 0, qb, 0)),
            pl.BlockSpec((1, n_rows, head_dim), lambda g, qb, lo, hi: (g, 0, 0)),
            pl.BlockSpec((1, n_rows, head_dim), lambda g, qb, lo, hi: (kv_heads + g, 0, 0)),
            pl.BlockSpec((Q_TILE, 1), lambda g, qb, lo, hi: (qb, 0)),
            pl.BlockSpec((Q_TILE, 1), lambda g, qb, lo, hi: (qb, 0)),
        ],
        out_specs=pl.BlockSpec((1, ratio, Q_TILE, head_dim), lambda g, qb, lo, hi: (g, 0, qb, 0)),
    )
    out = pl.pallas_call(
        flash_body,
        grid_spec=grid_spec,
        out_shape=jax.ShapeDtypeStruct(query_grouped.shape, jnp.bfloat16),
    )(lo, hi, query_grouped, kv_all, kv_all, q_index[:, None], q_begin[:, None])
    return out


def body(
    tokens,
    seg_ids,
    routes,
    route_weights,
    norm1_gain,
    norm2_gain,
    w_query,
    key_weight,
    value_weight,
    w_out_attn,
    w_in,
    w_out,
    paged_key_value_cache,
    page_table,
):
    tok_dev = tokens.shape[0]
    ep_count = lax.axis_size("ep")
    group_len = tok_dev * ep_count
    req_pos = lax.axis_index("req")
    all_segs = gather_rows(seg_ids, ("req", "ep"))
    all_pos = positions_of(all_segs)
    group_start = req_pos * group_len
    group_pos = lax.dynamic_slice_in_dim(all_pos, group_start, group_len)
    group_seg = lax.dynamic_slice_in_dim(all_segs, group_start, group_len)
    normed = rms_scale(tokens.astype(jnp.float32), norm1_gain).astype(jnp.bfloat16)
    joined = jnp.concatenate([w_query, key_weight, value_weight], axis=1)
    projected = jnp.dot(
        gather_ep(normed), joined, preferred_element_type=jnp.float32
    )
    query_width = w_query.shape[1]
    kv_width = key_weight.shape[1]
    q_heads = query_width // HEAD_SIZE
    kv_heads = kv_width // HEAD_SIZE
    heads_ratio = q_heads // kv_heads
    query_rows = rotary_apply(
        projected[:, :query_width].reshape(group_len, q_heads, HEAD_SIZE), group_pos
    ).astype(jnp.bfloat16)
    key_rows = rotary_apply(
        projected[:, query_width : query_width + kv_width].reshape(
            group_len, kv_heads, HEAD_SIZE
        ),
        group_pos,
    ).astype(jnp.bfloat16)
    value_rows = (
        projected[:, query_width + kv_width :]
        .astype(jnp.bfloat16)
        .reshape(group_len, kv_heads, HEAD_SIZE)
    )
    query_grouped = query_rows.reshape(group_len, kv_heads, heads_ratio, HEAD_SIZE).transpose(
        1, 2, 0, 3
    )
    kv_local = jnp.concatenate(
        [key_rows.transpose(1, 0, 2), value_rows.transpose(1, 0, 2)], axis=0
    )
    req_count = lax.axis_size("req")
    stream_len = group_len * req_count
    reach = min(req_count - 1, -(-(stream_len // 2 - 1) // group_len))

    def shifted(data, shift):
        pairs = [(src_at, (src_at + shift) % req_count) for src_at in range(req_count)]
        return lax.ppermute(data, "req", pairs)

    by_shift = [kv_local] + [shifted(kv_local, shift) for shift in range(1, reach + 1)]
    kv_window = jnp.concatenate(by_shift[::-1], axis=1)
    window_base = (req_pos - reach) * group_len
    q_index = group_start + jnp.arange(group_len, dtype=jnp.int32)
    q_begin = q_index - group_pos
    head_out = flash_attention(
        query_grouped, kv_window, q_index - window_base, q_begin - window_base
    )
    kv_late, _ = lax.optimization_barrier((kv_local, kv_window))
    by_shift = by_shift + [shifted(kv_late, shift) for shift in range(reach + 1, req_count)]
    pages_here = paged_key_value_cache.shape[0]
    page_first = req_pos * pages_here
    group_pages = group_len // PAGE_TOKENS
    local_pages = page_first + jnp.arange(pages_here, dtype=jnp.int32)
    match = local_pages[:, None] == page_table[None, :]
    hit = jnp.any(match, axis=1)
    block_of = jnp.argmax(match, axis=1).astype(jnp.int32)
    shift_of = (req_pos - block_of // group_pages) % req_count
    kv_stack = jnp.stack(by_shift).reshape(
        req_count, 2, kv_heads, group_pages, PAGE_TOKENS, HEAD_SIZE
    )
    picked = kv_stack[shift_of, :, :, block_of % group_pages].transpose(0, 2, 1, 3, 4)
    new_cache = jnp.where(hit[:, None, None, None, None], picked, paged_key_value_cache)
    head_out = head_out.transpose(2, 0, 1, 3).reshape(group_len, query_width)
    attention = scatter_sum_ep(
        jnp.dot(head_out, w_out_attn, preferred_element_type=jnp.float32).astype(jnp.bfloat16)
    )
    attn_out = attention.astype(jnp.bfloat16)
    moe_in = rms_scale(tokens.astype(jnp.float32) + residual_scale * attention, norm2_gain).astype(
        jnp.bfloat16
    )
    ffe_width = w_out.shape[1]
    exp_here = w_in.shape[0]
    expert_ids = jnp.arange(E, dtype=jnp.int32)
    shares = jnp.sum(
        jnp.where(routes[:, :, None] == expert_ids[None, None, :], route_weights[:, :, None], 0.0),
        axis=1,
    )
    rows_all = gather_ep(moe_in)
    shares_all = gather_rows(shares, "ep")
    first_expert = lax.axis_index("ep") * exp_here
    shares_here = lax.dynamic_slice_in_dim(shares_all, first_expert, exp_here, 1)
    total_rows = rows_all.shape[0]
    chosen = (shares_here > 0.0).astype(jnp.int32).reshape(ep_count, tok_dev, exp_here)
    slot_in = jnp.cumsum(chosen, axis=1) - 1
    source_ids = jnp.arange(ep_count, dtype=jnp.int32)[:, None, None]
    local_slot = (source_ids * CAP + slot_in).reshape(total_rows, exp_here)
    live = (chosen > 0).reshape(total_rows, exp_here)
    slot_ids = jnp.arange(ep_count * CAP, dtype=jnp.int32)
    dispatch = (local_slot.T[:, None, :] == slot_ids[None, :, None]) & live.T[:, None, :]
    arrived = jnp.einsum(
        "esr,rd->esd", dispatch.astype(jnp.bfloat16), rows_all, preferred_element_type=jnp.float32
    ).astype(jnp.bfloat16)
    gate_up = jnp.einsum("esd,edf->esf", arrived, w_in, preferred_element_type=jnp.float32)
    activated = (jax.nn.silu(gate_up[..., :ffe_width]) * gate_up[..., ffe_width:]).astype(
        jnp.bfloat16
    )
    result = jnp.einsum(
        "esf,efd->esd", activated, w_out, preferred_element_type=jnp.float32
    ).astype(jnp.bfloat16)
    combine = jnp.where(dispatch, shares_here.T[:, None, :], 0.0)
    combine_hi = combine.astype(jnp.bfloat16)
    combine_lo = (combine - combine_hi.astype(jnp.float32)).astype(jnp.bfloat16)
    partial_rows = jnp.einsum(
        "esr,esd->rd", combine_hi, result, preferred_element_type=jnp.float32
    ) + jnp.einsum("esr,esd->rd", combine_lo, result, preferred_element_type=jnp.float32)
    moe_out = scatter_sum_ep(partial_rows.astype(jnp.bfloat16)).astype(jnp.bfloat16)
    return (attn_out, moe_out, new_cache)


def solution(mesh):
    in_specs = (
        P(("req", "ep"), None),
        P(("req", "ep")),
        P(("req", "ep"), None),
        P(("req", "ep"), None),
        P(),
        P(),
        P(None, "ep"),
        P(None, "ep"),
        P(None, "ep"),
        P("ep", None),
        P("ep", None, None),
        P("ep", None, None),
        P("req", "ep", None, None, None),
        P(),
    )
    out_specs = (P(("req", "ep"), None), P(("req", "ep"), None), P("req", "ep", None, None, None))
    return jax.shard_map(body, mesh=mesh, in_specs=in_specs, out_specs=out_specs, check_vma=False)
```

```python
import jax
import jax.numpy as jnp
from jax import lax
from jax.sharding import PartitionSpec as P
from jax.experimental import pallas as pl
from jax.experimental.pallas import tpu as pltpu

HEAD_SIZE = 64
E = 40
PAGE_TOKENS = 64
CAP = 48


norm_eps = 1e-06
score_scale = 0.015625
residual_scale = 0.22
rope_base = 10000.0
neg_fill = -1e30


def rms_scale(rows, gain):
    mean_sq = jnp.mean(rows * rows, axis=-1, keepdims=True)
    return rows * lax.rsqrt(mean_sq + norm_eps) * gain


def positions_of(segments):
    tok_index = jnp.arange(segments.shape[0], dtype=jnp.int32)
    previous = jnp.concatenate([jnp.full((1,), -1, jnp.int32), segments[:-1]])
    starts = jnp.where(segments != previous, tok_index, 0)
    return tok_index - lax.cummax(starts, axis=0)


def rotary_apply(heads_in, token_positions):
    half_dim = heads_in.shape[-1] // 2
    inverse_freq = rope_base ** (
        -jnp.arange(half_dim, dtype=jnp.float32) * 2.0 / heads_in.shape[-1]
    )
    angles = token_positions.astype(jnp.float32)[:, None] * inverse_freq[None, :]
    cos_part = jnp.cos(angles)[:, None, :]
    sine_part = jnp.sin(angles)[:, None, :]
    first_half = heads_in[..., :half_dim]
    second_half = heads_in[..., half_dim:]
    return jnp.concatenate(
        [
            first_half * cos_part - second_half * sine_part,
            second_half * cos_part + first_half * sine_part,
        ],
        axis=-1,
    )


def gather_rows(x, axis_name, axis=0):
    count = lax.axis_size(axis_name)
    spread = jnp.broadcast_to(x[None], (count,) + x.shape)
    got = lax.all_to_all(spread, axis_name, 0, 0, tiled=True)
    got = jnp.moveaxis(got, 0, axis)
    shape = list(x.shape)
    shape[axis] = shape[axis] * count
    return got.reshape(shape)


def scatter_sum_rows(x, axis_name):
    count = lax.axis_size(axis_name)
    parts = x.reshape((count, x.shape[0] // count) + x.shape[1:])
    got = lax.all_to_all(parts, axis_name, 0, 0, tiled=True)
    return jnp.sum(got.astype(jnp.float32), axis=0)


def chip_pairs(count, shift):
    chips = count // 2
    return [(d, ((d // 2 + shift) % chips) * 2 + d % 2) for d in range(count)]


def gather_ep(x):
    count = lax.axis_size("ep")
    if count % 2:
        return gather_rows(x, "ep")
    chips = count // 2
    me = lax.axis_index("ep")
    chip = me // 2
    core = me % 2
    side = [x]
    for shift in range(1, chips):
        side.append(lax.ppermute(x, "ep", chip_pairs(count, shift)))
    side = jnp.stack(side)
    other = lax.ppermute(side, "ep", [(d, d ^ 1) for d in range(count)])
    both = jnp.where(core == 0, jnp.stack([side, other], 1), jnp.stack([other, side], 1))
    order = (chip - jnp.arange(chips, dtype=jnp.int32)) % chips
    full = jnp.take(both, order, axis=0, mode="clip")
    return full.reshape((count * x.shape[0],) + x.shape[1:])


def scatter_sum_ep(p):
    count = lax.axis_size("ep")
    if count % 2:
        return scatter_sum_rows(p, "ep")
    chips = count // 2
    me = lax.axis_index("ep")
    chip = me // 2
    core = me % 2
    rows = p.shape[0] // count
    parts = p.reshape((chips, 2, rows) + p.shape[1:])
    mine = jnp.where(core == 0, parts[:, 0], parts[:, 1])
    theirs = jnp.where(core == 0, parts[:, 1], parts[:, 0])
    got = lax.ppermute(theirs, "ep", [(d, d ^ 1) for d in range(count)])
    sums = mine.astype(jnp.float32) + got.astype(jnp.float32)
    total = lax.dynamic_index_in_dim(sums, chip, 0, keepdims=False)
    for shift in range(1, chips):
        piece = lax.dynamic_index_in_dim(sums, (chip + shift) % chips, 0, keepdims=False)
        total = total + lax.ppermute(
            piece.astype(jnp.bfloat16), "ep", chip_pairs(count, shift)
        ).astype(jnp.float32)
    return total


Q_TILE = 128
K_TILE = 256


def flash_body(lo_ref, hi_ref, q_ref, k_ref, v_ref, tok_ref, begin_ref, o_ref):
    qb = pl.program_id(1)
    ratio = q_ref.shape[1]
    q_tile = q_ref.shape[2]
    head_dim = q_ref.shape[3]
    q = q_ref[0].reshape(ratio * q_tile, head_dim)
    tok = tok_ref[...]
    begin = begin_ref[...]

    def step(kb, carry):
        m_old, l_old, acc_old = carry
        k0 = pl.multiple_of(kb * K_TILE, K_TILE)
        k_blk = k_ref[0, pl.ds(k0, K_TILE), :]
        v_blk = v_ref[0, pl.ds(k0, K_TILE), :]
        s = lax.dot_general(
            q, k_blk, (((1,), (1,)), ((), ())), preferred_element_type=jnp.float32
        )
        s = (s * score_scale).reshape(ratio, q_tile, K_TILE)
        key_at = k0 + lax.broadcasted_iota(jnp.int32, (q_tile, K_TILE), 1)
        allowed = (key_at >= begin) & (key_at <= tok)
        s = jnp.where(allowed[None], s, -jnp.inf)
        m_new = jnp.maximum(m_old, jnp.max(s, axis=-1, keepdims=True))
        alpha = jnp.exp(m_old - m_new)
        p = jnp.exp(s - m_new)
        l_new = alpha * l_old + jnp.sum(p, axis=-1, keepdims=True)
        pv = lax.dot_general(
            p.reshape(ratio * q_tile, K_TILE).astype(jnp.bfloat16),
            v_blk,
            (((1,), (0,)), ((), ())),
            preferred_element_type=jnp.float32,
        )
        acc_new = alpha * acc_old + pv.reshape(ratio, q_tile, head_dim)
        return m_new, l_new, acc_new

    init = (
        jnp.full((ratio, q_tile, 1), neg_fill, jnp.float32),
        jnp.zeros((ratio, q_tile, 1), jnp.float32),
        jnp.zeros((ratio, q_tile, head_dim), jnp.float32),
    )
    m_fin, l_fin, acc_fin = lax.fori_loop(lo_ref[qb], hi_ref[qb] + 1, step, init)
    o_ref[0] = (acc_fin / l_fin).astype(o_ref.dtype)


def flash_attention(query_grouped, kv_all, q_index, q_begin):
    kv_heads, ratio, group_len, head_dim = query_grouped.shape
    n_rows = kv_all.shape[1]
    n_q = group_len // Q_TILE
    lo = jnp.min(q_begin.reshape(n_q, Q_TILE), axis=1) // K_TILE
    hi = jnp.max(q_index.reshape(n_q, Q_TILE), axis=1) // K_TILE
    grid_spec = pltpu.PrefetchScalarGridSpec(
        num_scalar_prefetch=2,
        grid=(kv_heads, n_q),
        in_specs=[
            pl.BlockSpec((1, ratio, Q_TILE, head_dim), lambda g, qb, lo, hi: (g, 0, qb, 0)),
            pl.BlockSpec((1, n_rows, head_dim), lambda g, qb, lo, hi: (g, 0, 0)),
            pl.BlockSpec((1, n_rows, head_dim), lambda g, qb, lo, hi: (kv_heads + g, 0, 0)),
            pl.BlockSpec((Q_TILE, 1), lambda g, qb, lo, hi: (qb, 0)),
            pl.BlockSpec((Q_TILE, 1), lambda g, qb, lo, hi: (qb, 0)),
        ],
        out_specs=pl.BlockSpec((1, ratio, Q_TILE, head_dim), lambda g, qb, lo, hi: (g, 0, qb, 0)),
    )
    out = pl.pallas_call(
        flash_body,
        grid_spec=grid_spec,
        out_shape=jax.ShapeDtypeStruct(query_grouped.shape, jnp.bfloat16),
    )(lo, hi, query_grouped, kv_all, kv_all, q_index[:, None], q_begin[:, None])
    return out


def body(
    tokens,
    seg_ids,
    routes,
    route_weights,
    norm1_gain,
    norm2_gain,
    w_query,
    key_weight,
    value_weight,
    w_out_attn,
    w_in,
    w_out,
    paged_key_value_cache,
    page_table,
):
    tok_dev = tokens.shape[0]
    ep_count = lax.axis_size("ep")
    group_len = tok_dev * ep_count
    req_pos = lax.axis_index("req")
    all_segs = gather_rows(seg_ids, ("req", "ep"))
    all_pos = positions_of(all_segs)
    group_start = req_pos * group_len
    group_pos = lax.dynamic_slice_in_dim(all_pos, group_start, group_len)
    group_seg = lax.dynamic_slice_in_dim(all_segs, group_start, group_len)
    normed = rms_scale(tokens.astype(jnp.float32), norm1_gain).astype(jnp.bfloat16)
    joined = jnp.concatenate([w_query, key_weight, value_weight], axis=1)
    projected = jnp.dot(
        gather_ep(normed), joined, preferred_element_type=jnp.float32
    )
    query_width = w_query.shape[1]
    kv_width = key_weight.shape[1]
    q_heads = query_width // HEAD_SIZE
    kv_heads = kv_width // HEAD_SIZE
    heads_ratio = q_heads // kv_heads
    query_rows = rotary_apply(
        projected[:, :query_width].reshape(group_len, q_heads, HEAD_SIZE), group_pos
    ).astype(jnp.bfloat16)
    key_rows = rotary_apply(
        projected[:, query_width : query_width + kv_width].reshape(
            group_len, kv_heads, HEAD_SIZE
        ),
        group_pos,
    ).astype(jnp.bfloat16)
    value_rows = (
        projected[:, query_width + kv_width :]
        .astype(jnp.bfloat16)
        .reshape(group_len, kv_heads, HEAD_SIZE)
    )
    query_grouped = query_rows.reshape(group_len, kv_heads, heads_ratio, HEAD_SIZE).transpose(
        1, 2, 0, 3
    )
    kv_local = jnp.concatenate(
        [key_rows.transpose(1, 0, 2), value_rows.transpose(1, 0, 2)], axis=0
    )
    kv_all = gather_rows(kv_local, "req", axis=1)
    n_rows = kv_all.shape[1]
    q_index = group_start + jnp.arange(group_len, dtype=jnp.int32)
    q_begin = q_index - group_pos
    head_out = flash_attention(query_grouped, kv_all, q_index, q_begin)
    pages_here = paged_key_value_cache.shape[0]
    page_first = req_pos * pages_here
    piece_pages = n_rows // PAGE_TOKENS
    local_pages = page_first + jnp.arange(pages_here, dtype=jnp.int32)
    match = local_pages[:, None] == page_table[None, :]
    hit = jnp.any(match, axis=1)
    block_of = jnp.argmax(match, axis=1).astype(jnp.int32)
    kv_paged = kv_all.reshape(2, kv_heads, piece_pages, PAGE_TOKENS, HEAD_SIZE)
    picked = jnp.take(kv_paged, block_of, axis=2, mode="clip").transpose(2, 1, 0, 3, 4)
    new_cache = jnp.where(hit[:, None, None, None, None], picked, paged_key_value_cache)
    head_out = head_out.transpose(2, 0, 1, 3).reshape(group_len, query_width)
    attention = scatter_sum_ep(
        jnp.dot(head_out, w_out_attn, preferred_element_type=jnp.float32).astype(jnp.bfloat16)
    )
    attn_out = attention.astype(jnp.bfloat16)
    moe_in = rms_scale(tokens.astype(jnp.float32) + residual_scale * attention, norm2_gain).astype(
        jnp.bfloat16
    )
    ffe_width = w_out.shape[1]
    exp_here = w_in.shape[0]
    expert_ids = jnp.arange(E, dtype=jnp.int32)
    shares = jnp.sum(
        jnp.where(routes[:, :, None] == expert_ids[None, None, :], route_weights[:, :, None], 0.0),
        axis=1,
    )
    rows_all = gather_ep(moe_in)
    shares_all = gather_rows(shares, "ep")
    first_expert = lax.axis_index("ep") * exp_here
    shares_here = lax.dynamic_slice_in_dim(shares_all, first_expert, exp_here, 1)
    total_rows = rows_all.shape[0]
    chosen = (shares_here > 0.0).astype(jnp.int32).reshape(ep_count, tok_dev, exp_here)
    slot_in = jnp.cumsum(chosen, axis=1) - 1
    source_ids = jnp.arange(ep_count, dtype=jnp.int32)[:, None, None]
    local_slot = (source_ids * CAP + slot_in).reshape(total_rows, exp_here)
    live = (chosen > 0).reshape(total_rows, exp_here)
    slot_ids = jnp.arange(ep_count * CAP, dtype=jnp.int32)
    dispatch = (local_slot.T[:, None, :] == slot_ids[None, :, None]) & live.T[:, None, :]
    arrived = jnp.einsum(
        "esr,rd->esd", dispatch.astype(jnp.bfloat16), rows_all, preferred_element_type=jnp.float32
    ).astype(jnp.bfloat16)
    gate_up = jnp.einsum("esd,edf->esf", arrived, w_in, preferred_element_type=jnp.float32)
    activated = (jax.nn.silu(gate_up[..., :ffe_width]) * gate_up[..., ffe_width:]).astype(
        jnp.bfloat16
    )
    result = jnp.einsum(
        "esf,efd->esd", activated, w_out, preferred_element_type=jnp.float32
    ).astype(jnp.bfloat16)
    combine = jnp.where(dispatch, shares_here.T[:, None, :], 0.0)
    partial_rows = jnp.einsum(
        "esr,esd->rd", combine.astype(jnp.bfloat16), result, preferred_element_type=jnp.float32
    )
    moe_out = scatter_sum_ep(partial_rows.astype(jnp.bfloat16)).astype(jnp.bfloat16)
    return (attn_out, moe_out, new_cache)


def solution(mesh):
    in_specs = (
        P(("req", "ep"), None),
        P(("req", "ep")),
        P(("req", "ep"), None),
        P(("req", "ep"), None),
        P(),
        P(),
        P(None, "ep"),
        P(None, "ep"),
        P(None, "ep"),
        P("ep", None),
        P("ep", None, None),
        P("ep", None, None),
        P("req", "ep", None, None, None),
        P(),
    )
    out_specs = (P(("req", "ep"), None), P(("req", "ep"), None), P("req", "ep", None, None, None))
    return jax.shard_map(body, mesh=mesh, in_specs=in_specs, out_specs=out_specs, check_vma=False)
```

```python
import jax
import jax.numpy as jnp
from jax import lax
from jax.sharding import PartitionSpec as P
from jax.experimental import pallas as pl
from jax.experimental.pallas import tpu as pltpu

HEAD_SIZE = 64
E = 40
PAGE_TOKENS = 64
CAP = 48


norm_eps = 1e-06
score_scale = 0.015625
residual_scale = 0.22
rope_base = 10000.0
neg_fill = -1e30


def rms_scale(rows, gain):
    mean_sq = jnp.mean(rows * rows, axis=-1, keepdims=True)
    return rows * lax.rsqrt(mean_sq + norm_eps) * gain


def positions_of(segments):
    tok_index = jnp.arange(segments.shape[0], dtype=jnp.int32)
    previous = jnp.concatenate([jnp.full((1,), -1, jnp.int32), segments[:-1]])
    starts = jnp.where(segments != previous, tok_index, 0)
    return tok_index - lax.cummax(starts, axis=0)


def rotary_apply(heads_in, token_positions):
    half_dim = heads_in.shape[-1] // 2
    inverse_freq = rope_base ** (
        -jnp.arange(half_dim, dtype=jnp.float32) * 2.0 / heads_in.shape[-1]
    )
    angles = token_positions.astype(jnp.float32)[:, None] * inverse_freq[None, :]
    cos_part = jnp.cos(angles)[:, None, :]
    sine_part = jnp.sin(angles)[:, None, :]
    first_half = heads_in[..., :half_dim]
    second_half = heads_in[..., half_dim:]
    return jnp.concatenate(
        [
            first_half * cos_part - second_half * sine_part,
            second_half * cos_part + first_half * sine_part,
        ],
        axis=-1,
    )


def gather_rows(x, axis_name, axis=0):
    count = lax.axis_size(axis_name)
    spread = jnp.broadcast_to(x[None], (count,) + x.shape)
    got = lax.all_to_all(spread, axis_name, 0, 0, tiled=True)
    got = jnp.moveaxis(got, 0, axis)
    shape = list(x.shape)
    shape[axis] = shape[axis] * count
    return got.reshape(shape)


def scatter_sum_rows(x, axis_name):
    count = lax.axis_size(axis_name)
    parts = x.reshape((count, x.shape[0] // count) + x.shape[1:])
    got = lax.all_to_all(parts, axis_name, 0, 0, tiled=True)
    return jnp.sum(got.astype(jnp.float32), axis=0)


def chip_pairs(count, shift):
    chips = count // 2
    return [(d, ((d // 2 + shift) % chips) * 2 + d % 2) for d in range(count)]


def gather_ep(x):
    count = lax.axis_size("ep")
    if count % 2:
        return gather_rows(x, "ep")
    chips = count // 2
    me = lax.axis_index("ep")
    chip = me // 2
    core = me % 2
    side = [x]
    for shift in range(1, chips):
        side.append(lax.ppermute(x, "ep", chip_pairs(count, shift)))
    side = jnp.stack(side)
    other = lax.ppermute(side, "ep", [(d, d ^ 1) for d in range(count)])
    both = jnp.where(core == 0, jnp.stack([side, other], 1), jnp.stack([other, side], 1))
    order = (chip - jnp.arange(chips, dtype=jnp.int32)) % chips
    full = jnp.take(both, order, axis=0, mode="clip")
    return full.reshape((count * x.shape[0],) + x.shape[1:])


def scatter_sum_ep(p):
    count = lax.axis_size("ep")
    if count % 2:
        return scatter_sum_rows(p, "ep")
    chips = count // 2
    me = lax.axis_index("ep")
    chip = me // 2
    core = me % 2
    rows = p.shape[0] // count
    parts = p.reshape((chips, 2, rows) + p.shape[1:])
    mine = jnp.where(core == 0, parts[:, 0], parts[:, 1])
    theirs = jnp.where(core == 0, parts[:, 1], parts[:, 0])
    got = lax.ppermute(theirs, "ep", [(d, d ^ 1) for d in range(count)])
    sums = mine.astype(jnp.float32) + got.astype(jnp.float32)
    total = lax.dynamic_index_in_dim(sums, chip, 0, keepdims=False)
    for shift in range(1, chips):
        piece = lax.dynamic_index_in_dim(sums, (chip + shift) % chips, 0, keepdims=False)
        total = total + lax.ppermute(
            piece.astype(jnp.bfloat16), "ep", chip_pairs(count, shift)
        ).astype(jnp.float32)
    return total


Q_TILE = 128
K_TILE = 256


def flash_body(lo_ref, hi_ref, q_ref, k_ref, v_ref, tok_ref, begin_ref, o_ref):
    qb = pl.program_id(1)
    ratio = q_ref.shape[1]
    q_tile = q_ref.shape[2]
    head_dim = q_ref.shape[3]
    q = q_ref[0].reshape(ratio * q_tile, head_dim)
    tok = tok_ref[...]
    begin = begin_ref[...]

    def step(kb, carry):
        m_old, l_old, acc_old = carry
        k0 = pl.multiple_of(kb * K_TILE, K_TILE)
        k_blk = k_ref[0, pl.ds(k0, K_TILE), :]
        v_blk = v_ref[0, pl.ds(k0, K_TILE), :]
        s = lax.dot_general(
            q, k_blk, (((1,), (1,)), ((), ())), preferred_element_type=jnp.float32
        )
        s = (s * score_scale).reshape(ratio, q_tile, K_TILE)
        key_at = k0 + lax.broadcasted_iota(jnp.int32, (q_tile, K_TILE), 1)
        allowed = (key_at >= begin) & (key_at <= tok)
        s = jnp.where(allowed[None], s, -jnp.inf)
        m_new = jnp.maximum(m_old, jnp.max(s, axis=-1, keepdims=True))
        alpha = jnp.exp(m_old - m_new)
        p = jnp.exp(s - m_new)
        l_new = alpha * l_old + jnp.sum(p, axis=-1, keepdims=True)
        pv = lax.dot_general(
            p.reshape(ratio * q_tile, K_TILE).astype(jnp.bfloat16),
            v_blk,
            (((1,), (0,)), ((), ())),
            preferred_element_type=jnp.float32,
        )
        acc_new = alpha * acc_old + pv.reshape(ratio, q_tile, head_dim)
        return m_new, l_new, acc_new

    init = (
        jnp.full((ratio, q_tile, 1), neg_fill, jnp.float32),
        jnp.zeros((ratio, q_tile, 1), jnp.float32),
        jnp.zeros((ratio, q_tile, head_dim), jnp.float32),
    )
    m_fin, l_fin, acc_fin = lax.fori_loop(lo_ref[qb], hi_ref[qb] + 1, step, init)
    o_ref[0] = (acc_fin / l_fin).astype(o_ref.dtype)


def flash_attention(query_grouped, kv_all, q_index, q_begin):
    kv_heads, ratio, group_len, head_dim = query_grouped.shape
    n_rows = kv_all.shape[1]
    n_q = group_len // Q_TILE
    lo = jnp.min(q_begin.reshape(n_q, Q_TILE), axis=1) // K_TILE
    hi = jnp.max(q_index.reshape(n_q, Q_TILE), axis=1) // K_TILE
    grid_spec = pltpu.PrefetchScalarGridSpec(
        num_scalar_prefetch=2,
        grid=(kv_heads, n_q),
        in_specs=[
            pl.BlockSpec((1, ratio, Q_TILE, head_dim), lambda g, qb, lo, hi: (g, 0, qb, 0)),
            pl.BlockSpec((1, n_rows, head_dim), lambda g, qb, lo, hi: (g, 0, 0)),
            pl.BlockSpec((1, n_rows, head_dim), lambda g, qb, lo, hi: (kv_heads + g, 0, 0)),
            pl.BlockSpec((Q_TILE, 1), lambda g, qb, lo, hi: (qb, 0)),
            pl.BlockSpec((Q_TILE, 1), lambda g, qb, lo, hi: (qb, 0)),
        ],
        out_specs=pl.BlockSpec((1, ratio, Q_TILE, head_dim), lambda g, qb, lo, hi: (g, 0, qb, 0)),
    )
    out = pl.pallas_call(
        flash_body,
        grid_spec=grid_spec,
        out_shape=jax.ShapeDtypeStruct(query_grouped.shape, jnp.bfloat16),
    )(lo, hi, query_grouped, kv_all, kv_all, q_index[:, None], q_begin[:, None])
    return out


def body(
    tokens,
    seg_ids,
    routes,
    route_weights,
    norm1_gain,
    norm2_gain,
    w_query,
    key_weight,
    value_weight,
    w_out_attn,
    w_in,
    w_out,
    paged_key_value_cache,
    page_table,
):
    tok_dev = tokens.shape[0]
    ep_count = lax.axis_size("ep")
    group_len = tok_dev * ep_count
    req_pos = lax.axis_index("req")
    all_segs = gather_rows(seg_ids, ("req", "ep"))
    all_pos = positions_of(all_segs)
    group_start = req_pos * group_len
    group_pos = lax.dynamic_slice_in_dim(all_pos, group_start, group_len)
    group_seg = lax.dynamic_slice_in_dim(all_segs, group_start, group_len)
    normed = rms_scale(tokens.astype(jnp.float32), norm1_gain).astype(jnp.bfloat16)
    joined = jnp.concatenate([w_query, key_weight, value_weight], axis=1)
    projected = jnp.dot(
        gather_ep(normed), joined, preferred_element_type=jnp.float32
    )
    query_width = w_query.shape[1]
    kv_width = key_weight.shape[1]
    q_heads = query_width // HEAD_SIZE
    kv_heads = kv_width // HEAD_SIZE
    heads_ratio = q_heads // kv_heads
    query_rows = rotary_apply(
        projected[:, :query_width].reshape(group_len, q_heads, HEAD_SIZE), group_pos
    ).astype(jnp.bfloat16)
    key_rows = rotary_apply(
        projected[:, query_width : query_width + kv_width].reshape(
            group_len, kv_heads, HEAD_SIZE
        ),
        group_pos,
    ).astype(jnp.bfloat16)
    value_rows = (
        projected[:, query_width + kv_width :]
        .astype(jnp.bfloat16)
        .reshape(group_len, kv_heads, HEAD_SIZE)
    )
    query_grouped = query_rows.reshape(group_len, kv_heads, heads_ratio, HEAD_SIZE).transpose(
        1, 2, 0, 3
    )
    kv_local = jnp.concatenate(
        [key_rows.transpose(1, 0, 2), value_rows.transpose(1, 0, 2)], axis=0
    )
    req_count = lax.axis_size("req")
    stream_len = group_len * req_count
    reach = min(req_count - 1, -(-(stream_len // 2 - 1) // group_len))
    pieces = [kv_local]
    for shift in range(1, reach + 1):
        pairs = [(src_at, src_at + shift) for src_at in range(req_count - shift)]
        pieces.insert(0, lax.ppermute(kv_local, "req", pairs))
    kv_window = jnp.concatenate(pieces, axis=1)
    window_base = (req_pos - reach) * group_len
    q_index = group_start + jnp.arange(group_len, dtype=jnp.int32)
    q_begin = q_index - group_pos
    head_out = flash_attention(
        query_grouped, kv_window, q_index - window_base, q_begin - window_base
    )
    kv_all = lax.all_gather(kv_local, "req", axis=1, tiled=True)
    n_rows = kv_all.shape[1]
    pages_here = paged_key_value_cache.shape[0]
    page_first = req_pos * pages_here
    piece_pages = n_rows // PAGE_TOKENS
    local_pages = page_first + jnp.arange(pages_here, dtype=jnp.int32)
    match = local_pages[:, None] == page_table[None, :]
    hit = jnp.any(match, axis=1)
    block_of = jnp.argmax(match, axis=1).astype(jnp.int32)
    kv_paged = kv_all.reshape(2, kv_heads, piece_pages, PAGE_TOKENS, HEAD_SIZE)
    picked = jnp.take(kv_paged, block_of, axis=2, mode="clip").transpose(2, 1, 0, 3, 4)
    new_cache = jnp.where(hit[:, None, None, None, None], picked, paged_key_value_cache)
    head_out = head_out.transpose(2, 0, 1, 3).reshape(group_len, query_width)
    attention = scatter_sum_ep(
        jnp.dot(head_out, w_out_attn, preferred_element_type=jnp.float32).astype(jnp.bfloat16)
    )
    attn_out = attention.astype(jnp.bfloat16)
    moe_in = rms_scale(tokens.astype(jnp.float32) + residual_scale * attention, norm2_gain).astype(
        jnp.bfloat16
    )
    ffe_width = w_out.shape[1]
    exp_here = w_in.shape[0]
    expert_ids = jnp.arange(E, dtype=jnp.int32)
    shares = jnp.sum(
        jnp.where(routes[:, :, None] == expert_ids[None, None, :], route_weights[:, :, None], 0.0),
        axis=1,
    )
    rows_all = gather_ep(moe_in)
    rows_all, kv_all = lax.optimization_barrier((rows_all, kv_all))
    shares_all = gather_rows(shares, "ep")
    first_expert = lax.axis_index("ep") * exp_here
    shares_here = lax.dynamic_slice_in_dim(shares_all, first_expert, exp_here, 1)
    total_rows = rows_all.shape[0]
    chosen = (shares_here > 0.0).astype(jnp.int32).reshape(ep_count, tok_dev, exp_here)
    slot_in = jnp.cumsum(chosen, axis=1) - 1
    source_ids = jnp.arange(ep_count, dtype=jnp.int32)[:, None, None]
    local_slot = (source_ids * CAP + slot_in).reshape(total_rows, exp_here)
    live = (chosen > 0).reshape(total_rows, exp_here)
    slot_ids = jnp.arange(ep_count * CAP, dtype=jnp.int32)
    dispatch = (local_slot.T[:, None, :] == slot_ids[None, :, None]) & live.T[:, None, :]
    arrived = jnp.einsum(
        "esr,rd->esd", dispatch.astype(jnp.bfloat16), rows_all, preferred_element_type=jnp.float32
    ).astype(jnp.bfloat16)
    gate_up = jnp.einsum("esd,edf->esf", arrived, w_in, preferred_element_type=jnp.float32)
    activated = (jax.nn.silu(gate_up[..., :ffe_width]) * gate_up[..., ffe_width:]).astype(
        jnp.bfloat16
    )
    result = jnp.einsum(
        "esf,efd->esd", activated, w_out, preferred_element_type=jnp.float32
    ).astype(jnp.bfloat16)
    combine = jnp.where(dispatch, shares_here.T[:, None, :], 0.0)
    partial_rows = jnp.einsum(
        "esr,esd->rd", combine.astype(jnp.bfloat16), result, preferred_element_type=jnp.float32
    )
    moe_out = scatter_sum_ep(partial_rows.astype(jnp.bfloat16)).astype(jnp.bfloat16)
    return (attn_out, moe_out, new_cache)


def solution(mesh):
    in_specs = (
        P(("req", "ep"), None),
        P(("req", "ep")),
        P(("req", "ep"), None),
        P(("req", "ep"), None),
        P(),
        P(),
        P(None, "ep"),
        P(None, "ep"),
        P(None, "ep"),
        P("ep", None),
        P("ep", None, None),
        P("ep", None, None),
        P("req", "ep", None, None, None),
        P(),
    )
    out_specs = (P(("req", "ep"), None), P(("req", "ep"), None), P("req", "ep", None, None, None))
    return jax.shard_map(body, mesh=mesh, in_specs=in_specs, out_specs=out_specs, check_vma=False)
```

```python
import jax
import jax.numpy as jnp
from jax import lax
from jax.sharding import PartitionSpec as P
from jax.experimental import pallas as pl
from jax.experimental.pallas import tpu as pltpu

HEAD_SIZE = 64
E = 40
PAGE_TOKENS = 64
CAP = 48


norm_eps = 1e-06
score_scale = 0.015625
residual_scale = 0.22
rope_base = 10000.0
neg_fill = -1e30


def rms_scale(rows, gain):
    mean_sq = jnp.mean(rows * rows, axis=-1, keepdims=True)
    return rows * lax.rsqrt(mean_sq + norm_eps) * gain


def positions_of(segments):
    tok_index = jnp.arange(segments.shape[0], dtype=jnp.int32)
    previous = jnp.concatenate([jnp.full((1,), -1, jnp.int32), segments[:-1]])
    starts = jnp.where(segments != previous, tok_index, 0)
    return tok_index - lax.cummax(starts, axis=0)


def rotary_apply(heads_in, token_positions):
    half_dim = heads_in.shape[-1] // 2
    inverse_freq = rope_base ** (
        -jnp.arange(half_dim, dtype=jnp.float32) * 2.0 / heads_in.shape[-1]
    )
    angles = token_positions.astype(jnp.float32)[:, None] * inverse_freq[None, :]
    cos_part = jnp.cos(angles)[:, None, :]
    sine_part = jnp.sin(angles)[:, None, :]
    first_half = heads_in[..., :half_dim]
    second_half = heads_in[..., half_dim:]
    return jnp.concatenate(
        [
            first_half * cos_part - second_half * sine_part,
            second_half * cos_part + first_half * sine_part,
        ],
        axis=-1,
    )


def gather_rows(x, axis_name, axis=0):
    count = lax.axis_size(axis_name)
    spread = jnp.broadcast_to(x[None], (count,) + x.shape)
    got = lax.all_to_all(spread, axis_name, 0, 0, tiled=True)
    got = jnp.moveaxis(got, 0, axis)
    shape = list(x.shape)
    shape[axis] = shape[axis] * count
    return got.reshape(shape)


def scatter_sum_rows(x, axis_name):
    count = lax.axis_size(axis_name)
    parts = x.reshape((count, x.shape[0] // count) + x.shape[1:])
    got = lax.all_to_all(parts, axis_name, 0, 0, tiled=True)
    return jnp.sum(got.astype(jnp.float32), axis=0)


def chip_pairs(count, shift):
    chips = count // 2
    return [(d, ((d // 2 + shift) % chips) * 2 + d % 2) for d in range(count)]


def gather_ep(x):
    count = lax.axis_size("ep")
    if count % 2:
        return gather_rows(x, "ep")
    chips = count // 2
    me = lax.axis_index("ep")
    chip = me // 2
    core = me % 2
    side = [x]
    for shift in range(1, chips):
        side.append(lax.ppermute(x, "ep", chip_pairs(count, shift)))
    side = jnp.stack(side)
    other = lax.ppermute(side, "ep", [(d, d ^ 1) for d in range(count)])
    both = jnp.where(core == 0, jnp.stack([side, other], 1), jnp.stack([other, side], 1))
    order = (chip - jnp.arange(chips, dtype=jnp.int32)) % chips
    full = jnp.take(both, order, axis=0, mode="clip")
    return full.reshape((count * x.shape[0],) + x.shape[1:])


def scatter_sum_ep(p):
    count = lax.axis_size("ep")
    if count % 2:
        return scatter_sum_rows(p, "ep")
    chips = count // 2
    me = lax.axis_index("ep")
    chip = me // 2
    core = me % 2
    rows = p.shape[0] // count
    parts = p.reshape((chips, 2, rows) + p.shape[1:])
    mine = jnp.where(core == 0, parts[:, 0], parts[:, 1])
    theirs = jnp.where(core == 0, parts[:, 1], parts[:, 0])
    got = lax.ppermute(theirs, "ep", [(d, d ^ 1) for d in range(count)])
    sums = mine.astype(jnp.float32) + got.astype(jnp.float32)
    total = lax.dynamic_index_in_dim(sums, chip, 0, keepdims=False)
    for shift in range(1, chips):
        piece = lax.dynamic_index_in_dim(sums, (chip + shift) % chips, 0, keepdims=False)
        total = total + lax.ppermute(
            piece.astype(jnp.bfloat16), "ep", chip_pairs(count, shift)
        ).astype(jnp.float32)
    return total


Q_TILE = 128
K_TILE = 256


def flash_body(lo_ref, hi_ref, q_ref, k_ref, v_ref, tok_ref, begin_ref, o_ref):
    qb = pl.program_id(1)
    ratio = q_ref.shape[1]
    q_tile = q_ref.shape[2]
    head_dim = q_ref.shape[3]
    q = q_ref[0].reshape(ratio * q_tile, head_dim)
    tok = tok_ref[...]
    begin = begin_ref[...]

    def step(kb, carry):
        m_old, l_old, acc_old = carry
        k0 = pl.multiple_of(kb * K_TILE, K_TILE)
        k_blk = k_ref[0, pl.ds(k0, K_TILE), :]
        v_blk = v_ref[0, pl.ds(k0, K_TILE), :]
        s = lax.dot_general(
            q, k_blk, (((1,), (1,)), ((), ())), preferred_element_type=jnp.float32
        )
        s = (s * score_scale).reshape(ratio, q_tile, K_TILE)
        key_at = k0 + lax.broadcasted_iota(jnp.int32, (q_tile, K_TILE), 1)
        allowed = (key_at >= begin) & (key_at <= tok)
        s = jnp.where(allowed[None], s, -jnp.inf)
        m_new = jnp.maximum(m_old, jnp.max(s, axis=-1, keepdims=True))
        alpha = jnp.exp(m_old - m_new)
        p = jnp.exp(s - m_new)
        l_new = alpha * l_old + jnp.sum(p, axis=-1, keepdims=True)
        pv = lax.dot_general(
            p.reshape(ratio * q_tile, K_TILE).astype(jnp.bfloat16),
            v_blk,
            (((1,), (0,)), ((), ())),
            preferred_element_type=jnp.float32,
        )
        acc_new = alpha * acc_old + pv.reshape(ratio, q_tile, head_dim)
        return m_new, l_new, acc_new

    init = (
        jnp.full((ratio, q_tile, 1), neg_fill, jnp.float32),
        jnp.zeros((ratio, q_tile, 1), jnp.float32),
        jnp.zeros((ratio, q_tile, head_dim), jnp.float32),
    )
    m_fin, l_fin, acc_fin = lax.fori_loop(lo_ref[qb], hi_ref[qb] + 1, step, init)
    o_ref[0] = (acc_fin / l_fin).astype(o_ref.dtype)


def flash_attention(query_grouped, kv_all, q_index, q_begin):
    kv_heads, ratio, group_len, head_dim = query_grouped.shape
    n_rows = kv_all.shape[1]
    n_q = group_len // Q_TILE
    lo = jnp.min(q_begin.reshape(n_q, Q_TILE), axis=1) // K_TILE
    hi = jnp.max(q_index.reshape(n_q, Q_TILE), axis=1) // K_TILE
    grid_spec = pltpu.PrefetchScalarGridSpec(
        num_scalar_prefetch=2,
        grid=(kv_heads, n_q),
        in_specs=[
            pl.BlockSpec((1, ratio, Q_TILE, head_dim), lambda g, qb, lo, hi: (g, 0, qb, 0)),
            pl.BlockSpec((1, n_rows, head_dim), lambda g, qb, lo, hi: (g, 0, 0)),
            pl.BlockSpec((1, n_rows, head_dim), lambda g, qb, lo, hi: (kv_heads + g, 0, 0)),
            pl.BlockSpec((Q_TILE, 1), lambda g, qb, lo, hi: (qb, 0)),
            pl.BlockSpec((Q_TILE, 1), lambda g, qb, lo, hi: (qb, 0)),
        ],
        out_specs=pl.BlockSpec((1, ratio, Q_TILE, head_dim), lambda g, qb, lo, hi: (g, 0, qb, 0)),
    )
    out = pl.pallas_call(
        flash_body,
        grid_spec=grid_spec,
        out_shape=jax.ShapeDtypeStruct(query_grouped.shape, jnp.bfloat16),
    )(lo, hi, query_grouped, kv_all, kv_all, q_index[:, None], q_begin[:, None])
    return out


def body(
    tokens,
    seg_ids,
    routes,
    route_weights,
    norm1_gain,
    norm2_gain,
    w_query,
    key_weight,
    value_weight,
    w_out_attn,
    w_in,
    w_out,
    paged_key_value_cache,
    page_table,
):
    tok_dev = tokens.shape[0]
    ep_count = lax.axis_size("ep")
    group_len = tok_dev * ep_count
    req_pos = lax.axis_index("req")
    normed = rms_scale(tokens.astype(jnp.float32), norm1_gain).astype(jnp.bfloat16)
    seg_ids, normed = lax.optimization_barrier((seg_ids, normed))
    all_segs = gather_rows(seg_ids, ("req", "ep"))
    all_pos = positions_of(all_segs)
    group_start = req_pos * group_len
    group_pos = lax.dynamic_slice_in_dim(all_pos, group_start, group_len)
    joined = jnp.concatenate([w_query, key_weight, value_weight], axis=1)
    projected = jnp.dot(
        gather_ep(normed), joined, preferred_element_type=jnp.float32
    )
    query_width = w_query.shape[1]
    kv_width = key_weight.shape[1]
    q_heads = query_width // HEAD_SIZE
    kv_heads = kv_width // HEAD_SIZE
    heads_ratio = q_heads // kv_heads
    query_rows = rotary_apply(
        projected[:, :query_width].reshape(group_len, q_heads, HEAD_SIZE), group_pos
    ).astype(jnp.bfloat16)
    key_rows = rotary_apply(
        projected[:, query_width : query_width + kv_width].reshape(
            group_len, kv_heads, HEAD_SIZE
        ),
        group_pos,
    ).astype(jnp.bfloat16)
    value_rows = (
        projected[:, query_width + kv_width :]
        .astype(jnp.bfloat16)
        .reshape(group_len, kv_heads, HEAD_SIZE)
    )
    query_grouped = query_rows.reshape(group_len, kv_heads, heads_ratio, HEAD_SIZE).transpose(
        1, 2, 0, 3
    )
    kv_local = jnp.concatenate(
        [key_rows.transpose(1, 0, 2), value_rows.transpose(1, 0, 2)], axis=0
    )
    kv_all = gather_rows(kv_local, "req", axis=1)
    n_rows = kv_all.shape[1]
    q_index = group_start + jnp.arange(group_len, dtype=jnp.int32)
    q_begin = q_index - group_pos
    head_out = flash_attention(query_grouped, kv_all, q_index, q_begin)
    pages_here = paged_key_value_cache.shape[0]
    page_first = req_pos * pages_here
    piece_pages = n_rows // PAGE_TOKENS
    local_pages = page_first + jnp.arange(pages_here, dtype=jnp.int32)
    match = local_pages[:, None] == page_table[None, :]
    hit = jnp.any(match, axis=1)
    block_of = jnp.argmax(match, axis=1).astype(jnp.int32)
    kv_paged = kv_all.reshape(2, kv_heads, piece_pages, PAGE_TOKENS, HEAD_SIZE)
    picked = jnp.take(kv_paged, block_of, axis=2, mode="clip").transpose(2, 1, 0, 3, 4)
    new_cache = jnp.where(hit[:, None, None, None, None], picked, paged_key_value_cache)
    head_out = head_out.transpose(2, 0, 1, 3).reshape(group_len, query_width)
    attention = scatter_sum_ep(
        jnp.dot(head_out, w_out_attn, preferred_element_type=jnp.float32).astype(jnp.bfloat16)
    )
    attn_out = attention.astype(jnp.bfloat16)
    moe_in = rms_scale(tokens.astype(jnp.float32) + residual_scale * attention, norm2_gain).astype(
        jnp.bfloat16
    )
    ffe_width = w_out.shape[1]
    exp_here = w_in.shape[0]
    expert_ids = jnp.arange(E, dtype=jnp.int32)
    shares = jnp.sum(
        jnp.where(routes[:, :, None] == expert_ids[None, None, :], route_weights[:, :, None], 0.0),
        axis=1,
    )
    rows_all = gather_ep(moe_in)
    shares_all = gather_rows(shares, "ep")
    first_expert = lax.axis_index("ep") * exp_here
    shares_here = lax.dynamic_slice_in_dim(shares_all, first_expert, exp_here, 1)
    total_rows = rows_all.shape[0]
    chosen = (shares_here > 0.0).astype(jnp.int32).reshape(ep_count, tok_dev, exp_here)
    slot_in = jnp.cumsum(chosen, axis=1) - 1
    source_ids = jnp.arange(ep_count, dtype=jnp.int32)[:, None, None]
    local_slot = (source_ids * CAP + slot_in).reshape(total_rows, exp_here)
    live = (chosen > 0).reshape(total_rows, exp_here)
    slot_ids = jnp.arange(ep_count * CAP, dtype=jnp.int32)
    dispatch = (local_slot.T[:, None, :] == slot_ids[None, :, None]) & live.T[:, None, :]
    arrived = jnp.einsum(
        "esr,rd->esd", dispatch.astype(jnp.bfloat16), rows_all, preferred_element_type=jnp.float32
    ).astype(jnp.bfloat16)
    gate_up = jnp.einsum("esd,edf->esf", arrived, w_in, preferred_element_type=jnp.float32)
    activated = (jax.nn.silu(gate_up[..., :ffe_width]) * gate_up[..., ffe_width:]).astype(
        jnp.bfloat16
    )
    result = jnp.einsum(
        "esf,efd->esd", activated, w_out, preferred_element_type=jnp.float32
    ).astype(jnp.bfloat16)
    combine = jnp.where(dispatch, shares_here.T[:, None, :], 0.0)
    partial_rows = jnp.einsum(
        "esr,esd->rd", combine.astype(jnp.bfloat16), result, preferred_element_type=jnp.float32
    )
    moe_out = scatter_sum_ep(partial_rows.astype(jnp.bfloat16)).astype(jnp.bfloat16)
    return (attn_out, moe_out, new_cache)


def solution(mesh):
    in_specs = (
        P(("req", "ep"), None),
        P(("req", "ep")),
        P(("req", "ep"), None),
        P(("req", "ep"), None),
        P(),
        P(),
        P(None, "ep"),
        P(None, "ep"),
        P(None, "ep"),
        P("ep", None),
        P("ep", None, None),
        P("ep", None, None),
        P("req", "ep", None, None, None),
        P(),
    )
    out_specs = (P(("req", "ep"), None), P(("req", "ep"), None), P("req", "ep", None, None, None))
    return jax.shard_map(body, mesh=mesh, in_specs=in_specs, out_specs=out_specs, check_vma=False)
```

```python
import jax
import jax.numpy as jnp
from jax import lax
from jax.sharding import PartitionSpec as P
from jax.experimental import pallas as pl
from jax.experimental.pallas import tpu as pltpu

HEAD_SIZE = 64
E = 40
PAGE_TOKENS = 64
CAP = 48


norm_eps = 1e-06
score_scale = 0.015625
residual_scale = 0.22
rope_base = 10000.0
neg_fill = -1e30


def rms_scale(rows, gain):
    mean_sq = jnp.mean(rows * rows, axis=-1, keepdims=True)
    return rows * lax.rsqrt(mean_sq + norm_eps) * gain


def positions_of(segments):
    tok_index = jnp.arange(segments.shape[0], dtype=jnp.int32)
    previous = jnp.concatenate([jnp.full((1,), -1, jnp.int32), segments[:-1]])
    starts = jnp.where(segments != previous, tok_index, 0)
    return tok_index - lax.cummax(starts, axis=0)


def rotary_apply(heads_in, token_positions):
    half_dim = heads_in.shape[-1] // 2
    inverse_freq = rope_base ** (
        -jnp.arange(half_dim, dtype=jnp.float32) * 2.0 / heads_in.shape[-1]
    )
    angles = token_positions.astype(jnp.float32)[:, None] * inverse_freq[None, :]
    cos_part = jnp.cos(angles)[:, None, :]
    sine_part = jnp.sin(angles)[:, None, :]
    first_half = heads_in[..., :half_dim]
    second_half = heads_in[..., half_dim:]
    return jnp.concatenate(
        [
            first_half * cos_part - second_half * sine_part,
            second_half * cos_part + first_half * sine_part,
        ],
        axis=-1,
    )


def gather_rows(x, axis_name, axis=0):
    count = lax.axis_size(axis_name)
    spread = jnp.broadcast_to(x[None], (count,) + x.shape)
    got = lax.all_to_all(spread, axis_name, 0, 0, tiled=True)
    got = jnp.moveaxis(got, 0, axis)
    shape = list(x.shape)
    shape[axis] = shape[axis] * count
    return got.reshape(shape)


def scatter_sum_rows(x, axis_name):
    count = lax.axis_size(axis_name)
    parts = x.reshape((count, x.shape[0] // count) + x.shape[1:])
    got = lax.all_to_all(parts, axis_name, 0, 0, tiled=True)
    return jnp.sum(got.astype(jnp.float32), axis=0)


def chip_pairs(count, shift):
    chips = count // 2
    return [(d, ((d // 2 + shift) % chips) * 2 + d % 2) for d in range(count)]


def gather_ep(x):
    count = lax.axis_size("ep")
    if count % 2:
        return gather_rows(x, "ep")
    chips = count // 2
    me = lax.axis_index("ep")
    chip = me // 2
    core = me % 2
    side = [x]
    for shift in range(1, chips):
        side.append(lax.ppermute(x, "ep", chip_pairs(count, shift)))
    side = jnp.stack(side)
    other = lax.ppermute(side, "ep", [(d, d ^ 1) for d in range(count)])
    both = jnp.where(core == 0, jnp.stack([side, other], 1), jnp.stack([other, side], 1))
    order = (chip - jnp.arange(chips, dtype=jnp.int32)) % chips
    full = jnp.take(both, order, axis=0, mode="clip")
    return full.reshape((count * x.shape[0],) + x.shape[1:])


def scatter_sum_ep(p):
    count = lax.axis_size("ep")
    if count % 2:
        return scatter_sum_rows(p, "ep")
    chips = count // 2
    me = lax.axis_index("ep")
    chip = me // 2
    core = me % 2
    rows = p.shape[0] // count
    parts = p.reshape((chips, 2, rows) + p.shape[1:])
    mine = jnp.where(core == 0, parts[:, 0], parts[:, 1])
    theirs = jnp.where(core == 0, parts[:, 1], parts[:, 0])
    got = lax.ppermute(theirs, "ep", [(d, d ^ 1) for d in range(count)])
    sums = mine.astype(jnp.float32) + got.astype(jnp.float32)
    total = lax.dynamic_index_in_dim(sums, chip, 0, keepdims=False)
    for shift in range(1, chips):
        piece = lax.dynamic_index_in_dim(sums, (chip + shift) % chips, 0, keepdims=False)
        total = total + lax.ppermute(
            piece.astype(jnp.bfloat16), "ep", chip_pairs(count, shift)
        ).astype(jnp.float32)
    return total


Q_TILE = 128
K_TILE = 256


def flash_body(lo_ref, hi_ref, q_ref, k_ref, v_ref, tok_ref, begin_ref, o_ref):
    qb = pl.program_id(1)
    ratio = q_ref.shape[1]
    q_tile = q_ref.shape[2]
    head_dim = q_ref.shape[3]
    q = q_ref[0].reshape(ratio * q_tile, head_dim)
    tok = tok_ref[...]
    begin = begin_ref[...]

    def step(kb, carry):
        m_old, l_old, acc_old = carry
        k0 = pl.multiple_of(kb * K_TILE, K_TILE)
        k_blk = k_ref[0, pl.ds(k0, K_TILE), :]
        v_blk = v_ref[0, pl.ds(k0, K_TILE), :]
        s = lax.dot_general(
            q, k_blk, (((1,), (1,)), ((), ())), preferred_element_type=jnp.float32
        )
        s = (s * score_scale).reshape(ratio, q_tile, K_TILE)
        key_at = k0 + lax.broadcasted_iota(jnp.int32, (q_tile, K_TILE), 1)
        allowed = (key_at >= begin) & (key_at <= tok)
        s = jnp.where(allowed[None], s, -jnp.inf)
        m_new = jnp.maximum(m_old, jnp.max(s, axis=-1, keepdims=True))
        alpha = jnp.exp(m_old - m_new)
        p = jnp.exp(s - m_new)
        l_new = alpha * l_old + jnp.sum(p, axis=-1, keepdims=True)
        pv = lax.dot_general(
            p.reshape(ratio * q_tile, K_TILE).astype(jnp.bfloat16),
            v_blk,
            (((1,), (0,)), ((), ())),
            preferred_element_type=jnp.float32,
        )
        acc_new = alpha * acc_old + pv.reshape(ratio, q_tile, head_dim)
        return m_new, l_new, acc_new

    init = (
        jnp.full((ratio, q_tile, 1), neg_fill, jnp.float32),
        jnp.zeros((ratio, q_tile, 1), jnp.float32),
        jnp.zeros((ratio, q_tile, head_dim), jnp.float32),
    )
    m_fin, l_fin, acc_fin = lax.fori_loop(lo_ref[qb], hi_ref[qb] + 1, step, init)
    o_ref[0] = (acc_fin / l_fin).astype(o_ref.dtype)


def flash_attention(query_grouped, kv_all, q_index, q_begin):
    kv_heads, ratio, group_len, head_dim = query_grouped.shape
    n_rows = kv_all.shape[1]
    n_q = group_len // Q_TILE
    lo = jnp.min(q_begin.reshape(n_q, Q_TILE), axis=1) // K_TILE
    hi = jnp.max(q_index.reshape(n_q, Q_TILE), axis=1) // K_TILE
    grid_spec = pltpu.PrefetchScalarGridSpec(
        num_scalar_prefetch=2,
        grid=(kv_heads, n_q),
        in_specs=[
            pl.BlockSpec((1, ratio, Q_TILE, head_dim), lambda g, qb, lo, hi: (g, 0, qb, 0)),
            pl.BlockSpec((1, n_rows, head_dim), lambda g, qb, lo, hi: (g, 0, 0)),
            pl.BlockSpec((1, n_rows, head_dim), lambda g, qb, lo, hi: (kv_heads + g, 0, 0)),
            pl.BlockSpec((Q_TILE, 1), lambda g, qb, lo, hi: (qb, 0)),
            pl.BlockSpec((Q_TILE, 1), lambda g, qb, lo, hi: (qb, 0)),
        ],
        out_specs=pl.BlockSpec((1, ratio, Q_TILE, head_dim), lambda g, qb, lo, hi: (g, 0, qb, 0)),
    )
    out = pl.pallas_call(
        flash_body,
        grid_spec=grid_spec,
        out_shape=jax.ShapeDtypeStruct(query_grouped.shape, jnp.bfloat16),
    )(lo, hi, query_grouped, kv_all, kv_all, q_index[:, None], q_begin[:, None])
    return out


def body(
    tokens,
    seg_ids,
    routes,
    route_weights,
    norm1_gain,
    norm2_gain,
    w_query,
    key_weight,
    value_weight,
    w_out_attn,
    w_in,
    w_out,
    paged_key_value_cache,
    page_table,
):
    tok_dev = tokens.shape[0]
    ep_count = lax.axis_size("ep")
    group_len = tok_dev * ep_count
    req_pos = lax.axis_index("req")
    normed = rms_scale(tokens.astype(jnp.float32), norm1_gain).astype(jnp.bfloat16)
    expert_ids = jnp.arange(E, dtype=jnp.int32)
    shares = jnp.sum(
        jnp.where(routes[:, :, None] == expert_ids[None, None, :], route_weights[:, :, None], 0.0),
        axis=1,
    )
    share_cols = -(-E // 128) * 128
    packed = jnp.concatenate(
        [normed, jnp.pad(shares, ((0, 0), (0, share_cols - E))).astype(jnp.bfloat16)], axis=1
    )
    seg_ids, packed = lax.optimization_barrier((seg_ids, packed))
    all_segs = gather_rows(seg_ids, ("req", "ep"))
    all_pos = positions_of(all_segs)
    group_start = req_pos * group_len
    group_pos = lax.dynamic_slice_in_dim(all_pos, group_start, group_len)
    joined = jnp.concatenate([w_query, key_weight, value_weight], axis=1)
    rows_packed = gather_ep(packed)
    shares_all = rows_packed[:, tokens.shape[1] : tokens.shape[1] + E].astype(jnp.float32)
    projected = jnp.dot(
        rows_packed[:, : tokens.shape[1]], joined, preferred_element_type=jnp.float32
    )
    query_width = w_query.shape[1]
    kv_width = key_weight.shape[1]
    q_heads = query_width // HEAD_SIZE
    kv_heads = kv_width // HEAD_SIZE
    heads_ratio = q_heads // kv_heads
    query_rows = rotary_apply(
        projected[:, :query_width].reshape(group_len, q_heads, HEAD_SIZE), group_pos
    ).astype(jnp.bfloat16)
    key_rows = rotary_apply(
        projected[:, query_width : query_width + kv_width].reshape(
            group_len, kv_heads, HEAD_SIZE
        ),
        group_pos,
    ).astype(jnp.bfloat16)
    value_rows = (
        projected[:, query_width + kv_width :]
        .astype(jnp.bfloat16)
        .reshape(group_len, kv_heads, HEAD_SIZE)
    )
    query_grouped = query_rows.reshape(group_len, kv_heads, heads_ratio, HEAD_SIZE).transpose(
        1, 2, 0, 3
    )
    kv_local = jnp.concatenate(
        [key_rows.transpose(1, 0, 2), value_rows.transpose(1, 0, 2)], axis=0
    )
    kv_all = gather_rows(kv_local, "req", axis=1)
    n_rows = kv_all.shape[1]
    q_index = group_start + jnp.arange(group_len, dtype=jnp.int32)
    q_begin = q_index - group_pos
    head_out = flash_attention(query_grouped, kv_all, q_index, q_begin)
    pages_here = paged_key_value_cache.shape[0]
    page_first = req_pos * pages_here
    piece_pages = n_rows // PAGE_TOKENS
    local_pages = page_first + jnp.arange(pages_here, dtype=jnp.int32)
    match = local_pages[:, None] == page_table[None, :]
    hit = jnp.any(match, axis=1)
    block_of = jnp.argmax(match, axis=1).astype(jnp.int32)
    kv_paged = kv_all.reshape(2, kv_heads, piece_pages, PAGE_TOKENS, HEAD_SIZE)
    picked = jnp.take(kv_paged, block_of, axis=2, mode="clip").transpose(2, 1, 0, 3, 4)
    new_cache = jnp.where(hit[:, None, None, None, None], picked, paged_key_value_cache)
    head_out = head_out.transpose(2, 0, 1, 3).reshape(group_len, query_width)
    attention = scatter_sum_ep(
        jnp.dot(head_out, w_out_attn, preferred_element_type=jnp.float32).astype(jnp.bfloat16)
    )
    attn_out = attention.astype(jnp.bfloat16)
    moe_in = rms_scale(tokens.astype(jnp.float32) + residual_scale * attention, norm2_gain).astype(
        jnp.bfloat16
    )
    ffe_width = w_out.shape[1]
    exp_here = w_in.shape[0]
    rows_all = gather_ep(moe_in)
    first_expert = lax.axis_index("ep") * exp_here
    shares_here = lax.dynamic_slice_in_dim(shares_all, first_expert, exp_here, 1)
    total_rows = rows_all.shape[0]
    chosen = (shares_here > 0.0).astype(jnp.int32).reshape(ep_count, tok_dev, exp_here)
    slot_in = jnp.cumsum(chosen, axis=1) - 1
    source_ids = jnp.arange(ep_count, dtype=jnp.int32)[:, None, None]
    local_slot = (source_ids * CAP + slot_in).reshape(total_rows, exp_here)
    live = (chosen > 0).reshape(total_rows, exp_here)
    slot_ids = jnp.arange(ep_count * CAP, dtype=jnp.int32)
    dispatch = (local_slot.T[:, None, :] == slot_ids[None, :, None]) & live.T[:, None, :]
    arrived = jnp.einsum(
        "esr,rd->esd", dispatch.astype(jnp.bfloat16), rows_all, preferred_element_type=jnp.float32
    ).astype(jnp.bfloat16)
    gate_up = jnp.einsum("esd,edf->esf", arrived, w_in, preferred_element_type=jnp.float32)
    activated = (jax.nn.silu(gate_up[..., :ffe_width]) * gate_up[..., ffe_width:]).astype(
        jnp.bfloat16
    )
    result = jnp.einsum(
        "esf,efd->esd", activated, w_out, preferred_element_type=jnp.float32
    ).astype(jnp.bfloat16)
    combine = jnp.where(dispatch, shares_here.T[:, None, :], 0.0)
    partial_rows = jnp.einsum(
        "esr,esd->rd", combine.astype(jnp.bfloat16), result, preferred_element_type=jnp.float32
    )
    moe_out = scatter_sum_ep(partial_rows.astype(jnp.bfloat16)).astype(jnp.bfloat16)
    return (attn_out, moe_out, new_cache)


def solution(mesh):
    in_specs = (
        P(("req", "ep"), None),
        P(("req", "ep")),
        P(("req", "ep"), None),
        P(("req", "ep"), None),
        P(),
        P(),
        P(None, "ep"),
        P(None, "ep"),
        P(None, "ep"),
        P("ep", None),
        P("ep", None, None),
        P("ep", None, None),
        P("req", "ep", None, None, None),
        P(),
    )
    out_specs = (P(("req", "ep"), None), P(("req", "ep"), None), P("req", "ep", None, None, None))
    return jax.shard_map(body, mesh=mesh, in_specs=in_specs, out_specs=out_specs, check_vma=False)
```

```python
import jax
import jax.numpy as jnp
from jax import lax
from jax.sharding import PartitionSpec as P
from jax.experimental import pallas as pl
from jax.experimental.pallas import tpu as pltpu

HEAD_SIZE = 64
E = 40
PAGE_TOKENS = 64
CAP = 48


norm_eps = 1e-06
score_scale = 0.015625
residual_scale = 0.22
rope_base = 10000.0
neg_fill = -1e30


def rms_scale(rows, gain):
    mean_sq = jnp.mean(rows * rows, axis=-1, keepdims=True)
    return rows * lax.rsqrt(mean_sq + norm_eps) * gain


def positions_of(segments):
    tok_index = jnp.arange(segments.shape[0], dtype=jnp.int32)
    previous = jnp.concatenate([jnp.full((1,), -1, jnp.int32), segments[:-1]])
    starts = jnp.where(segments != previous, tok_index, 0)
    return tok_index - lax.cummax(starts, axis=0)


def rotary_apply(heads_in, token_positions):
    half_dim = heads_in.shape[-1] // 2
    inverse_freq = rope_base ** (
        -jnp.arange(half_dim, dtype=jnp.float32) * 2.0 / heads_in.shape[-1]
    )
    angles = token_positions.astype(jnp.float32)[:, None] * inverse_freq[None, :]
    cos_part = jnp.cos(angles)[:, None, :]
    sine_part = jnp.sin(angles)[:, None, :]
    first_half = heads_in[..., :half_dim]
    second_half = heads_in[..., half_dim:]
    return jnp.concatenate(
        [
            first_half * cos_part - second_half * sine_part,
            second_half * cos_part + first_half * sine_part,
        ],
        axis=-1,
    )


def gather_rows(x, axis_name, axis=0):
    count = lax.axis_size(axis_name)
    spread = jnp.broadcast_to(x[None], (count,) + x.shape)
    got = lax.all_to_all(spread, axis_name, 0, 0, tiled=True)
    got = jnp.moveaxis(got, 0, axis)
    shape = list(x.shape)
    shape[axis] = shape[axis] * count
    return got.reshape(shape)


def scatter_sum_rows(x, axis_name):
    count = lax.axis_size(axis_name)
    parts = x.reshape((count, x.shape[0] // count) + x.shape[1:])
    got = lax.all_to_all(parts, axis_name, 0, 0, tiled=True)
    return jnp.sum(got.astype(jnp.float32), axis=0)


def chip_pairs(count, shift):
    chips = count // 2
    return [(d, ((d // 2 + shift) % chips) * 2 + d % 2) for d in range(count)]


def gather_ep(x):
    count = lax.axis_size("ep")
    if count % 2:
        return gather_rows(x, "ep")
    chips = count // 2
    me = lax.axis_index("ep")
    chip = me // 2
    core = me % 2
    side = [x]
    for shift in range(1, chips):
        side.append(lax.ppermute(x, "ep", chip_pairs(count, shift)))
    side = jnp.stack(side)
    other = lax.ppermute(side, "ep", [(d, d ^ 1) for d in range(count)])
    both = jnp.where(core == 0, jnp.stack([side, other], 1), jnp.stack([other, side], 1))
    order = (chip - jnp.arange(chips, dtype=jnp.int32)) % chips
    full = jnp.take(both, order, axis=0, mode="clip")
    return full.reshape((count * x.shape[0],) + x.shape[1:])


def scatter_sum_ep(p):
    count = lax.axis_size("ep")
    if count % 2:
        return scatter_sum_rows(p, "ep")
    chips = count // 2
    me = lax.axis_index("ep")
    chip = me // 2
    core = me % 2
    rows = p.shape[0] // count
    parts = p.reshape((chips, 2, rows) + p.shape[1:])
    mine = jnp.where(core == 0, parts[:, 0], parts[:, 1])
    theirs = jnp.where(core == 0, parts[:, 1], parts[:, 0])
    got = lax.ppermute(theirs, "ep", [(d, d ^ 1) for d in range(count)])
    sums = mine.astype(jnp.float32) + got.astype(jnp.float32)
    total = lax.dynamic_index_in_dim(sums, chip, 0, keepdims=False)
    for shift in range(1, chips):
        piece = lax.dynamic_index_in_dim(sums, (chip + shift) % chips, 0, keepdims=False)
        total = total + lax.ppermute(
            piece.astype(jnp.bfloat16), "ep", chip_pairs(count, shift)
        ).astype(jnp.float32)
    return total


Q_TILE = 128
K_TILE = 256


def flash_body(lo_ref, hi_ref, q_ref, k_ref, v_ref, tok_ref, begin_ref, o_ref):
    qb = pl.program_id(1)
    ratio = q_ref.shape[1]
    q_tile = q_ref.shape[2]
    head_dim = q_ref.shape[3]
    q = q_ref[0].reshape(ratio * q_tile, head_dim)
    per_group = k_ref.shape[2] // K_TILE
    tok = tok_ref[...]
    begin = begin_ref[...]

    def step(kb, carry):
        m_old, l_old, acc_old = carry
        k0 = kb * K_TILE
        grp = kb // per_group
        off = pl.multiple_of((kb % per_group) * K_TILE, K_TILE)
        k_blk = k_ref[grp, 0, pl.ds(off, K_TILE), :]
        v_blk = v_ref[grp, 0, pl.ds(off, K_TILE), :]
        s = lax.dot_general(
            q, k_blk, (((1,), (1,)), ((), ())), preferred_element_type=jnp.float32
        )
        s = (s * score_scale).reshape(ratio, q_tile, K_TILE)
        key_at = k0 + lax.broadcasted_iota(jnp.int32, (q_tile, K_TILE), 1)
        allowed = (key_at >= begin) & (key_at <= tok)
        s = jnp.where(allowed[None], s, -jnp.inf)
        m_new = jnp.maximum(m_old, jnp.max(s, axis=-1, keepdims=True))
        alpha = jnp.exp(m_old - m_new)
        p = jnp.exp(s - m_new)
        l_new = alpha * l_old + jnp.sum(p, axis=-1, keepdims=True)
        pv = lax.dot_general(
            p.reshape(ratio * q_tile, K_TILE).astype(jnp.bfloat16),
            v_blk,
            (((1,), (0,)), ((), ())),
            preferred_element_type=jnp.float32,
        )
        acc_new = alpha * acc_old + pv.reshape(ratio, q_tile, head_dim)
        return m_new, l_new, acc_new

    init = (
        jnp.full((ratio, q_tile, 1), neg_fill, jnp.float32),
        jnp.zeros((ratio, q_tile, 1), jnp.float32),
        jnp.zeros((ratio, q_tile, head_dim), jnp.float32),
    )
    m_fin, l_fin, acc_fin = lax.fori_loop(lo_ref[qb], hi_ref[qb] + 1, step, init)
    o_ref[0] = (acc_fin / l_fin).astype(o_ref.dtype)


def flash_attention(query_grouped, kv_all, q_index, q_begin):
    kv_heads, ratio, group_len, head_dim = query_grouped.shape
    n_grp, _, grp_len, _ = kv_all.shape
    n_q = group_len // Q_TILE
    lo = jnp.min(q_begin.reshape(n_q, Q_TILE), axis=1) // K_TILE
    hi = jnp.max(q_index.reshape(n_q, Q_TILE), axis=1) // K_TILE
    grid_spec = pltpu.PrefetchScalarGridSpec(
        num_scalar_prefetch=2,
        grid=(kv_heads, n_q),
        in_specs=[
            pl.BlockSpec((1, ratio, Q_TILE, head_dim), lambda g, qb, lo, hi: (g, 0, qb, 0)),
            pl.BlockSpec((n_grp, 1, grp_len, head_dim), lambda g, qb, lo, hi: (0, g, 0, 0)),
            pl.BlockSpec(
                (n_grp, 1, grp_len, head_dim), lambda g, qb, lo, hi: (0, kv_heads + g, 0, 0)
            ),
            pl.BlockSpec((Q_TILE, 1), lambda g, qb, lo, hi: (qb, 0)),
            pl.BlockSpec((Q_TILE, 1), lambda g, qb, lo, hi: (qb, 0)),
        ],
        out_specs=pl.BlockSpec((1, ratio, Q_TILE, head_dim), lambda g, qb, lo, hi: (g, 0, qb, 0)),
    )
    out = pl.pallas_call(
        flash_body,
        grid_spec=grid_spec,
        out_shape=jax.ShapeDtypeStruct(query_grouped.shape, jnp.bfloat16),
    )(lo, hi, query_grouped, kv_all, kv_all, q_index[:, None], q_begin[:, None])
    return out


def body(
    tokens,
    seg_ids,
    routes,
    route_weights,
    norm1_gain,
    norm2_gain,
    w_query,
    key_weight,
    value_weight,
    w_out_attn,
    w_in,
    w_out,
    paged_key_value_cache,
    page_table,
):
    tok_dev = tokens.shape[0]
    ep_count = lax.axis_size("ep")
    group_len = tok_dev * ep_count
    req_pos = lax.axis_index("req")
    normed = rms_scale(tokens.astype(jnp.float32), norm1_gain).astype(jnp.bfloat16)
    seg_ids, normed = lax.optimization_barrier((seg_ids, normed))
    all_segs = gather_rows(seg_ids, ("req", "ep"))
    all_pos = positions_of(all_segs)
    group_start = req_pos * group_len
    group_pos = lax.dynamic_slice_in_dim(all_pos, group_start, group_len)
    joined = jnp.concatenate([w_query, key_weight, value_weight], axis=1)
    projected = jnp.dot(
        gather_ep(normed), joined, preferred_element_type=jnp.float32
    )
    query_width = w_query.shape[1]
    kv_width = key_weight.shape[1]
    q_heads = query_width // HEAD_SIZE
    kv_heads = kv_width // HEAD_SIZE
    heads_ratio = q_heads // kv_heads
    query_rows = rotary_apply(
        projected[:, :query_width].reshape(group_len, q_heads, HEAD_SIZE), group_pos
    ).astype(jnp.bfloat16)
    key_rows = rotary_apply(
        projected[:, query_width : query_width + kv_width].reshape(
            group_len, kv_heads, HEAD_SIZE
        ),
        group_pos,
    ).astype(jnp.bfloat16)
    value_rows = (
        projected[:, query_width + kv_width :]
        .astype(jnp.bfloat16)
        .reshape(group_len, kv_heads, HEAD_SIZE)
    )
    query_grouped = query_rows.reshape(group_len, kv_heads, heads_ratio, HEAD_SIZE).transpose(
        1, 2, 0, 3
    )
    kv_local = jnp.concatenate(
        [key_rows.transpose(1, 0, 2), value_rows.transpose(1, 0, 2)], axis=0
    )
    req_count = lax.axis_size("req")
    kv_all = lax.all_to_all(
        jnp.broadcast_to(kv_local[None], (req_count,) + kv_local.shape), "req", 0, 0, tiled=True
    )
    q_index = group_start + jnp.arange(group_len, dtype=jnp.int32)
    q_begin = q_index - group_pos
    head_out = flash_attention(query_grouped, kv_all, q_index, q_begin)
    pages_here = paged_key_value_cache.shape[0]
    page_first = req_pos * pages_here
    group_pages = group_len // PAGE_TOKENS
    local_pages = page_first + jnp.arange(pages_here, dtype=jnp.int32)
    match = local_pages[:, None] == page_table[None, :]
    hit = jnp.any(match, axis=1)
    block_of = jnp.argmax(match, axis=1).astype(jnp.int32)
    kv_paged = kv_all.reshape(req_count, 2, kv_heads, group_pages, PAGE_TOKENS, HEAD_SIZE)
    picked = kv_paged[block_of // group_pages, :, :, block_of % group_pages].transpose(
        0, 2, 1, 3, 4
    )
    new_cache = jnp.where(hit[:, None, None, None, None], picked, paged_key_value_cache)
    head_out = head_out.transpose(2, 0, 1, 3).reshape(group_len, query_width)
    attention = scatter_sum_ep(
        jnp.dot(head_out, w_out_attn, preferred_element_type=jnp.float32).astype(jnp.bfloat16)
    )
    attn_out = attention.astype(jnp.bfloat16)
    moe_in = rms_scale(tokens.astype(jnp.float32) + residual_scale * attention, norm2_gain).astype(
        jnp.bfloat16
    )
    ffe_width = w_out.shape[1]
    exp_here = w_in.shape[0]
    expert_ids = jnp.arange(E, dtype=jnp.int32)
    shares = jnp.sum(
        jnp.where(routes[:, :, None] == expert_ids[None, None, :], route_weights[:, :, None], 0.0),
        axis=1,
    )
    rows_all = gather_ep(moe_in)
    shares_all = gather_rows(shares, "ep")
    first_expert = lax.axis_index("ep") * exp_here
    shares_here = lax.dynamic_slice_in_dim(shares_all, first_expert, exp_here, 1)
    total_rows = rows_all.shape[0]
    chosen = (shares_here > 0.0).astype(jnp.int32).reshape(ep_count, tok_dev, exp_here)
    slot_in = jnp.cumsum(chosen, axis=1) - 1
    source_ids = jnp.arange(ep_count, dtype=jnp.int32)[:, None, None]
    local_slot = (source_ids * CAP + slot_in).reshape(total_rows, exp_here)
    live = (chosen > 0).reshape(total_rows, exp_here)
    slot_ids = jnp.arange(ep_count * CAP, dtype=jnp.int32)
    dispatch = (local_slot.T[:, None, :] == slot_ids[None, :, None]) & live.T[:, None, :]
    arrived = jnp.einsum(
        "esr,rd->esd", dispatch.astype(jnp.bfloat16), rows_all, preferred_element_type=jnp.float32
    ).astype(jnp.bfloat16)
    gate_up = jnp.einsum("esd,edf->esf", arrived, w_in, preferred_element_type=jnp.float32)
    activated = (jax.nn.silu(gate_up[..., :ffe_width]) * gate_up[..., ffe_width:]).astype(
        jnp.bfloat16
    )
    result = jnp.einsum(
        "esf,efd->esd", activated, w_out, preferred_element_type=jnp.float32
    ).astype(jnp.bfloat16)
    combine = jnp.where(dispatch, shares_here.T[:, None, :], 0.0)
    partial_rows = jnp.einsum(
        "esr,esd->rd", combine.astype(jnp.bfloat16), result, preferred_element_type=jnp.float32
    )
    moe_out = scatter_sum_ep(partial_rows.astype(jnp.bfloat16)).astype(jnp.bfloat16)
    return (attn_out, moe_out, new_cache)


def solution(mesh):
    in_specs = (
        P(("req", "ep"), None),
        P(("req", "ep")),
        P(("req", "ep"), None),
        P(("req", "ep"), None),
        P(),
        P(),
        P(None, "ep"),
        P(None, "ep"),
        P(None, "ep"),
        P("ep", None),
        P("ep", None, None),
        P("ep", None, None),
        P("req", "ep", None, None, None),
        P(),
    )
    out_specs = (P(("req", "ep"), None), P(("req", "ep"), None), P("req", "ep", None, None, None))
    return jax.shard_map(body, mesh=mesh, in_specs=in_specs, out_specs=out_specs, check_vma=False)
```

```python
import jax
import jax.numpy as jnp
from jax import lax
from jax.sharding import PartitionSpec as P
from jax.experimental import pallas as pl
from jax.experimental.pallas import tpu as pltpu

HEAD_SIZE = 64
E = 40
PAGE_TOKENS = 64
CAP = 48


norm_eps = 1e-06
score_scale = 0.015625
residual_scale = 0.22
rope_base = 10000.0
neg_fill = -1e30


def rms_scale(rows, gain):
    mean_sq = jnp.mean(rows * rows, axis=-1, keepdims=True)
    return rows * lax.rsqrt(mean_sq + norm_eps) * gain


def positions_of(segments):
    tok_index = jnp.arange(segments.shape[0], dtype=jnp.int32)
    previous = jnp.concatenate([jnp.full((1,), -1, jnp.int32), segments[:-1]])
    starts = jnp.where(segments != previous, tok_index, 0)
    return tok_index - lax.cummax(starts, axis=0)


def rotary_apply(heads_in, token_positions):
    half_dim = heads_in.shape[-1] // 2
    inverse_freq = rope_base ** (
        -jnp.arange(half_dim, dtype=jnp.float32) * 2.0 / heads_in.shape[-1]
    )
    angles = token_positions.astype(jnp.float32)[:, None] * inverse_freq[None, :]
    cos_part = jnp.cos(angles)[:, None, :]
    sine_part = jnp.sin(angles)[:, None, :]
    first_half = heads_in[..., :half_dim]
    second_half = heads_in[..., half_dim:]
    return jnp.concatenate(
        [
            first_half * cos_part - second_half * sine_part,
            second_half * cos_part + first_half * sine_part,
        ],
        axis=-1,
    )


def gather_rows(x, axis_name, axis=0):
    count = lax.axis_size(axis_name)
    spread = jnp.broadcast_to(x[None], (count,) + x.shape)
    got = lax.all_to_all(spread, axis_name, 0, 0, tiled=True)
    got = jnp.moveaxis(got, 0, axis)
    shape = list(x.shape)
    shape[axis] = shape[axis] * count
    return got.reshape(shape)


def scatter_sum_rows(x, axis_name):
    count = lax.axis_size(axis_name)
    parts = x.reshape((count, x.shape[0] // count) + x.shape[1:])
    got = lax.all_to_all(parts, axis_name, 0, 0, tiled=True)
    return jnp.sum(got.astype(jnp.float32), axis=0)


def chip_pairs(count, shift):
    chips = count // 2
    return [(d, ((d // 2 + shift) % chips) * 2 + d % 2) for d in range(count)]


def gather_ep(x):
    count = lax.axis_size("ep")
    if count % 2:
        return gather_rows(x, "ep")
    chips = count // 2
    me = lax.axis_index("ep")
    chip = me // 2
    core = me % 2
    side = [x]
    for shift in range(1, chips):
        side.append(lax.ppermute(x, "ep", chip_pairs(count, shift)))
    side = jnp.stack(side)
    other = lax.ppermute(side, "ep", [(d, d ^ 1) for d in range(count)])
    both = jnp.where(core == 0, jnp.stack([side, other], 1), jnp.stack([other, side], 1))
    order = (chip - jnp.arange(chips, dtype=jnp.int32)) % chips
    full = jnp.take(both, order, axis=0, mode="clip")
    return full.reshape((count * x.shape[0],) + x.shape[1:])


def scatter_sum_ep(p):
    count = lax.axis_size("ep")
    if count % 2:
        return scatter_sum_rows(p, "ep")
    chips = count // 2
    me = lax.axis_index("ep")
    chip = me // 2
    core = me % 2
    rows = p.shape[0] // count
    parts = p.reshape((chips, 2, rows) + p.shape[1:])
    mine = jnp.where(core == 0, parts[:, 0], parts[:, 1])
    theirs = jnp.where(core == 0, parts[:, 1], parts[:, 0])
    got = lax.ppermute(theirs, "ep", [(d, d ^ 1) for d in range(count)])
    sums = mine.astype(jnp.float32) + got.astype(jnp.float32)
    total = lax.dynamic_index_in_dim(sums, chip, 0, keepdims=False)
    for shift in range(1, chips):
        piece = lax.dynamic_index_in_dim(sums, (chip + shift) % chips, 0, keepdims=False)
        total = total + lax.ppermute(
            piece.astype(jnp.bfloat16), "ep", chip_pairs(count, shift)
        ).astype(jnp.float32)
    return total


Q_TILE = 128
K_TILE = 256


def flash_body(lo_ref, hi_ref, q_ref, k_ref, v_ref, tok_ref, begin_ref, o_ref):
    qb = pl.program_id(1)
    ratio = q_ref.shape[1]
    q_tile = q_ref.shape[2]
    head_dim = q_ref.shape[3]
    q = q_ref[0].reshape(ratio * q_tile, head_dim)
    per_group = k_ref.shape[2] // K_TILE
    tok = tok_ref[...]
    begin = begin_ref[...]

    def step(kb, carry):
        m_old, l_old, acc_old = carry
        k0 = kb * K_TILE
        grp = kb // per_group
        off = pl.multiple_of((kb % per_group) * K_TILE, K_TILE)
        k_blk = k_ref[grp, 0, pl.ds(off, K_TILE), :]
        v_blk = v_ref[grp, 0, pl.ds(off, K_TILE), :]
        s = lax.dot_general(
            q, k_blk, (((1,), (1,)), ((), ())), preferred_element_type=jnp.float32
        )
        s = (s * score_scale).reshape(ratio, q_tile, K_TILE)
        key_at = k0 + lax.broadcasted_iota(jnp.int32, (q_tile, K_TILE), 1)
        allowed = (key_at >= begin) & (key_at <= tok)
        s = jnp.where(allowed[None], s, -jnp.inf)
        m_new = jnp.maximum(m_old, jnp.max(s, axis=-1, keepdims=True))
        alpha = jnp.exp(m_old - m_new)
        p = jnp.exp(s - m_new)
        l_new = alpha * l_old + jnp.sum(p, axis=-1, keepdims=True)
        pv = lax.dot_general(
            p.reshape(ratio * q_tile, K_TILE).astype(jnp.bfloat16),
            v_blk,
            (((1,), (0,)), ((), ())),
            preferred_element_type=jnp.float32,
        )
        acc_new = alpha * acc_old + pv.reshape(ratio, q_tile, head_dim)
        return m_new, l_new, acc_new

    init = (
        jnp.full((ratio, q_tile, 1), neg_fill, jnp.float32),
        jnp.zeros((ratio, q_tile, 1), jnp.float32),
        jnp.zeros((ratio, q_tile, head_dim), jnp.float32),
    )
    m_fin, l_fin, acc_fin = lax.fori_loop(lo_ref[qb], hi_ref[qb] + 1, step, init)
    o_ref[0] = (acc_fin / l_fin).astype(o_ref.dtype)


def flash_attention(query_grouped, kv_all, q_index, q_begin):
    kv_heads, ratio, group_len, head_dim = query_grouped.shape
    n_grp, _, grp_len, _ = kv_all.shape
    n_q = group_len // Q_TILE
    lo = jnp.min(q_begin.reshape(n_q, Q_TILE), axis=1) // K_TILE
    hi = jnp.max(q_index.reshape(n_q, Q_TILE), axis=1) // K_TILE
    grid_spec = pltpu.PrefetchScalarGridSpec(
        num_scalar_prefetch=2,
        grid=(kv_heads, n_q),
        in_specs=[
            pl.BlockSpec((1, ratio, Q_TILE, head_dim), lambda g, qb, lo, hi: (g, 0, qb, 0)),
            pl.BlockSpec((n_grp, 1, grp_len, head_dim), lambda g, qb, lo, hi: (0, g, 0, 0)),
            pl.BlockSpec(
                (n_grp, 1, grp_len, head_dim), lambda g, qb, lo, hi: (0, kv_heads + g, 0, 0)
            ),
            pl.BlockSpec((Q_TILE, 1), lambda g, qb, lo, hi: (qb, 0)),
            pl.BlockSpec((Q_TILE, 1), lambda g, qb, lo, hi: (qb, 0)),
        ],
        out_specs=pl.BlockSpec((1, ratio, Q_TILE, head_dim), lambda g, qb, lo, hi: (g, 0, qb, 0)),
    )
    out = pl.pallas_call(
        flash_body,
        grid_spec=grid_spec,
        out_shape=jax.ShapeDtypeStruct(query_grouped.shape, jnp.bfloat16),
    )(lo, hi, query_grouped, kv_all, kv_all, q_index[:, None], q_begin[:, None])
    return out


def body(
    tokens,
    seg_ids,
    routes,
    route_weights,
    norm1_gain,
    norm2_gain,
    w_query,
    key_weight,
    value_weight,
    w_out_attn,
    w_in,
    w_out,
    paged_key_value_cache,
    page_table,
):
    tok_dev = tokens.shape[0]
    ep_count = lax.axis_size("ep")
    group_len = tok_dev * ep_count
    req_pos = lax.axis_index("req")
    normed = rms_scale(tokens.astype(jnp.float32), norm1_gain).astype(jnp.bfloat16)
    seg_ids, normed = lax.optimization_barrier((seg_ids, normed))
    all_segs = gather_rows(seg_ids, ("req", "ep"))
    all_pos = positions_of(all_segs)
    group_start = req_pos * group_len
    group_pos = lax.dynamic_slice_in_dim(all_pos, group_start, group_len)
    joined = jnp.concatenate([w_query, key_weight, value_weight], axis=1)
    projected = jnp.dot(
        gather_ep(normed), joined, preferred_element_type=jnp.float32
    )
    query_width = w_query.shape[1]
    kv_width = key_weight.shape[1]
    q_heads = query_width // HEAD_SIZE
    kv_heads = kv_width // HEAD_SIZE
    heads_ratio = q_heads // kv_heads
    query_rows = rotary_apply(
        projected[:, :query_width].reshape(group_len, q_heads, HEAD_SIZE), group_pos
    ).astype(jnp.bfloat16)
    key_rows = rotary_apply(
        projected[:, query_width : query_width + kv_width].reshape(
            group_len, kv_heads, HEAD_SIZE
        ),
        group_pos,
    ).astype(jnp.bfloat16)
    value_rows = (
        projected[:, query_width + kv_width :]
        .astype(jnp.bfloat16)
        .reshape(group_len, kv_heads, HEAD_SIZE)
    )
    query_grouped = query_rows.reshape(group_len, kv_heads, heads_ratio, HEAD_SIZE).transpose(
        1, 2, 0, 3
    )
    kv_local = jnp.concatenate(
        [key_rows.transpose(1, 0, 2), value_rows.transpose(1, 0, 2)], axis=0
    )
    req_count = lax.axis_size("req")
    kv_all = lax.all_to_all(
        jnp.broadcast_to(kv_local[None], (req_count,) + kv_local.shape), "req", 0, 0, tiled=True
    )
    q_index = group_start + jnp.arange(group_len, dtype=jnp.int32)
    q_begin = q_index - group_pos
    head_out = flash_attention(query_grouped, kv_all, q_index, q_begin)
    pages_here = paged_key_value_cache.shape[0]
    page_first = req_pos * pages_here
    group_pages = group_len // PAGE_TOKENS
    local_pages = page_first + jnp.arange(pages_here, dtype=jnp.int32)
    match = local_pages[:, None] == page_table[None, :]
    hit = jnp.any(match, axis=1)
    block_of = jnp.argmax(match, axis=1).astype(jnp.int32)
    kv_paged = kv_all.reshape(req_count, 2, kv_heads, group_pages, PAGE_TOKENS, HEAD_SIZE)
    picked = kv_paged[block_of // group_pages, :, :, block_of % group_pages].transpose(
        0, 2, 1, 3, 4
    )
    new_cache = jnp.where(hit[:, None, None, None, None], picked, paged_key_value_cache)
    out_weight = w_out_attn.reshape(kv_heads, heads_ratio, HEAD_SIZE, w_out_attn.shape[1])
    attention = scatter_sum_ep(
        jnp.einsum(
            "grtd,grdo->to", head_out, out_weight, preferred_element_type=jnp.float32
        ).astype(jnp.bfloat16)
    )
    attn_out = attention.astype(jnp.bfloat16)
    moe_in = rms_scale(tokens.astype(jnp.float32) + residual_scale * attention, norm2_gain).astype(
        jnp.bfloat16
    )
    ffe_width = w_out.shape[1]
    exp_here = w_in.shape[0]
    expert_ids = jnp.arange(E, dtype=jnp.int32)
    shares = jnp.sum(
        jnp.where(routes[:, :, None] == expert_ids[None, None, :], route_weights[:, :, None], 0.0),
        axis=1,
    )
    rows_all = gather_ep(moe_in)
    shares_all = gather_rows(shares, "ep")
    first_expert = lax.axis_index("ep") * exp_here
    shares_here = lax.dynamic_slice_in_dim(shares_all, first_expert, exp_here, 1)
    total_rows = rows_all.shape[0]
    chosen = (shares_here > 0.0).astype(jnp.int32).reshape(ep_count, tok_dev, exp_here)
    slot_in = jnp.cumsum(chosen, axis=1) - 1
    source_ids = jnp.arange(ep_count, dtype=jnp.int32)[:, None, None]
    local_slot = (source_ids * CAP + slot_in).reshape(total_rows, exp_here)
    live = (chosen > 0).reshape(total_rows, exp_here)
    slot_ids = jnp.arange(ep_count * CAP, dtype=jnp.int32)
    dispatch = (local_slot.T[:, None, :] == slot_ids[None, :, None]) & live.T[:, None, :]
    arrived = jnp.einsum(
        "esr,rd->esd", dispatch.astype(jnp.bfloat16), rows_all, preferred_element_type=jnp.float32
    ).astype(jnp.bfloat16)
    gate_up = jnp.einsum("esd,edf->esf", arrived, w_in, preferred_element_type=jnp.float32)
    activated = (jax.nn.silu(gate_up[..., :ffe_width]) * gate_up[..., ffe_width:]).astype(
        jnp.bfloat16
    )
    result = jnp.einsum(
        "esf,efd->esd", activated, w_out, preferred_element_type=jnp.float32
    ).astype(jnp.bfloat16)
    combine = jnp.where(dispatch, shares_here.T[:, None, :], 0.0)
    partial_rows = jnp.einsum(
        "esr,esd->rd", combine.astype(jnp.bfloat16), result, preferred_element_type=jnp.float32
    )
    moe_out = scatter_sum_ep(partial_rows.astype(jnp.bfloat16)).astype(jnp.bfloat16)
    return (attn_out, moe_out, new_cache)


def solution(mesh):
    in_specs = (
        P(("req", "ep"), None),
        P(("req", "ep")),
        P(("req", "ep"), None),
        P(("req", "ep"), None),
        P(),
        P(),
        P(None, "ep"),
        P(None, "ep"),
        P(None, "ep"),
        P("ep", None),
        P("ep", None, None),
        P("ep", None, None),
        P("req", "ep", None, None, None),
        P(),
    )
    out_specs = (P(("req", "ep"), None), P(("req", "ep"), None), P("req", "ep", None, None, None))
    return jax.shard_map(body, mesh=mesh, in_specs=in_specs, out_specs=out_specs, check_vma=False)
```

```python
import jax
import jax.numpy as jnp
from jax import lax
from jax.sharding import PartitionSpec as P
from jax.experimental import pallas as pl
from jax.experimental.pallas import tpu as pltpu

HEAD_SIZE = 64
E = 40
PAGE_TOKENS = 64
CAP = 48


norm_eps = 1e-06
score_scale = 0.015625
residual_scale = 0.22
rope_base = 10000.0
neg_fill = -1e30


def rms_scale(rows, gain):
    mean_sq = jnp.mean(rows * rows, axis=-1, keepdims=True)
    return rows * lax.rsqrt(mean_sq + norm_eps) * gain


def positions_of(segments):
    tok_index = jnp.arange(segments.shape[0], dtype=jnp.int32)
    previous = jnp.concatenate([jnp.full((1,), -1, jnp.int32), segments[:-1]])
    starts = jnp.where(segments != previous, tok_index, 0)
    return tok_index - lax.cummax(starts, axis=0)


def rotary_apply(heads_in, token_positions):
    half_dim = heads_in.shape[-1] // 2
    inverse_freq = rope_base ** (
        -jnp.arange(half_dim, dtype=jnp.float32) * 2.0 / heads_in.shape[-1]
    )
    angles = token_positions.astype(jnp.float32)[:, None] * inverse_freq[None, :]
    cos_part = jnp.cos(angles)[:, None, :]
    sine_part = jnp.sin(angles)[:, None, :]
    first_half = heads_in[..., :half_dim]
    second_half = heads_in[..., half_dim:]
    return jnp.concatenate(
        [
            first_half * cos_part - second_half * sine_part,
            second_half * cos_part + first_half * sine_part,
        ],
        axis=-1,
    )


def gather_rows(x, axis_name, axis=0):
    count = lax.axis_size(axis_name)
    spread = jnp.broadcast_to(x[None], (count,) + x.shape)
    got = lax.all_to_all(spread, axis_name, 0, 0, tiled=True)
    got = jnp.moveaxis(got, 0, axis)
    shape = list(x.shape)
    shape[axis] = shape[axis] * count
    return got.reshape(shape)


def scatter_sum_rows(x, axis_name):
    count = lax.axis_size(axis_name)
    parts = x.reshape((count, x.shape[0] // count) + x.shape[1:])
    got = lax.all_to_all(parts, axis_name, 0, 0, tiled=True)
    return jnp.sum(got.astype(jnp.float32), axis=0)


def chip_pairs(count, shift):
    chips = count // 2
    return [(d, ((d // 2 + shift) % chips) * 2 + d % 2) for d in range(count)]


def gather_ep(x):
    count = lax.axis_size("ep")
    if count % 2:
        return gather_rows(x, "ep")
    chips = count // 2
    me = lax.axis_index("ep")
    chip = me // 2
    core = me % 2
    side = [x]
    for shift in range(1, chips):
        side.append(lax.ppermute(x, "ep", chip_pairs(count, shift)))
    side = jnp.stack(side)
    other = lax.ppermute(side, "ep", [(d, d ^ 1) for d in range(count)])
    both = jnp.where(core == 0, jnp.stack([side, other], 1), jnp.stack([other, side], 1))
    order = (chip - jnp.arange(chips, dtype=jnp.int32)) % chips
    full = jnp.take(both, order, axis=0, mode="clip")
    return full.reshape((count * x.shape[0],) + x.shape[1:])


def scatter_sum_ep(p):
    count = lax.axis_size("ep")
    if count % 2:
        return scatter_sum_rows(p, "ep")
    chips = count // 2
    me = lax.axis_index("ep")
    chip = me // 2
    core = me % 2
    rows = p.shape[0] // count
    parts = p.reshape((chips, 2, rows) + p.shape[1:])
    mine = jnp.where(core == 0, parts[:, 0], parts[:, 1])
    theirs = jnp.where(core == 0, parts[:, 1], parts[:, 0])
    got = lax.ppermute(theirs, "ep", [(d, d ^ 1) for d in range(count)])
    sums = mine.astype(jnp.float32) + got.astype(jnp.float32)
    total = lax.dynamic_index_in_dim(sums, chip, 0, keepdims=False)
    for shift in range(1, chips):
        piece = lax.dynamic_index_in_dim(sums, (chip + shift) % chips, 0, keepdims=False)
        total = total + lax.ppermute(
            piece.astype(jnp.bfloat16), "ep", chip_pairs(count, shift)
        ).astype(jnp.float32)
    return total


Q_TILE = 128
K_TILE = 256


def flash_body(lo_ref, hi_ref, q_ref, k_ref, v_ref, tok_ref, begin_ref, o_ref):
    qb = pl.program_id(1)
    ratio = q_ref.shape[1]
    q_tile = q_ref.shape[2]
    head_dim = q_ref.shape[3]
    q = q_ref[0].reshape(ratio * q_tile, head_dim)
    per_group = k_ref.shape[3] // K_TILE
    tok = tok_ref[...]
    begin = begin_ref[...]

    def step(kb, carry):
        m_old, l_old, acc_old = carry
        k0 = kb * K_TILE
        grp = kb // per_group
        off = pl.multiple_of((kb % per_group) * K_TILE, K_TILE)
        k_blk = k_ref[grp, 0, :, pl.ds(off, K_TILE)]
        v_blk = v_ref[grp, 0, :, pl.ds(off, K_TILE)]
        s = lax.dot_general(
            q, k_blk, (((1,), (0,)), ((), ())), preferred_element_type=jnp.float32
        )
        s = (s * score_scale).reshape(ratio, q_tile, K_TILE)
        key_at = k0 + lax.broadcasted_iota(jnp.int32, (q_tile, K_TILE), 1)
        allowed = (key_at >= begin) & (key_at <= tok)
        s = jnp.where(allowed[None], s, -jnp.inf)
        m_new = jnp.maximum(m_old, jnp.max(s, axis=-1, keepdims=True))
        alpha = jnp.exp(m_old - m_new)
        p = jnp.exp(s - m_new)
        l_new = alpha * l_old + jnp.sum(p, axis=-1, keepdims=True)
        pv = lax.dot_general(
            p.reshape(ratio * q_tile, K_TILE).astype(jnp.bfloat16),
            v_blk,
            (((1,), (1,)), ((), ())),
            preferred_element_type=jnp.float32,
        )
        acc_new = alpha * acc_old + pv.reshape(ratio, q_tile, head_dim)
        return m_new, l_new, acc_new

    init = (
        jnp.full((ratio, q_tile, 1), neg_fill, jnp.float32),
        jnp.zeros((ratio, q_tile, 1), jnp.float32),
        jnp.zeros((ratio, q_tile, head_dim), jnp.float32),
    )
    m_fin, l_fin, acc_fin = lax.fori_loop(lo_ref[qb], hi_ref[qb] + 1, step, init)
    o_ref[0] = (acc_fin / l_fin).astype(o_ref.dtype)


def flash_attention(query_grouped, kv_all, q_index, q_begin):
    kv_heads, ratio, group_len, head_dim = query_grouped.shape
    n_grp, _, _, grp_len = kv_all.shape
    n_q = group_len // Q_TILE
    lo = jnp.min(q_begin.reshape(n_q, Q_TILE), axis=1) // K_TILE
    hi = jnp.max(q_index.reshape(n_q, Q_TILE), axis=1) // K_TILE
    grid_spec = pltpu.PrefetchScalarGridSpec(
        num_scalar_prefetch=2,
        grid=(kv_heads, n_q),
        in_specs=[
            pl.BlockSpec((1, ratio, Q_TILE, head_dim), lambda g, qb, lo, hi: (g, 0, qb, 0)),
            pl.BlockSpec((n_grp, 1, head_dim, grp_len), lambda g, qb, lo, hi: (0, g, 0, 0)),
            pl.BlockSpec(
                (n_grp, 1, head_dim, grp_len), lambda g, qb, lo, hi: (0, kv_heads + g, 0, 0)
            ),
            pl.BlockSpec((Q_TILE, 1), lambda g, qb, lo, hi: (qb, 0)),
            pl.BlockSpec((Q_TILE, 1), lambda g, qb, lo, hi: (qb, 0)),
        ],
        out_specs=pl.BlockSpec((1, ratio, Q_TILE, head_dim), lambda g, qb, lo, hi: (g, 0, qb, 0)),
    )
    out = pl.pallas_call(
        flash_body,
        grid_spec=grid_spec,
        out_shape=jax.ShapeDtypeStruct(query_grouped.shape, jnp.bfloat16),
    )(lo, hi, query_grouped, kv_all, kv_all, q_index[:, None], q_begin[:, None])
    return out


def body(
    tokens,
    seg_ids,
    routes,
    route_weights,
    norm1_gain,
    norm2_gain,
    w_query,
    key_weight,
    value_weight,
    w_out_attn,
    w_in,
    w_out,
    paged_key_value_cache,
    page_table,
):
    tok_dev = tokens.shape[0]
    ep_count = lax.axis_size("ep")
    group_len = tok_dev * ep_count
    req_pos = lax.axis_index("req")
    normed = rms_scale(tokens.astype(jnp.float32), norm1_gain).astype(jnp.bfloat16)
    seg_ids, normed = lax.optimization_barrier((seg_ids, normed))
    all_segs = gather_rows(seg_ids, ("req", "ep"))
    all_pos = positions_of(all_segs)
    group_start = req_pos * group_len
    group_pos = lax.dynamic_slice_in_dim(all_pos, group_start, group_len)
    joined = jnp.concatenate([w_query, key_weight, value_weight], axis=1)
    projected = jnp.dot(
        gather_ep(normed), joined, preferred_element_type=jnp.float32
    )
    query_width = w_query.shape[1]
    kv_width = key_weight.shape[1]
    q_heads = query_width // HEAD_SIZE
    kv_heads = kv_width // HEAD_SIZE
    heads_ratio = q_heads // kv_heads
    query_rows = rotary_apply(
        projected[:, :query_width].reshape(group_len, q_heads, HEAD_SIZE), group_pos
    ).astype(jnp.bfloat16)
    key_rows = rotary_apply(
        projected[:, query_width : query_width + kv_width].reshape(
            group_len, kv_heads, HEAD_SIZE
        ),
        group_pos,
    ).astype(jnp.bfloat16)
    value_rows = (
        projected[:, query_width + kv_width :]
        .astype(jnp.bfloat16)
        .reshape(group_len, kv_heads, HEAD_SIZE)
    )
    query_grouped = query_rows.reshape(group_len, kv_heads, heads_ratio, HEAD_SIZE).transpose(
        1, 2, 0, 3
    )
    kv_local = jnp.concatenate(
        [key_rows.transpose(1, 0, 2), value_rows.transpose(1, 0, 2)], axis=0
    )
    req_count = lax.axis_size("req")
    kv_local = kv_local.swapaxes(1, 2)
    kv_all = lax.all_to_all(
        jnp.broadcast_to(kv_local[None], (req_count,) + kv_local.shape), "req", 0, 0, tiled=True
    )
    q_index = group_start + jnp.arange(group_len, dtype=jnp.int32)
    q_begin = q_index - group_pos
    head_out = flash_attention(query_grouped, kv_all, q_index, q_begin)
    pages_here = paged_key_value_cache.shape[0]
    page_first = req_pos * pages_here
    group_pages = group_len // PAGE_TOKENS
    local_pages = page_first + jnp.arange(pages_here, dtype=jnp.int32)
    match = local_pages[:, None] == page_table[None, :]
    hit = jnp.any(match, axis=1)
    block_of = jnp.argmax(match, axis=1).astype(jnp.int32)
    kv_paged = kv_all.reshape(req_count, 2, kv_heads, HEAD_SIZE, group_pages, PAGE_TOKENS)
    picked = kv_paged[block_of // group_pages, :, :, :, block_of % group_pages].transpose(
        0, 2, 1, 4, 3
    )
    new_cache = jnp.where(hit[:, None, None, None, None], picked, paged_key_value_cache)
    out_weight = w_out_attn.reshape(kv_heads, heads_ratio, HEAD_SIZE, w_out_attn.shape[1])
    attention = scatter_sum_ep(
        jnp.einsum(
            "grtd,grdo->to", head_out, out_weight, preferred_element_type=jnp.float32
        ).astype(jnp.bfloat16)
    )
    attn_out = attention.astype(jnp.bfloat16)
    moe_in = rms_scale(tokens.astype(jnp.float32) + residual_scale * attention, norm2_gain).astype(
        jnp.bfloat16
    )
    ffe_width = w_out.shape[1]
    exp_here = w_in.shape[0]
    expert_ids = jnp.arange(E, dtype=jnp.int32)
    shares = jnp.sum(
        jnp.where(routes[:, :, None] == expert_ids[None, None, :], route_weights[:, :, None], 0.0),
        axis=1,
    )
    rows_all = gather_ep(moe_in)
    shares_all = gather_rows(shares, "ep")
    first_expert = lax.axis_index("ep") * exp_here
    shares_here = lax.dynamic_slice_in_dim(shares_all, first_expert, exp_here, 1)
    total_rows = rows_all.shape[0]
    chosen = (shares_here > 0.0).astype(jnp.int32).reshape(ep_count, tok_dev, exp_here)
    slot_in = jnp.cumsum(chosen, axis=1) - 1
    source_ids = jnp.arange(ep_count, dtype=jnp.int32)[:, None, None]
    local_slot = (source_ids * CAP + slot_in).reshape(total_rows, exp_here)
    live = (chosen > 0).reshape(total_rows, exp_here)
    slot_ids = jnp.arange(ep_count * CAP, dtype=jnp.int32)
    dispatch = (local_slot.T[:, None, :] == slot_ids[None, :, None]) & live.T[:, None, :]
    arrived = jnp.einsum(
        "esr,rd->esd", dispatch.astype(jnp.bfloat16), rows_all, preferred_element_type=jnp.float32
    ).astype(jnp.bfloat16)
    gate_up = jnp.einsum("esd,edf->esf", arrived, w_in, preferred_element_type=jnp.float32)
    activated = (jax.nn.silu(gate_up[..., :ffe_width]) * gate_up[..., ffe_width:]).astype(
        jnp.bfloat16
    )
    result = jnp.einsum(
        "esf,efd->esd", activated, w_out, preferred_element_type=jnp.float32
    ).astype(jnp.bfloat16)
    combine = jnp.where(dispatch, shares_here.T[:, None, :], 0.0)
    partial_rows = jnp.einsum(
        "esr,esd->rd", combine.astype(jnp.bfloat16), result, preferred_element_type=jnp.float32
    )
    moe_out = scatter_sum_ep(partial_rows.astype(jnp.bfloat16)).astype(jnp.bfloat16)
    return (attn_out, moe_out, new_cache)


def solution(mesh):
    in_specs = (
        P(("req", "ep"), None),
        P(("req", "ep")),
        P(("req", "ep"), None),
        P(("req", "ep"), None),
        P(),
        P(),
        P(None, "ep"),
        P(None, "ep"),
        P(None, "ep"),
        P("ep", None),
        P("ep", None, None),
        P("ep", None, None),
        P("req", "ep", None, None, None),
        P(),
    )
    out_specs = (P(("req", "ep"), None), P(("req", "ep"), None), P("req", "ep", None, None, None))
    return jax.shard_map(body, mesh=mesh, in_specs=in_specs, out_specs=out_specs, check_vma=False)
```

```python
import jax
import jax.numpy as jnp
from jax import lax
from jax.sharding import PartitionSpec as P
from jax.experimental import pallas as pl
from jax.experimental.pallas import tpu as pltpu

HEAD_SIZE = 64
E = 40
PAGE_TOKENS = 64
CAP = 48


norm_eps = 1e-06
score_scale = 0.015625
residual_scale = 0.22
rope_base = 10000.0
neg_fill = -1e30


def rms_scale(rows, gain):
    mean_sq = jnp.mean(rows * rows, axis=-1, keepdims=True)
    return rows * lax.rsqrt(mean_sq + norm_eps) * gain


def positions_of(segments):
    tok_index = jnp.arange(segments.shape[0], dtype=jnp.int32)
    previous = jnp.concatenate([jnp.full((1,), -1, jnp.int32), segments[:-1]])
    starts = jnp.where(segments != previous, tok_index, 0)
    return tok_index - lax.cummax(starts, axis=0)


def rotary_apply(heads_in, token_positions):
    half_dim = heads_in.shape[-1] // 2
    inverse_freq = rope_base ** (
        -jnp.arange(half_dim, dtype=jnp.float32) * 2.0 / heads_in.shape[-1]
    )
    angles = token_positions.astype(jnp.float32)[:, None] * inverse_freq[None, :]
    cos_part = jnp.cos(angles)[:, None, :]
    sine_part = jnp.sin(angles)[:, None, :]
    first_half = heads_in[..., :half_dim]
    second_half = heads_in[..., half_dim:]
    return jnp.concatenate(
        [
            first_half * cos_part - second_half * sine_part,
            second_half * cos_part + first_half * sine_part,
        ],
        axis=-1,
    )


def gather_rows(x, axis_name, axis=0):
    count = lax.axis_size(axis_name)
    spread = jnp.broadcast_to(x[None], (count,) + x.shape)
    got = lax.all_to_all(spread, axis_name, 0, 0, tiled=True)
    got = jnp.moveaxis(got, 0, axis)
    shape = list(x.shape)
    shape[axis] = shape[axis] * count
    return got.reshape(shape)


def scatter_sum_rows(x, axis_name):
    count = lax.axis_size(axis_name)
    parts = x.reshape((count, x.shape[0] // count) + x.shape[1:])
    got = lax.all_to_all(parts, axis_name, 0, 0, tiled=True)
    return jnp.sum(got.astype(jnp.float32), axis=0)


def chip_pairs(count, shift):
    chips = count // 2
    return [(d, ((d // 2 + shift) % chips) * 2 + d % 2) for d in range(count)]


def gather_ep(x):
    count = lax.axis_size("ep")
    if count % 2:
        return gather_rows(x, "ep")
    chips = count // 2
    me = lax.axis_index("ep")
    chip = me // 2
    core = me % 2
    side = [x]
    for shift in range(1, chips):
        side.append(lax.ppermute(x, "ep", chip_pairs(count, shift)))
    side = jnp.stack(side)
    other = lax.ppermute(side, "ep", [(d, d ^ 1) for d in range(count)])
    both = jnp.where(core == 0, jnp.stack([side, other], 1), jnp.stack([other, side], 1))
    order = (chip - jnp.arange(chips, dtype=jnp.int32)) % chips
    full = jnp.take(both, order, axis=0, mode="clip")
    return full.reshape((count * x.shape[0],) + x.shape[1:])


def scatter_sum_ep(p):
    count = lax.axis_size("ep")
    if count % 2:
        return scatter_sum_rows(p, "ep")
    chips = count // 2
    me = lax.axis_index("ep")
    chip = me // 2
    core = me % 2
    rows = p.shape[0] // count
    parts = p.reshape((chips, 2, rows) + p.shape[1:])
    mine = jnp.where(core == 0, parts[:, 0], parts[:, 1])
    theirs = jnp.where(core == 0, parts[:, 1], parts[:, 0])
    got = lax.ppermute(theirs, "ep", [(d, d ^ 1) for d in range(count)])
    sums = mine.astype(jnp.float32) + got.astype(jnp.float32)
    total = lax.dynamic_index_in_dim(sums, chip, 0, keepdims=False)
    for shift in range(1, chips):
        piece = lax.dynamic_index_in_dim(sums, (chip + shift) % chips, 0, keepdims=False)
        total = total + lax.ppermute(
            piece.astype(jnp.bfloat16), "ep", chip_pairs(count, shift)
        ).astype(jnp.float32)
    return total


Q_TILE = 128
K_TILE = 512


def flash_body(lo_ref, hi_ref, q_ref, k_ref, v_ref, tok_ref, begin_ref, o_ref):
    qb = pl.program_id(1)
    ratio = q_ref.shape[1]
    q_tile = q_ref.shape[2]
    head_dim = q_ref.shape[3]
    q = q_ref[0].reshape(ratio * q_tile, head_dim)
    per_group = k_ref.shape[2] // K_TILE
    tok = tok_ref[...]
    begin = begin_ref[...]

    def step(kb, carry):
        m_old, l_old, acc_old = carry
        k0 = kb * K_TILE
        grp = kb // per_group
        off = pl.multiple_of((kb % per_group) * K_TILE, K_TILE)
        k_blk = k_ref[grp, 0, pl.ds(off, K_TILE), :]
        v_blk = v_ref[grp, 0, pl.ds(off, K_TILE), :]
        s = lax.dot_general(
            q, k_blk, (((1,), (1,)), ((), ())), preferred_element_type=jnp.float32
        )
        s = (s * score_scale).reshape(ratio, q_tile, K_TILE)
        key_at = k0 + lax.broadcasted_iota(jnp.int32, (q_tile, K_TILE), 1)
        allowed = (key_at >= begin) & (key_at <= tok)
        s = jnp.where(allowed[None], s, -jnp.inf)
        m_new = jnp.maximum(m_old, jnp.max(s, axis=-1, keepdims=True))
        alpha = jnp.exp(m_old - m_new)
        p = jnp.exp(s - m_new)
        l_new = alpha * l_old + jnp.sum(p, axis=-1, keepdims=True)
        pv = lax.dot_general(
            p.reshape(ratio * q_tile, K_TILE).astype(jnp.bfloat16),
            v_blk,
            (((1,), (0,)), ((), ())),
            preferred_element_type=jnp.float32,
        )
        acc_new = alpha * acc_old + pv.reshape(ratio, q_tile, head_dim)
        return m_new, l_new, acc_new

    init = (
        jnp.full((ratio, q_tile, 1), neg_fill, jnp.float32),
        jnp.zeros((ratio, q_tile, 1), jnp.float32),
        jnp.zeros((ratio, q_tile, head_dim), jnp.float32),
    )
    m_fin, l_fin, acc_fin = lax.fori_loop(lo_ref[qb], hi_ref[qb] + 1, step, init)
    o_ref[0] = (acc_fin / l_fin).astype(o_ref.dtype)


def flash_attention(query_grouped, kv_all, q_index, q_begin):
    kv_heads, ratio, group_len, head_dim = query_grouped.shape
    n_grp, _, grp_len, _ = kv_all.shape
    n_q = group_len // Q_TILE
    lo = jnp.min(q_begin.reshape(n_q, Q_TILE), axis=1) // K_TILE
    hi = jnp.max(q_index.reshape(n_q, Q_TILE), axis=1) // K_TILE
    grid_spec = pltpu.PrefetchScalarGridSpec(
        num_scalar_prefetch=2,
        grid=(kv_heads, n_q),
        in_specs=[
            pl.BlockSpec((1, ratio, Q_TILE, head_dim), lambda g, qb, lo, hi: (g, 0, qb, 0)),
            pl.BlockSpec((n_grp, 1, grp_len, head_dim), lambda g, qb, lo, hi: (0, g, 0, 0)),
            pl.BlockSpec(
                (n_grp, 1, grp_len, head_dim), lambda g, qb, lo, hi: (0, kv_heads + g, 0, 0)
            ),
            pl.BlockSpec((Q_TILE, 1), lambda g, qb, lo, hi: (qb, 0)),
            pl.BlockSpec((Q_TILE, 1), lambda g, qb, lo, hi: (qb, 0)),
        ],
        out_specs=pl.BlockSpec((1, ratio, Q_TILE, head_dim), lambda g, qb, lo, hi: (g, 0, qb, 0)),
    )
    out = pl.pallas_call(
        flash_body,
        grid_spec=grid_spec,
        out_shape=jax.ShapeDtypeStruct(query_grouped.shape, jnp.bfloat16),
    )(lo, hi, query_grouped, kv_all, kv_all, q_index[:, None], q_begin[:, None])
    return out


def body(
    tokens,
    seg_ids,
    routes,
    route_weights,
    norm1_gain,
    norm2_gain,
    w_query,
    key_weight,
    value_weight,
    w_out_attn,
    w_in,
    w_out,
    paged_key_value_cache,
    page_table,
):
    tok_dev = tokens.shape[0]
    ep_count = lax.axis_size("ep")
    group_len = tok_dev * ep_count
    req_pos = lax.axis_index("req")
    normed = rms_scale(tokens.astype(jnp.float32), norm1_gain).astype(jnp.bfloat16)
    seg_ids, normed = lax.optimization_barrier((seg_ids, normed))
    all_segs = gather_rows(seg_ids, ("req", "ep"))
    all_pos = positions_of(all_segs)
    group_start = req_pos * group_len
    group_pos = lax.dynamic_slice_in_dim(all_pos, group_start, group_len)
    joined = jnp.concatenate([w_query, key_weight, value_weight], axis=1)
    projected = jnp.dot(
        gather_ep(normed), joined, preferred_element_type=jnp.float32
    )
    query_width = w_query.shape[1]
    kv_width = key_weight.shape[1]
    q_heads = query_width // HEAD_SIZE
    kv_heads = kv_width // HEAD_SIZE
    heads_ratio = q_heads // kv_heads
    query_rows = rotary_apply(
        projected[:, :query_width].reshape(group_len, q_heads, HEAD_SIZE), group_pos
    ).astype(jnp.bfloat16)
    key_rows = rotary_apply(
        projected[:, query_width : query_width + kv_width].reshape(
            group_len, kv_heads, HEAD_SIZE
        ),
        group_pos,
    ).astype(jnp.bfloat16)
    value_rows = (
        projected[:, query_width + kv_width :]
        .astype(jnp.bfloat16)
        .reshape(group_len, kv_heads, HEAD_SIZE)
    )
    query_grouped = query_rows.reshape(group_len, kv_heads, heads_ratio, HEAD_SIZE).transpose(
        1, 2, 0, 3
    )
    kv_local = jnp.concatenate(
        [key_rows.transpose(1, 0, 2), value_rows.transpose(1, 0, 2)], axis=0
    )
    req_count = lax.axis_size("req")
    kv_all = lax.all_to_all(
        jnp.broadcast_to(kv_local[None], (req_count,) + kv_local.shape), "req", 0, 0, tiled=True
    )
    q_index = group_start + jnp.arange(group_len, dtype=jnp.int32)
    q_begin = q_index - group_pos
    head_out = flash_attention(query_grouped, kv_all, q_index, q_begin)
    pages_here = paged_key_value_cache.shape[0]
    page_first = req_pos * pages_here
    group_pages = group_len // PAGE_TOKENS
    local_pages = page_first + jnp.arange(pages_here, dtype=jnp.int32)
    match = local_pages[:, None] == page_table[None, :]
    hit = jnp.any(match, axis=1)
    block_of = jnp.argmax(match, axis=1).astype(jnp.int32)
    kv_paged = kv_all.reshape(req_count, 2, kv_heads, group_pages, PAGE_TOKENS, HEAD_SIZE)
    picked = kv_paged[block_of // group_pages, :, :, block_of % group_pages].transpose(
        0, 2, 1, 3, 4
    )
    new_cache = jnp.where(hit[:, None, None, None, None], picked, paged_key_value_cache)
    out_weight = w_out_attn.reshape(kv_heads, heads_ratio, HEAD_SIZE, w_out_attn.shape[1])
    attention = scatter_sum_ep(
        jnp.einsum(
            "grtd,grdo->to", head_out, out_weight, preferred_element_type=jnp.float32
        ).astype(jnp.bfloat16)
    )
    attn_out = attention.astype(jnp.bfloat16)
    moe_in = rms_scale(tokens.astype(jnp.float32) + residual_scale * attention, norm2_gain).astype(
        jnp.bfloat16
    )
    ffe_width = w_out.shape[1]
    exp_here = w_in.shape[0]
    expert_ids = jnp.arange(E, dtype=jnp.int32)
    shares = jnp.sum(
        jnp.where(routes[:, :, None] == expert_ids[None, None, :], route_weights[:, :, None], 0.0),
        axis=1,
    )
    rows_all = gather_ep(moe_in)
    shares_all = gather_rows(shares, "ep")
    first_expert = lax.axis_index("ep") * exp_here
    shares_here = lax.dynamic_slice_in_dim(shares_all, first_expert, exp_here, 1)
    total_rows = rows_all.shape[0]
    chosen = (shares_here > 0.0).astype(jnp.int32).reshape(ep_count, tok_dev, exp_here)
    slot_in = jnp.cumsum(chosen, axis=1) - 1
    source_ids = jnp.arange(ep_count, dtype=jnp.int32)[:, None, None]
    local_slot = (source_ids * CAP + slot_in).reshape(total_rows, exp_here)
    live = (chosen > 0).reshape(total_rows, exp_here)
    slot_ids = jnp.arange(ep_count * CAP, dtype=jnp.int32)
    dispatch = (local_slot.T[:, None, :] == slot_ids[None, :, None]) & live.T[:, None, :]
    arrived = jnp.einsum(
        "esr,rd->esd", dispatch.astype(jnp.bfloat16), rows_all, preferred_element_type=jnp.float32
    ).astype(jnp.bfloat16)
    gate_up = jnp.einsum("esd,edf->esf", arrived, w_in, preferred_element_type=jnp.float32)
    activated = (jax.nn.silu(gate_up[..., :ffe_width]) * gate_up[..., ffe_width:]).astype(
        jnp.bfloat16
    )
    result = jnp.einsum(
        "esf,efd->esd", activated, w_out, preferred_element_type=jnp.float32
    ).astype(jnp.bfloat16)
    combine = jnp.where(dispatch, shares_here.T[:, None, :], 0.0)
    partial_rows = jnp.einsum(
        "esr,esd->rd", combine.astype(jnp.bfloat16), result, preferred_element_type=jnp.float32
    )
    moe_out = scatter_sum_ep(partial_rows.astype(jnp.bfloat16)).astype(jnp.bfloat16)
    return (attn_out, moe_out, new_cache)


def solution(mesh):
    in_specs = (
        P(("req", "ep"), None),
        P(("req", "ep")),
        P(("req", "ep"), None),
        P(("req", "ep"), None),
        P(),
        P(),
        P(None, "ep"),
        P(None, "ep"),
        P(None, "ep"),
        P("ep", None),
        P("ep", None, None),
        P("ep", None, None),
        P("req", "ep", None, None, None),
        P(),
    )
    out_specs = (P(("req", "ep"), None), P(("req", "ep"), None), P("req", "ep", None, None, None))
    return jax.shard_map(body, mesh=mesh, in_specs=in_specs, out_specs=out_specs, check_vma=False)
```

```python
import jax
import jax.numpy as jnp
from jax import lax
from jax.sharding import PartitionSpec as P
from jax.experimental import pallas as pl
from jax.experimental.pallas import tpu as pltpu

HEAD_SIZE = 64
E = 40
PAGE_TOKENS = 64
CAP = 48


norm_eps = 1e-06
score_scale = 0.015625
residual_scale = 0.22
rope_base = 10000.0
neg_fill = -1e30


def rms_scale(rows, gain):
    mean_sq = jnp.mean(rows * rows, axis=-1, keepdims=True)
    return rows * lax.rsqrt(mean_sq + norm_eps) * gain


def positions_of(segments):
    tok_index = jnp.arange(segments.shape[0], dtype=jnp.int32)
    previous = jnp.concatenate([jnp.full((1,), -1, jnp.int32), segments[:-1]])
    starts = jnp.where(segments != previous, tok_index, 0)
    return tok_index - lax.cummax(starts, axis=0)


def rotary_apply(heads_in, token_positions):
    half_dim = heads_in.shape[-1] // 2
    inverse_freq = rope_base ** (
        -jnp.arange(half_dim, dtype=jnp.float32) * 2.0 / heads_in.shape[-1]
    )
    angles = token_positions.astype(jnp.float32)[:, None] * inverse_freq[None, :]
    cos_part = jnp.cos(angles)[:, None, :]
    sine_part = jnp.sin(angles)[:, None, :]
    first_half = heads_in[..., :half_dim]
    second_half = heads_in[..., half_dim:]
    return jnp.concatenate(
        [
            first_half * cos_part - second_half * sine_part,
            second_half * cos_part + first_half * sine_part,
        ],
        axis=-1,
    )


def gather_rows(x, axis_name, axis=0):
    count = lax.axis_size(axis_name)
    spread = jnp.broadcast_to(x[None], (count,) + x.shape)
    got = lax.all_to_all(spread, axis_name, 0, 0, tiled=True)
    got = jnp.moveaxis(got, 0, axis)
    shape = list(x.shape)
    shape[axis] = shape[axis] * count
    return got.reshape(shape)


def scatter_sum_rows(x, axis_name):
    count = lax.axis_size(axis_name)
    parts = x.reshape((count, x.shape[0] // count) + x.shape[1:])
    got = lax.all_to_all(parts, axis_name, 0, 0, tiled=True)
    return jnp.sum(got.astype(jnp.float32), axis=0)


def chip_pairs(count, shift):
    chips = count // 2
    return [(d, ((d // 2 + shift) % chips) * 2 + d % 2) for d in range(count)]


def gather_ep(x):
    count = lax.axis_size("ep")
    if count % 2:
        return gather_rows(x, "ep")
    chips = count // 2
    me = lax.axis_index("ep")
    chip = me // 2
    core = me % 2
    side = [x]
    for shift in range(1, chips):
        side.append(lax.ppermute(x, "ep", chip_pairs(count, shift)))
    side = jnp.stack(side)
    other = lax.ppermute(side, "ep", [(d, d ^ 1) for d in range(count)])
    both = jnp.where(core == 0, jnp.stack([side, other], 1), jnp.stack([other, side], 1))
    order = (chip - jnp.arange(chips, dtype=jnp.int32)) % chips
    full = jnp.take(both, order, axis=0, mode="clip")
    return full.reshape((count * x.shape[0],) + x.shape[1:])


def scatter_sum_ep(p):
    count = lax.axis_size("ep")
    if count % 2:
        return scatter_sum_rows(p, "ep")
    chips = count // 2
    me = lax.axis_index("ep")
    chip = me // 2
    core = me % 2
    rows = p.shape[0] // count
    parts = p.reshape((chips, 2, rows) + p.shape[1:])
    mine = jnp.where(core == 0, parts[:, 0], parts[:, 1])
    theirs = jnp.where(core == 0, parts[:, 1], parts[:, 0])
    got = lax.ppermute(theirs, "ep", [(d, d ^ 1) for d in range(count)])
    sums = mine.astype(jnp.float32) + got.astype(jnp.float32)
    total = lax.dynamic_index_in_dim(sums, chip, 0, keepdims=False)
    for shift in range(1, chips):
        piece = lax.dynamic_index_in_dim(sums, (chip + shift) % chips, 0, keepdims=False)
        total = total + lax.ppermute(
            piece.astype(jnp.bfloat16), "ep", chip_pairs(count, shift)
        ).astype(jnp.float32)
    return total


Q_TILE = 256
K_TILE = 512


def flash_body(lo_ref, hi_ref, q_ref, k_ref, v_ref, tok_ref, begin_ref, o_ref):
    qb = pl.program_id(1)
    ratio = q_ref.shape[1]
    q_tile = q_ref.shape[2]
    head_dim = q_ref.shape[3]
    q = q_ref[0].reshape(ratio * q_tile, head_dim)
    per_group = k_ref.shape[2] // K_TILE
    tok = tok_ref[...]
    begin = begin_ref[...]

    def step(kb, carry):
        m_old, l_old, acc_old = carry
        k0 = kb * K_TILE
        grp = kb // per_group
        off = pl.multiple_of((kb % per_group) * K_TILE, K_TILE)
        k_blk = k_ref[grp, 0, pl.ds(off, K_TILE), :]
        v_blk = v_ref[grp, 0, pl.ds(off, K_TILE), :]
        s = lax.dot_general(
            q, k_blk, (((1,), (1,)), ((), ())), preferred_element_type=jnp.float32
        )
        s = (s * score_scale).reshape(ratio, q_tile, K_TILE)
        key_at = k0 + lax.broadcasted_iota(jnp.int32, (q_tile, K_TILE), 1)
        allowed = (key_at >= begin) & (key_at <= tok)
        s = jnp.where(allowed[None], s, -jnp.inf)
        m_new = jnp.maximum(m_old, jnp.max(s, axis=-1, keepdims=True))
        alpha = jnp.exp(m_old - m_new)
        p = jnp.exp(s - m_new)
        l_new = alpha * l_old + jnp.sum(p, axis=-1, keepdims=True)
        pv = lax.dot_general(
            p.reshape(ratio * q_tile, K_TILE).astype(jnp.bfloat16),
            v_blk,
            (((1,), (0,)), ((), ())),
            preferred_element_type=jnp.float32,
        )
        acc_new = alpha * acc_old + pv.reshape(ratio, q_tile, head_dim)
        return m_new, l_new, acc_new

    init = (
        jnp.full((ratio, q_tile, 1), neg_fill, jnp.float32),
        jnp.zeros((ratio, q_tile, 1), jnp.float32),
        jnp.zeros((ratio, q_tile, head_dim), jnp.float32),
    )
    m_fin, l_fin, acc_fin = lax.fori_loop(lo_ref[qb], hi_ref[qb] + 1, step, init)
    o_ref[0] = (acc_fin / l_fin).astype(o_ref.dtype)


def flash_attention(query_grouped, kv_all, q_index, q_begin):
    kv_heads, ratio, group_len, head_dim = query_grouped.shape
    n_grp, _, grp_len, _ = kv_all.shape
    n_q = group_len // Q_TILE
    lo = jnp.min(q_begin.reshape(n_q, Q_TILE), axis=1) // K_TILE
    hi = jnp.max(q_index.reshape(n_q, Q_TILE), axis=1) // K_TILE
    grid_spec = pltpu.PrefetchScalarGridSpec(
        num_scalar_prefetch=2,
        grid=(kv_heads, n_q),
        in_specs=[
            pl.BlockSpec((1, ratio, Q_TILE, head_dim), lambda g, qb, lo, hi: (g, 0, qb, 0)),
            pl.BlockSpec((n_grp, 1, grp_len, head_dim), lambda g, qb, lo, hi: (0, g, 0, 0)),
            pl.BlockSpec(
                (n_grp, 1, grp_len, head_dim), lambda g, qb, lo, hi: (0, kv_heads + g, 0, 0)
            ),
            pl.BlockSpec((Q_TILE, 1), lambda g, qb, lo, hi: (qb, 0)),
            pl.BlockSpec((Q_TILE, 1), lambda g, qb, lo, hi: (qb, 0)),
        ],
        out_specs=pl.BlockSpec((1, ratio, Q_TILE, head_dim), lambda g, qb, lo, hi: (g, 0, qb, 0)),
    )
    out = pl.pallas_call(
        flash_body,
        grid_spec=grid_spec,
        out_shape=jax.ShapeDtypeStruct(query_grouped.shape, jnp.bfloat16),
    )(lo, hi, query_grouped, kv_all, kv_all, q_index[:, None], q_begin[:, None])
    return out


def body(
    tokens,
    seg_ids,
    routes,
    route_weights,
    norm1_gain,
    norm2_gain,
    w_query,
    key_weight,
    value_weight,
    w_out_attn,
    w_in,
    w_out,
    paged_key_value_cache,
    page_table,
):
    tok_dev = tokens.shape[0]
    ep_count = lax.axis_size("ep")
    group_len = tok_dev * ep_count
    req_pos = lax.axis_index("req")
    normed = rms_scale(tokens.astype(jnp.float32), norm1_gain).astype(jnp.bfloat16)
    seg_ids, normed = lax.optimization_barrier((seg_ids, normed))
    all_segs = gather_rows(seg_ids, ("req", "ep"))
    all_pos = positions_of(all_segs)
    group_start = req_pos * group_len
    group_pos = lax.dynamic_slice_in_dim(all_pos, group_start, group_len)
    joined = jnp.concatenate([w_query, key_weight, value_weight], axis=1)
    projected = jnp.dot(
        gather_ep(normed), joined, preferred_element_type=jnp.float32
    )
    query_width = w_query.shape[1]
    kv_width = key_weight.shape[1]
    q_heads = query_width // HEAD_SIZE
    kv_heads = kv_width // HEAD_SIZE
    heads_ratio = q_heads // kv_heads
    query_rows = rotary_apply(
        projected[:, :query_width].reshape(group_len, q_heads, HEAD_SIZE), group_pos
    ).astype(jnp.bfloat16)
    key_rows = rotary_apply(
        projected[:, query_width : query_width + kv_width].reshape(
            group_len, kv_heads, HEAD_SIZE
        ),
        group_pos,
    ).astype(jnp.bfloat16)
    value_rows = (
        projected[:, query_width + kv_width :]
        .astype(jnp.bfloat16)
        .reshape(group_len, kv_heads, HEAD_SIZE)
    )
    query_grouped = query_rows.reshape(group_len, kv_heads, heads_ratio, HEAD_SIZE).transpose(
        1, 2, 0, 3
    )
    kv_local = jnp.concatenate(
        [key_rows.transpose(1, 0, 2), value_rows.transpose(1, 0, 2)], axis=0
    )
    req_count = lax.axis_size("req")
    kv_all = lax.all_to_all(
        jnp.broadcast_to(kv_local[None], (req_count,) + kv_local.shape), "req", 0, 0, tiled=True
    )
    q_index = group_start + jnp.arange(group_len, dtype=jnp.int32)
    q_begin = q_index - group_pos
    head_out = flash_attention(query_grouped, kv_all, q_index, q_begin)
    pages_here = paged_key_value_cache.shape[0]
    page_first = req_pos * pages_here
    group_pages = group_len // PAGE_TOKENS
    local_pages = page_first + jnp.arange(pages_here, dtype=jnp.int32)
    match = local_pages[:, None] == page_table[None, :]
    hit = jnp.any(match, axis=1)
    block_of = jnp.argmax(match, axis=1).astype(jnp.int32)
    kv_paged = kv_all.reshape(req_count, 2, kv_heads, group_pages, PAGE_TOKENS, HEAD_SIZE)
    picked = kv_paged[block_of // group_pages, :, :, block_of % group_pages].transpose(
        0, 2, 1, 3, 4
    )
    new_cache = jnp.where(hit[:, None, None, None, None], picked, paged_key_value_cache)
    out_weight = w_out_attn.reshape(kv_heads, heads_ratio, HEAD_SIZE, w_out_attn.shape[1])
    attention = scatter_sum_ep(
        jnp.einsum(
            "grtd,grdo->to", head_out, out_weight, preferred_element_type=jnp.float32
        ).astype(jnp.bfloat16)
    )
    attn_out = attention.astype(jnp.bfloat16)
    moe_in = rms_scale(tokens.astype(jnp.float32) + residual_scale * attention, norm2_gain).astype(
        jnp.bfloat16
    )
    ffe_width = w_out.shape[1]
    exp_here = w_in.shape[0]
    expert_ids = jnp.arange(E, dtype=jnp.int32)
    shares = jnp.sum(
        jnp.where(routes[:, :, None] == expert_ids[None, None, :], route_weights[:, :, None], 0.0),
        axis=1,
    )
    rows_all = gather_ep(moe_in)
    shares_all = gather_rows(shares, "ep")
    first_expert = lax.axis_index("ep") * exp_here
    shares_here = lax.dynamic_slice_in_dim(shares_all, first_expert, exp_here, 1)
    total_rows = rows_all.shape[0]
    chosen = (shares_here > 0.0).astype(jnp.int32).reshape(ep_count, tok_dev, exp_here)
    slot_in = jnp.cumsum(chosen, axis=1) - 1
    source_ids = jnp.arange(ep_count, dtype=jnp.int32)[:, None, None]
    local_slot = (source_ids * CAP + slot_in).reshape(total_rows, exp_here)
    live = (chosen > 0).reshape(total_rows, exp_here)
    slot_ids = jnp.arange(ep_count * CAP, dtype=jnp.int32)
    dispatch = (local_slot.T[:, None, :] == slot_ids[None, :, None]) & live.T[:, None, :]
    arrived = jnp.einsum(
        "esr,rd->esd", dispatch.astype(jnp.bfloat16), rows_all, preferred_element_type=jnp.float32
    ).astype(jnp.bfloat16)
    gate_up = jnp.einsum("esd,edf->esf", arrived, w_in, preferred_element_type=jnp.float32)
    activated = (jax.nn.silu(gate_up[..., :ffe_width]) * gate_up[..., ffe_width:]).astype(
        jnp.bfloat16
    )
    result = jnp.einsum(
        "esf,efd->esd", activated, w_out, preferred_element_type=jnp.float32
    ).astype(jnp.bfloat16)
    combine = jnp.where(dispatch, shares_here.T[:, None, :], 0.0)
    partial_rows = jnp.einsum(
        "esr,esd->rd", combine.astype(jnp.bfloat16), result, preferred_element_type=jnp.float32
    )
    moe_out = scatter_sum_ep(partial_rows.astype(jnp.bfloat16)).astype(jnp.bfloat16)
    return (attn_out, moe_out, new_cache)


def solution(mesh):
    in_specs = (
        P(("req", "ep"), None),
        P(("req", "ep")),
        P(("req", "ep"), None),
        P(("req", "ep"), None),
        P(),
        P(),
        P(None, "ep"),
        P(None, "ep"),
        P(None, "ep"),
        P("ep", None),
        P("ep", None, None),
        P("ep", None, None),
        P("req", "ep", None, None, None),
        P(),
    )
    out_specs = (P(("req", "ep"), None), P(("req", "ep"), None), P("req", "ep", None, None, None))
    return jax.shard_map(body, mesh=mesh, in_specs=in_specs, out_specs=out_specs, check_vma=False)
```

```python
import jax
import jax.numpy as jnp
from jax import lax
from jax.sharding import PartitionSpec as P
from jax.experimental import pallas as pl
from jax.experimental.pallas import tpu as pltpu

HEAD_SIZE = 64
E = 40
PAGE_TOKENS = 64
CAP = 48


norm_eps = 1e-06
score_scale = 0.015625
residual_scale = 0.22
rope_base = 10000.0
neg_fill = -1e30


def rms_scale(rows, gain):
    mean_sq = jnp.mean(rows * rows, axis=-1, keepdims=True)
    return rows * lax.rsqrt(mean_sq + norm_eps) * gain


def positions_of(segments):
    tok_index = jnp.arange(segments.shape[0], dtype=jnp.int32)
    previous = jnp.concatenate([jnp.full((1,), -1, jnp.int32), segments[:-1]])
    starts = jnp.where(segments != previous, tok_index, 0)
    return tok_index - lax.cummax(starts, axis=0)


def rotary_apply(heads_in, token_positions):
    half_dim = heads_in.shape[-1] // 2
    inverse_freq = rope_base ** (
        -jnp.arange(half_dim, dtype=jnp.float32) * 2.0 / heads_in.shape[-1]
    )
    angles = token_positions.astype(jnp.float32)[:, None] * inverse_freq[None, :]
    cos_part = jnp.cos(angles)[:, None, :]
    sine_part = jnp.sin(angles)[:, None, :]
    first_half = heads_in[..., :half_dim]
    second_half = heads_in[..., half_dim:]
    return jnp.concatenate(
        [
            first_half * cos_part - second_half * sine_part,
            second_half * cos_part + first_half * sine_part,
        ],
        axis=-1,
    )


def gather_rows(x, axis_name, axis=0):
    count = lax.axis_size(axis_name)
    spread = jnp.broadcast_to(x[None], (count,) + x.shape)
    got = lax.all_to_all(spread, axis_name, 0, 0, tiled=True)
    got = jnp.moveaxis(got, 0, axis)
    shape = list(x.shape)
    shape[axis] = shape[axis] * count
    return got.reshape(shape)


def scatter_sum_rows(x, axis_name):
    count = lax.axis_size(axis_name)
    parts = x.reshape((count, x.shape[0] // count) + x.shape[1:])
    got = lax.all_to_all(parts, axis_name, 0, 0, tiled=True)
    return jnp.sum(got.astype(jnp.float32), axis=0)


def chip_pairs(count, shift):
    chips = count // 2
    return [(d, ((d // 2 + shift) % chips) * 2 + d % 2) for d in range(count)]


def gather_ep(x):
    count = lax.axis_size("ep")
    if count % 2:
        return gather_rows(x, "ep")
    chips = count // 2
    me = lax.axis_index("ep")
    chip = me // 2
    core = me % 2
    side = [x]
    for shift in range(1, chips):
        side.append(lax.ppermute(x, "ep", chip_pairs(count, shift)))
    side = jnp.stack(side)
    other = lax.ppermute(side, "ep", [(d, d ^ 1) for d in range(count)])
    both = jnp.where(core == 0, jnp.stack([side, other], 1), jnp.stack([other, side], 1))
    order = (chip - jnp.arange(chips, dtype=jnp.int32)) % chips
    full = jnp.take(both, order, axis=0, mode="clip")
    return full.reshape((count * x.shape[0],) + x.shape[1:])


def scatter_sum_ep(p):
    count = lax.axis_size("ep")
    if count % 2:
        return scatter_sum_rows(p, "ep")
    chips = count // 2
    me = lax.axis_index("ep")
    chip = me // 2
    core = me % 2
    rows = p.shape[0] // count
    parts = p.reshape((chips, 2, rows) + p.shape[1:])
    mine = jnp.where(core == 0, parts[:, 0], parts[:, 1])
    theirs = jnp.where(core == 0, parts[:, 1], parts[:, 0])
    got = lax.ppermute(theirs, "ep", [(d, d ^ 1) for d in range(count)])
    sums = mine.astype(jnp.float32) + got.astype(jnp.float32)
    total = lax.dynamic_index_in_dim(sums, chip, 0, keepdims=False)
    for shift in range(1, chips):
        piece = lax.dynamic_index_in_dim(sums, (chip + shift) % chips, 0, keepdims=False)
        total = total + lax.ppermute(
            piece.astype(jnp.bfloat16), "ep", chip_pairs(count, shift)
        ).astype(jnp.float32)
    return total


Q_TILE = 512
K_TILE = 512


def flash_body(lo_ref, hi_ref, q_ref, k_ref, v_ref, tok_ref, begin_ref, o_ref):
    qb = pl.program_id(1)
    ratio = q_ref.shape[1]
    q_tile = q_ref.shape[2]
    head_dim = q_ref.shape[3]
    q = q_ref[0].reshape(ratio * q_tile, head_dim)
    per_group = k_ref.shape[2] // K_TILE
    tok = tok_ref[...]
    begin = begin_ref[...]

    def step(kb, carry):
        m_old, l_old, acc_old = carry
        k0 = kb * K_TILE
        grp = kb // per_group
        off = pl.multiple_of((kb % per_group) * K_TILE, K_TILE)
        k_blk = k_ref[grp, 0, pl.ds(off, K_TILE), :]
        v_blk = v_ref[grp, 0, pl.ds(off, K_TILE), :]
        s = lax.dot_general(
            q, k_blk, (((1,), (1,)), ((), ())), preferred_element_type=jnp.float32
        )
        s = (s * score_scale).reshape(ratio, q_tile, K_TILE)
        key_at = k0 + lax.broadcasted_iota(jnp.int32, (q_tile, K_TILE), 1)
        allowed = (key_at >= begin) & (key_at <= tok)
        s = jnp.where(allowed[None], s, -jnp.inf)
        m_new = jnp.maximum(m_old, jnp.max(s, axis=-1, keepdims=True))
        alpha = jnp.exp(m_old - m_new)
        p = jnp.exp(s - m_new)
        l_new = alpha * l_old + jnp.sum(p, axis=-1, keepdims=True)
        pv = lax.dot_general(
            p.reshape(ratio * q_tile, K_TILE).astype(jnp.bfloat16),
            v_blk,
            (((1,), (0,)), ((), ())),
            preferred_element_type=jnp.float32,
        )
        acc_new = alpha * acc_old + pv.reshape(ratio, q_tile, head_dim)
        return m_new, l_new, acc_new

    init = (
        jnp.full((ratio, q_tile, 1), neg_fill, jnp.float32),
        jnp.zeros((ratio, q_tile, 1), jnp.float32),
        jnp.zeros((ratio, q_tile, head_dim), jnp.float32),
    )
    m_fin, l_fin, acc_fin = lax.fori_loop(lo_ref[qb], hi_ref[qb] + 1, step, init)
    o_ref[0] = (acc_fin / l_fin).astype(o_ref.dtype)


def flash_attention(query_grouped, kv_all, q_index, q_begin):
    kv_heads, ratio, group_len, head_dim = query_grouped.shape
    n_grp, _, grp_len, _ = kv_all.shape
    n_q = group_len // Q_TILE
    lo = jnp.min(q_begin.reshape(n_q, Q_TILE), axis=1) // K_TILE
    hi = jnp.max(q_index.reshape(n_q, Q_TILE), axis=1) // K_TILE
    grid_spec = pltpu.PrefetchScalarGridSpec(
        num_scalar_prefetch=2,
        grid=(kv_heads, n_q),
        in_specs=[
            pl.BlockSpec((1, ratio, Q_TILE, head_dim), lambda g, qb, lo, hi: (g, 0, qb, 0)),
            pl.BlockSpec((n_grp, 1, grp_len, head_dim), lambda g, qb, lo, hi: (0, g, 0, 0)),
            pl.BlockSpec(
                (n_grp, 1, grp_len, head_dim), lambda g, qb, lo, hi: (0, kv_heads + g, 0, 0)
            ),
            pl.BlockSpec((Q_TILE, 1), lambda g, qb, lo, hi: (qb, 0)),
            pl.BlockSpec((Q_TILE, 1), lambda g, qb, lo, hi: (qb, 0)),
        ],
        out_specs=pl.BlockSpec((1, ratio, Q_TILE, head_dim), lambda g, qb, lo, hi: (g, 0, qb, 0)),
    )
    out = pl.pallas_call(
        flash_body,
        grid_spec=grid_spec,
        out_shape=jax.ShapeDtypeStruct(query_grouped.shape, jnp.bfloat16),
    )(lo, hi, query_grouped, kv_all, kv_all, q_index[:, None], q_begin[:, None])
    return out


def body(
    tokens,
    seg_ids,
    routes,
    route_weights,
    norm1_gain,
    norm2_gain,
    w_query,
    key_weight,
    value_weight,
    w_out_attn,
    w_in,
    w_out,
    paged_key_value_cache,
    page_table,
):
    tok_dev = tokens.shape[0]
    ep_count = lax.axis_size("ep")
    group_len = tok_dev * ep_count
    req_pos = lax.axis_index("req")
    normed = rms_scale(tokens.astype(jnp.float32), norm1_gain).astype(jnp.bfloat16)
    seg_ids, normed = lax.optimization_barrier((seg_ids, normed))
    all_segs = gather_rows(seg_ids, ("req", "ep"))
    all_pos = positions_of(all_segs)
    group_start = req_pos * group_len
    group_pos = lax.dynamic_slice_in_dim(all_pos, group_start, group_len)
    joined = jnp.concatenate([w_query, key_weight, value_weight], axis=1)
    projected = jnp.dot(
        gather_ep(normed), joined, preferred_element_type=jnp.float32
    )
    query_width = w_query.shape[1]
    kv_width = key_weight.shape[1]
    q_heads = query_width // HEAD_SIZE
    kv_heads = kv_width // HEAD_SIZE
    heads_ratio = q_heads // kv_heads
    query_rows = rotary_apply(
        projected[:, :query_width].reshape(group_len, q_heads, HEAD_SIZE), group_pos
    ).astype(jnp.bfloat16)
    key_rows = rotary_apply(
        projected[:, query_width : query_width + kv_width].reshape(
            group_len, kv_heads, HEAD_SIZE
        ),
        group_pos,
    ).astype(jnp.bfloat16)
    value_rows = (
        projected[:, query_width + kv_width :]
        .astype(jnp.bfloat16)
        .reshape(group_len, kv_heads, HEAD_SIZE)
    )
    query_grouped = query_rows.reshape(group_len, kv_heads, heads_ratio, HEAD_SIZE).transpose(
        1, 2, 0, 3
    )
    kv_local = jnp.concatenate(
        [key_rows.transpose(1, 0, 2), value_rows.transpose(1, 0, 2)], axis=0
    )
    req_count = lax.axis_size("req")
    kv_all = lax.all_to_all(
        jnp.broadcast_to(kv_local[None], (req_count,) + kv_local.shape), "req", 0, 0, tiled=True
    )
    q_index = group_start + jnp.arange(group_len, dtype=jnp.int32)
    q_begin = q_index - group_pos
    head_out = flash_attention(query_grouped, kv_all, q_index, q_begin)
    pages_here = paged_key_value_cache.shape[0]
    page_first = req_pos * pages_here
    group_pages = group_len // PAGE_TOKENS
    local_pages = page_first + jnp.arange(pages_here, dtype=jnp.int32)
    match = local_pages[:, None] == page_table[None, :]
    hit = jnp.any(match, axis=1)
    block_of = jnp.argmax(match, axis=1).astype(jnp.int32)
    kv_paged = kv_all.reshape(req_count, 2, kv_heads, group_pages, PAGE_TOKENS, HEAD_SIZE)
    picked = kv_paged[block_of // group_pages, :, :, block_of % group_pages].transpose(
        0, 2, 1, 3, 4
    )
    new_cache = jnp.where(hit[:, None, None, None, None], picked, paged_key_value_cache)
    out_weight = w_out_attn.reshape(kv_heads, heads_ratio, HEAD_SIZE, w_out_attn.shape[1])
    attention = scatter_sum_ep(
        jnp.einsum(
            "grtd,grdo->to", head_out, out_weight, preferred_element_type=jnp.float32
        ).astype(jnp.bfloat16)
    )
    attn_out = attention.astype(jnp.bfloat16)
    moe_in = rms_scale(tokens.astype(jnp.float32) + residual_scale * attention, norm2_gain).astype(
        jnp.bfloat16
    )
    ffe_width = w_out.shape[1]
    exp_here = w_in.shape[0]
    expert_ids = jnp.arange(E, dtype=jnp.int32)
    shares = jnp.sum(
        jnp.where(routes[:, :, None] == expert_ids[None, None, :], route_weights[:, :, None], 0.0),
        axis=1,
    )
    rows_all = gather_ep(moe_in)
    shares_all = gather_rows(shares, "ep")
    first_expert = lax.axis_index("ep") * exp_here
    shares_here = lax.dynamic_slice_in_dim(shares_all, first_expert, exp_here, 1)
    total_rows = rows_all.shape[0]
    chosen = (shares_here > 0.0).astype(jnp.int32).reshape(ep_count, tok_dev, exp_here)
    slot_in = jnp.cumsum(chosen, axis=1) - 1
    source_ids = jnp.arange(ep_count, dtype=jnp.int32)[:, None, None]
    local_slot = (source_ids * CAP + slot_in).reshape(total_rows, exp_here)
    live = (chosen > 0).reshape(total_rows, exp_here)
    slot_ids = jnp.arange(ep_count * CAP, dtype=jnp.int32)
    dispatch = (local_slot.T[:, None, :] == slot_ids[None, :, None]) & live.T[:, None, :]
    arrived = jnp.einsum(
        "esr,rd->esd", dispatch.astype(jnp.bfloat16), rows_all, preferred_element_type=jnp.float32
    ).astype(jnp.bfloat16)
    gate_up = jnp.einsum("esd,edf->esf", arrived, w_in, preferred_element_type=jnp.float32)
    activated = (jax.nn.silu(gate_up[..., :ffe_width]) * gate_up[..., ffe_width:]).astype(
        jnp.bfloat16
    )
    result = jnp.einsum(
        "esf,efd->esd", activated, w_out, preferred_element_type=jnp.float32
    ).astype(jnp.bfloat16)
    combine = jnp.where(dispatch, shares_here.T[:, None, :], 0.0)
    partial_rows = jnp.einsum(
        "esr,esd->rd", combine.astype(jnp.bfloat16), result, preferred_element_type=jnp.float32
    )
    moe_out = scatter_sum_ep(partial_rows.astype(jnp.bfloat16)).astype(jnp.bfloat16)
    return (attn_out, moe_out, new_cache)


def solution(mesh):
    in_specs = (
        P(("req", "ep"), None),
        P(("req", "ep")),
        P(("req", "ep"), None),
        P(("req", "ep"), None),
        P(),
        P(),
        P(None, "ep"),
        P(None, "ep"),
        P(None, "ep"),
        P("ep", None),
        P("ep", None, None),
        P("ep", None, None),
        P("req", "ep", None, None, None),
        P(),
    )
    out_specs = (P(("req", "ep"), None), P(("req", "ep"), None), P("req", "ep", None, None, None))
    return jax.shard_map(body, mesh=mesh, in_specs=in_specs, out_specs=out_specs, check_vma=False)
```

```python
import jax
import jax.numpy as jnp
from jax import lax
from jax.sharding import PartitionSpec as P
from jax.experimental import pallas as pl
from jax.experimental.pallas import tpu as pltpu

HEAD_SIZE = 64
E = 40
PAGE_TOKENS = 64
CAP = 48


norm_eps = 1e-06
score_scale = 0.015625
residual_scale = 0.22
rope_base = 10000.0
neg_fill = -1e30


def rms_scale(rows, gain):
    mean_sq = jnp.mean(rows * rows, axis=-1, keepdims=True)
    return rows * lax.rsqrt(mean_sq + norm_eps) * gain


def positions_of(segments):
    tok_index = jnp.arange(segments.shape[0], dtype=jnp.int32)
    previous = jnp.concatenate([jnp.full((1,), -1, jnp.int32), segments[:-1]])
    starts = jnp.where(segments != previous, tok_index, 0)
    return tok_index - lax.cummax(starts, axis=0)


def rotary_apply(heads_in, token_positions):
    half_dim = heads_in.shape[-1] // 2
    inverse_freq = rope_base ** (
        -jnp.arange(half_dim, dtype=jnp.float32) * 2.0 / heads_in.shape[-1]
    )
    angles = token_positions.astype(jnp.float32)[:, None] * inverse_freq[None, :]
    cos_part = jnp.cos(angles)[:, None, :]
    sine_part = jnp.sin(angles)[:, None, :]
    first_half = heads_in[..., :half_dim]
    second_half = heads_in[..., half_dim:]
    return jnp.concatenate(
        [
            first_half * cos_part - second_half * sine_part,
            second_half * cos_part + first_half * sine_part,
        ],
        axis=-1,
    )


def gather_rows(x, axis_name, axis=0):
    count = lax.axis_size(axis_name)
    spread = jnp.broadcast_to(x[None], (count,) + x.shape)
    got = lax.all_to_all(spread, axis_name, 0, 0, tiled=True)
    got = jnp.moveaxis(got, 0, axis)
    shape = list(x.shape)
    shape[axis] = shape[axis] * count
    return got.reshape(shape)


def scatter_sum_rows(x, axis_name):
    count = lax.axis_size(axis_name)
    parts = x.reshape((count, x.shape[0] // count) + x.shape[1:])
    got = lax.all_to_all(parts, axis_name, 0, 0, tiled=True)
    return jnp.sum(got.astype(jnp.float32), axis=0)


def chip_pairs(count, shift):
    chips = count // 2
    return [(d, ((d // 2 + shift) % chips) * 2 + d % 2) for d in range(count)]


def gather_ep(x):
    count = lax.axis_size("ep")
    if count % 2:
        return gather_rows(x, "ep")
    chips = count // 2
    me = lax.axis_index("ep")
    chip = me // 2
    core = me % 2
    side = [x]
    for shift in range(1, chips):
        side.append(lax.ppermute(x, "ep", chip_pairs(count, shift)))
    side = jnp.stack(side)
    other = lax.ppermute(side, "ep", [(d, d ^ 1) for d in range(count)])
    both = jnp.where(core == 0, jnp.stack([side, other], 1), jnp.stack([other, side], 1))
    order = (chip - jnp.arange(chips, dtype=jnp.int32)) % chips
    full = jnp.take(both, order, axis=0, mode="clip")
    return full.reshape((count * x.shape[0],) + x.shape[1:])


def scatter_sum_ep(p):
    count = lax.axis_size("ep")
    if count % 2:
        return scatter_sum_rows(p, "ep")
    chips = count // 2
    me = lax.axis_index("ep")
    chip = me // 2
    core = me % 2
    rows = p.shape[0] // count
    parts = p.reshape((chips, 2, rows) + p.shape[1:])
    mine = jnp.where(core == 0, parts[:, 0], parts[:, 1])
    theirs = jnp.where(core == 0, parts[:, 1], parts[:, 0])
    got = lax.ppermute(theirs, "ep", [(d, d ^ 1) for d in range(count)])
    sums = mine.astype(jnp.float32) + got.astype(jnp.float32)
    total = lax.dynamic_index_in_dim(sums, chip, 0, keepdims=False)
    for shift in range(1, chips):
        piece = lax.dynamic_index_in_dim(sums, (chip + shift) % chips, 0, keepdims=False)
        total = total + lax.ppermute(
            piece.astype(jnp.bfloat16), "ep", chip_pairs(count, shift)
        ).astype(jnp.float32)
    return total


Q_TILE = 256
K_TILE = 512


def flash_body(lo_ref, hi_ref, in_lo_ref, in_hi_ref, q_ref, k_ref, v_ref, tok_ref, begin_ref, o_ref):
    qb = pl.program_id(1)
    ratio = q_ref.shape[1]
    q_tile = q_ref.shape[2]
    head_dim = q_ref.shape[3]
    q = q_ref[0].reshape(ratio * q_tile, head_dim)
    per_group = k_ref.shape[2] // K_TILE
    tok = tok_ref[...]
    begin = begin_ref[...]

    def step(kb, carry):
        m_old, l_old, acc_old = carry
        k0 = kb * K_TILE
        grp = kb // per_group
        off = pl.multiple_of((kb % per_group) * K_TILE, K_TILE)
        k_blk = k_ref[grp, 0, pl.ds(off, K_TILE), :]
        v_blk = v_ref[grp, 0, pl.ds(off, K_TILE), :]
        s = lax.dot_general(
            q, k_blk, (((1,), (1,)), ((), ())), preferred_element_type=jnp.float32
        )
        s = (s * score_scale).reshape(ratio, q_tile, K_TILE)
        inside = (kb >= in_lo_ref[qb]) & (kb <= in_hi_ref[qb])

        def masked(s_in):
            key_at = k0 + lax.broadcasted_iota(jnp.int32, (q_tile, K_TILE), 1)
            allowed = (key_at >= begin) & (key_at <= tok)
            return jnp.where(allowed[None], s_in, -jnp.inf)

        s = lax.cond(inside, lambda s_in: s_in, masked, s)
        m_new = jnp.maximum(m_old, jnp.max(s, axis=-1, keepdims=True))
        alpha = jnp.exp(m_old - m_new)
        p = jnp.exp(s - m_new)
        l_new = alpha * l_old + jnp.sum(p, axis=-1, keepdims=True)
        pv = lax.dot_general(
            p.reshape(ratio * q_tile, K_TILE).astype(jnp.bfloat16),
            v_blk,
            (((1,), (0,)), ((), ())),
            preferred_element_type=jnp.float32,
        )
        acc_new = alpha * acc_old + pv.reshape(ratio, q_tile, head_dim)
        return m_new, l_new, acc_new

    init = (
        jnp.full((ratio, q_tile, 1), neg_fill, jnp.float32),
        jnp.zeros((ratio, q_tile, 1), jnp.float32),
        jnp.zeros((ratio, q_tile, head_dim), jnp.float32),
    )
    m_fin, l_fin, acc_fin = lax.fori_loop(lo_ref[qb], hi_ref[qb] + 1, step, init)
    o_ref[0] = (acc_fin / l_fin).astype(o_ref.dtype)


def flash_attention(query_grouped, kv_all, q_index, q_begin):
    kv_heads, ratio, group_len, head_dim = query_grouped.shape
    n_grp, _, grp_len, _ = kv_all.shape
    n_q = group_len // Q_TILE
    lo = jnp.min(q_begin.reshape(n_q, Q_TILE), axis=1) // K_TILE
    hi = jnp.max(q_index.reshape(n_q, Q_TILE), axis=1) // K_TILE
    in_lo = -(-jnp.max(q_begin.reshape(n_q, Q_TILE), axis=1) // K_TILE)
    in_hi = (jnp.min(q_index.reshape(n_q, Q_TILE), axis=1) + 1) // K_TILE - 1
    grid_spec = pltpu.PrefetchScalarGridSpec(
        num_scalar_prefetch=4,
        grid=(kv_heads, n_q),
        in_specs=[
            pl.BlockSpec((1, ratio, Q_TILE, head_dim), lambda g, qb, lo, hi, il, ih: (g, 0, qb, 0)),
            pl.BlockSpec((n_grp, 1, grp_len, head_dim), lambda g, qb, lo, hi, il, ih: (0, g, 0, 0)),
            pl.BlockSpec(
                (n_grp, 1, grp_len, head_dim), lambda g, qb, lo, hi, il, ih: (0, kv_heads + g, 0, 0)
            ),
            pl.BlockSpec((Q_TILE, 1), lambda g, qb, lo, hi, il, ih: (qb, 0)),
            pl.BlockSpec((Q_TILE, 1), lambda g, qb, lo, hi, il, ih: (qb, 0)),
        ],
        out_specs=pl.BlockSpec((1, ratio, Q_TILE, head_dim), lambda g, qb, lo, hi, il, ih: (g, 0, qb, 0)),
    )
    out = pl.pallas_call(
        flash_body,
        grid_spec=grid_spec,
        out_shape=jax.ShapeDtypeStruct(query_grouped.shape, jnp.bfloat16),
    )(lo, hi, in_lo, in_hi, query_grouped, kv_all, kv_all, q_index[:, None], q_begin[:, None])
    return out


def body(
    tokens,
    seg_ids,
    routes,
    route_weights,
    norm1_gain,
    norm2_gain,
    w_query,
    key_weight,
    value_weight,
    w_out_attn,
    w_in,
    w_out,
    paged_key_value_cache,
    page_table,
):
    tok_dev = tokens.shape[0]
    ep_count = lax.axis_size("ep")
    group_len = tok_dev * ep_count
    req_pos = lax.axis_index("req")
    normed = rms_scale(tokens.astype(jnp.float32), norm1_gain).astype(jnp.bfloat16)
    seg_ids, normed = lax.optimization_barrier((seg_ids, normed))
    all_segs = gather_rows(seg_ids, ("req", "ep"))
    all_pos = positions_of(all_segs)
    group_start = req_pos * group_len
    group_pos = lax.dynamic_slice_in_dim(all_pos, group_start, group_len)
    joined = jnp.concatenate([w_query, key_weight, value_weight], axis=1)
    projected = jnp.dot(
        gather_ep(normed), joined, preferred_element_type=jnp.float32
    )
    query_width = w_query.shape[1]
    kv_width = key_weight.shape[1]
    q_heads = query_width // HEAD_SIZE
    kv_heads = kv_width // HEAD_SIZE
    heads_ratio = q_heads // kv_heads
    query_rows = rotary_apply(
        projected[:, :query_width].reshape(group_len, q_heads, HEAD_SIZE), group_pos
    ).astype(jnp.bfloat16)
    key_rows = rotary_apply(
        projected[:, query_width : query_width + kv_width].reshape(
            group_len, kv_heads, HEAD_SIZE
        ),
        group_pos,
    ).astype(jnp.bfloat16)
    value_rows = (
        projected[:, query_width + kv_width :]
        .astype(jnp.bfloat16)
        .reshape(group_len, kv_heads, HEAD_SIZE)
    )
    query_grouped = query_rows.reshape(group_len, kv_heads, heads_ratio, HEAD_SIZE).transpose(
        1, 2, 0, 3
    )
    kv_local = jnp.concatenate(
        [key_rows.transpose(1, 0, 2), value_rows.transpose(1, 0, 2)], axis=0
    )
    req_count = lax.axis_size("req")
    kv_all = lax.all_to_all(
        jnp.broadcast_to(kv_local[None], (req_count,) + kv_local.shape), "req", 0, 0, tiled=True
    )
    q_index = group_start + jnp.arange(group_len, dtype=jnp.int32)
    q_begin = q_index - group_pos
    head_out = flash_attention(query_grouped, kv_all, q_index, q_begin)
    pages_here = paged_key_value_cache.shape[0]
    page_first = req_pos * pages_here
    group_pages = group_len // PAGE_TOKENS
    local_pages = page_first + jnp.arange(pages_here, dtype=jnp.int32)
    match = local_pages[:, None] == page_table[None, :]
    hit = jnp.any(match, axis=1)
    block_of = jnp.argmax(match, axis=1).astype(jnp.int32)
    kv_paged = kv_all.reshape(req_count, 2, kv_heads, group_pages, PAGE_TOKENS, HEAD_SIZE)
    picked = kv_paged[block_of // group_pages, :, :, block_of % group_pages].transpose(
        0, 2, 1, 3, 4
    )
    new_cache = jnp.where(hit[:, None, None, None, None], picked, paged_key_value_cache)
    out_weight = w_out_attn.reshape(kv_heads, heads_ratio, HEAD_SIZE, w_out_attn.shape[1])
    attention = scatter_sum_ep(
        jnp.einsum(
            "grtd,grdo->to", head_out, out_weight, preferred_element_type=jnp.float32
        ).astype(jnp.bfloat16)
    )
    attn_out = attention.astype(jnp.bfloat16)
    moe_in = rms_scale(tokens.astype(jnp.float32) + residual_scale * attention, norm2_gain).astype(
        jnp.bfloat16
    )
    ffe_width = w_out.shape[1]
    exp_here = w_in.shape[0]
    expert_ids = jnp.arange(E, dtype=jnp.int32)
    shares = jnp.sum(
        jnp.where(routes[:, :, None] == expert_ids[None, None, :], route_weights[:, :, None], 0.0),
        axis=1,
    )
    rows_all = gather_ep(moe_in)
    shares_all = gather_rows(shares, "ep")
    first_expert = lax.axis_index("ep") * exp_here
    shares_here = lax.dynamic_slice_in_dim(shares_all, first_expert, exp_here, 1)
    total_rows = rows_all.shape[0]
    chosen = (shares_here > 0.0).astype(jnp.int32).reshape(ep_count, tok_dev, exp_here)
    slot_in = jnp.cumsum(chosen, axis=1) - 1
    source_ids = jnp.arange(ep_count, dtype=jnp.int32)[:, None, None]
    local_slot = (source_ids * CAP + slot_in).reshape(total_rows, exp_here)
    live = (chosen > 0).reshape(total_rows, exp_here)
    slot_ids = jnp.arange(ep_count * CAP, dtype=jnp.int32)
    dispatch = (local_slot.T[:, None, :] == slot_ids[None, :, None]) & live.T[:, None, :]
    arrived = jnp.einsum(
        "esr,rd->esd", dispatch.astype(jnp.bfloat16), rows_all, preferred_element_type=jnp.float32
    ).astype(jnp.bfloat16)
    gate_up = jnp.einsum("esd,edf->esf", arrived, w_in, preferred_element_type=jnp.float32)
    activated = (jax.nn.silu(gate_up[..., :ffe_width]) * gate_up[..., ffe_width:]).astype(
        jnp.bfloat16
    )
    result = jnp.einsum(
        "esf,efd->esd", activated, w_out, preferred_element_type=jnp.float32
    ).astype(jnp.bfloat16)
    combine = jnp.where(dispatch, shares_here.T[:, None, :], 0.0)
    partial_rows = jnp.einsum(
        "esr,esd->rd", combine.astype(jnp.bfloat16), result, preferred_element_type=jnp.float32
    )
    moe_out = scatter_sum_ep(partial_rows.astype(jnp.bfloat16)).astype(jnp.bfloat16)
    return (attn_out, moe_out, new_cache)


def solution(mesh):
    in_specs = (
        P(("req", "ep"), None),
        P(("req", "ep")),
        P(("req", "ep"), None),
        P(("req", "ep"), None),
        P(),
        P(),
        P(None, "ep"),
        P(None, "ep"),
        P(None, "ep"),
        P("ep", None),
        P("ep", None, None),
        P("ep", None, None),
        P("req", "ep", None, None, None),
        P(),
    )
    out_specs = (P(("req", "ep"), None), P(("req", "ep"), None), P("req", "ep", None, None, None))
    return jax.shard_map(body, mesh=mesh, in_specs=in_specs, out_specs=out_specs, check_vma=False)
```
